32 devices in a mesh: groups: 2 (over x), rows: 16 (over z, y, core).
Axes of the slice: x: 2, y: 2, z: 4, core: 2. Of those that a mesh axis runs over, the one named last changes fastest.
Arguments:
- inputs: bfloat16 [256, 512, 128], P(('groups', 'rows')), parts along dimension 0, may hold values from -6 to 6
- cotangent: bfloat16 [256, 512, 128], P(('groups', 'rows')), parts along dimension 0, may hold values from -48 to 48
- first_kernel: bfloat16 [9, 128, 128], replicated, may hold values from -0.1875 to 0.1875
- second_kernel: bfloat16 [9, 128, 128], replicated, may hold values from -0.1875 to 0.1875
- level_table: float32 [16, 2, 128], replicated, may hold values from -3 to 3
- level_index: int32 [2], P('groups'), parts along dimension 0, may hold values from 0 to 15
Outputs:
- outputs: bfloat16 [256, 512, 128], P(('groups', 'rows')), parts along dimension 0
- input_grad: bfloat16 [256, 512, 128], P(('groups', 'rows')), parts along dimension 0
- first_grad: float32 [18, 128, 128], P('groups'), parts along dimension 0
- second_grad: float32 [18, 128, 128], P('groups'), parts along dimension 0
- level_grad: float32 [4, 128], P('groups'), parts along dimension 0
The draws below stay inside these ranges and needn't reach their ends.
There are 2 independent parts, one for each index of `groups`. The reference program is written for one: setup_inputs(seed, part) draws one part's arguments, and reference() takes and returns one part's arrays. A program takes and returns all parts, laid end to end along the dimension named above; an argument that names none is the same for every part. Nothing has to cross between parts.
All inputs are finite; a program needn't handle non-finite values.
Results may differ from the reference program's by a relative error of at most 0.0036.
Values may be sent and summed in bfloat16 or wider, within the bound.
No kernel may reach another device: no remote copies, remote signals or barrier semaphores. Data moves between devices by JAX's collectives and lax.ppermute only.
A program may use at most 128 MiB of HBM per device.

```python
import math
import jax
import jax.numpy as jnp
from jax import lax

C = 128
W = 512
LEVELS = 16
NR = 128


def draw_cotangent(key, part):
    keys = jax.random.split(key, 3)
    ramp = 3.0 ** (jnp.arange(NR, dtype=jnp.float32) / NR)
    row_scale = ramp * jnp.exp(jax.random.uniform(keys[0], (NR,), jnp.float32, 0.0, math.log(2.0)))
    col_scale = jnp.exp(jax.random.uniform(keys[1], (W,), jnp.float32, 0.0, math.log(2.0)))
    noise = jnp.clip(jax.random.normal(keys[2], (NR, W, C), jnp.float32), -4.0, 4.0)
    return (noise * row_scale[:, None, None] * col_scale[None, :, None]).astype(jnp.bfloat16)


def level_of(own_key, dims, shards, least, top_value):
    def one(axis_at, blocks):
        heights = jax.random.uniform(jax.random.fold_in(jax.random.fold_in(own_key, 6), axis_at), (blocks,), jnp.float32, least / len(shards), top_value / len(shards))
        return jnp.repeat(jnp.exp(heights), dims[axis_at] // blocks).reshape((-1,) + (1,) * (len(dims) - axis_at - 1))

    factor_of = one(*shards[0])
    for cut in shards[1:]:
        factor_of = factor_of * one(*cut)
    return factor_of


def bell_draw(own_key, extent, deviation, bound, shards=(), held_as=jnp.bfloat16):
    level = level_of(own_key, extent, shards, -0.22, 0.18) if shards else 1.0
    values = jax.random.normal(own_key, extent, jnp.float32) * deviation * level
    return jnp.minimum(jnp.maximum(values, -bound), bound).astype(held_as)


def setup_inputs(seed: int = 0, part: int = 0) -> dict:
    arg_keys = jax.random.split(jax.random.key(seed), 7)
    part_splits = jax.random.split(jax.random.fold_in(arg_keys[6], part), 7)
    inputs = bell_draw(part_splits[0], (NR, W, C), 1.0, 6.0, ((0, 16),))
    cotangent = draw_cotangent(jax.random.fold_in(jax.random.fold_in(arg_keys[6], part), 71), part)
    first_kernel = bell_draw(arg_keys[2], (9, C, C), (9 * C) ** -0.5, 0.1875)
    second_kernel = bell_draw(arg_keys[3], (9, C, C), (9 * C) ** -0.5, 0.1875)
    level_table = bell_draw(arg_keys[4], (LEVELS, 2, C), 0.5, 3.0, (), jnp.float32)
    level_index = jax.random.randint(part_splits[5], (1,), 0, LEVELS).astype(jnp.int32)
    return dict(inputs=inputs, cotangent=cotangent, first_kernel=first_kernel, second_kernel=second_kernel, level_table=level_table, level_index=level_index)


def conv_forward(padded, kernel):
    rows = padded.shape[0] - 2
    cols = padded.shape[1] - 2
    total = jnp.zeros((rows, cols, kernel.shape[2]), jnp.float32)
    for a in range(3):
        for b in range(3):
            piece = padded[a:a + rows, b:b + cols].astype(jnp.float32)
            total = total + jnp.einsum('hwc,co->hwo', piece, kernel[3 * a + b].astype(jnp.float32))
    return total

def conv_back(padded, kernel):
    rows = padded.shape[0] - 2
    cols = padded.shape[1] - 2
    total = jnp.zeros((rows, cols, kernel.shape[1]), jnp.float32)
    for a in range(3):
        for b in range(3):
            piece = padded[2 - a:2 - a + rows, 2 - b:2 - b + cols].astype(jnp.float32)
            total = total + jnp.einsum('hwo,co->hwc', piece, kernel[3 * a + b].astype(jnp.float32))
    return total

def kernel_terms(padded, result):
    rows = result.shape[0]
    cols = result.shape[1]
    grad_out = result.astype(jnp.float32)
    terms = []
    for a in range(3):
        for b in range(3):
            piece = padded[a:a + rows, b:b + cols].astype(jnp.float32)
            terms.append(jnp.einsum('hwc,hwo->co', piece, grad_out))
    return jnp.stack(terms)

def pad_both(field):
    return jnp.pad(field, ((1, 1), (1, 1), (0, 0)))

def reference(inputs, cotangent, first_kernel, second_kernel, level_table, level_index):
    row = level_table[level_index[0]]
    scale = 1.0 + row[0]
    shift = row[1]
    input_pad = pad_both(inputs)
    first = conv_forward(input_pad, first_kernel)
    mixed = first * scale + shift
    sig = jax.nn.sigmoid(mixed)
    hidden = (mixed * sig).astype(jnp.bfloat16)
    hidden_pad = pad_both(hidden)
    outputs = (inputs.astype(jnp.float32) + conv_forward(hidden_pad, second_kernel)).astype(jnp.bfloat16)
    back_hidden = conv_back(pad_both(cotangent), second_kernel)
    back_mixed = back_hidden * (sig * (1.0 + mixed * (1.0 - sig)))
    back_first = (back_mixed * scale).astype(jnp.bfloat16)
    input_grad = (cotangent.astype(jnp.float32) + conv_back(pad_both(back_first), first_kernel)).astype(jnp.bfloat16)
    norm = 1.0 / math.sqrt(NR * W)
    first_grad = kernel_terms(input_pad, back_first) * norm
    second_grad = kernel_terms(hidden_pad, cotangent) * norm
    level_grad = jnp.stack([lax.optimization_barrier(jnp.sum(back_mixed * first, axis=(0, 1))), lax.optimization_barrier(jnp.sum(back_mixed, axis=(0, 1)))]) * norm
    return (outputs, input_grad, first_grad, second_grad, level_grad)
```

```python
import math

import jax
import jax.numpy as jnp
from jax import lax
from jax.sharding import PartitionSpec as P

COLS = ((0, 0), (1, 1))


def halo2(shard):
    size = lax.axis_size("rows")
    up = [(i, i + 1) for i in range(size - 1)]
    down = [(i + 1, i) for i in range(size - 1)]
    before = lax.ppermute(shard[-2:], "rows", up)
    after = lax.ppermute(shard[:2], "rows", down)
    return before, after


def conv_fwd(padded, kernel):
    c, o = kernel.shape[1], kernel.shape[2]
    out = lax.conv_general_dilated(
        padded[None],
        kernel.reshape(3, 3, c, o),
        (1, 1),
        COLS,
        dimension_numbers=("NHWC", "HWIO", "NHWC"),
        preferred_element_type=jnp.float32,
    )
    return out[0]


def conv_back(padded, kernel):
    c, o = kernel.shape[1], kernel.shape[2]
    flipped = kernel.reshape(3, 3, c, o)[::-1, ::-1]
    out = lax.conv_general_dilated(
        padded[None],
        flipped,
        (1, 1),
        COLS,
        dimension_numbers=("NHWC", "HWOI", "NHWC"),
        preferred_element_type=jnp.float32,
    )
    return out[0]


def kernel_terms(padded, result):
    out = lax.conv_general_dilated(
        padded[None],
        result[None],
        (1, 1),
        COLS,
        dimension_numbers=("CHWN", "IHWO", "HWNC"),
        preferred_element_type=jnp.float32,
    )
    return out.reshape(9, padded.shape[2], result.shape[2])


def butterfly_sum(flat):
    n = lax.axis_size("rows")
    me = lax.axis_index("rows")
    steps = []
    k = 1
    while k < n:
        steps.append(k)
        k *= 2
    piece = flat
    for k in steps:
        half = piece.shape[0] // 2
        bit = (me // k) % 2
        keep = lax.dynamic_slice_in_dim(piece, bit * half, half)
        send = lax.dynamic_slice_in_dim(piece, (1 - bit) * half, half)
        got = lax.ppermute(send, "rows", [(i, i ^ k) for i in range(n)])
        piece = keep + got
    for k in reversed(steps):
        half = piece.shape[0]
        bit = (me // k) % 2
        got = lax.ppermute(piece, "rows", [(i, i ^ k) for i in range(n)])
        whole = jnp.zeros((2 * half,), piece.dtype)
        whole = lax.dynamic_update_slice_in_dim(whole, piece, bit * half, 0)
        piece = lax.dynamic_update_slice_in_dim(whole, got, (1 - bit) * half, 0)
    return piece


def local(inputs, cotangent, first_kernel, second_kernel, level_table, level_index):
    count = inputs.shape[0]
    width = inputs.shape[1]
    size = lax.axis_size("rows")
    me = lax.axis_index("rows")
    total_rows = count * size
    selected = lax.dynamic_index_in_dim(level_table, level_index[0], 0, keepdims=False)
    scale = 1.0 + selected[0]
    shift = selected[1]

    in_before, in_after = halo2(inputs)
    cot_before, cot_after = halo2(cotangent)
    input12 = jnp.concatenate([in_before, inputs, in_after], axis=0)
    cot12 = jnp.concatenate([cot_before, cotangent, cot_after], axis=0)

    grid_row = me * count - 1 + lax.broadcasted_iota(jnp.int32, (count + 2, 1, 1), 0)
    inside = (grid_row >= 0) & (grid_row < total_rows)

    first = conv_fwd(input12, first_kernel)
    mixed = first * scale + shift
    sig = jax.nn.sigmoid(mixed)
    hidden = jnp.where(inside, mixed * sig, 0.0).astype(jnp.bfloat16)
    outputs = (inputs.astype(jnp.float32) + conv_fwd(hidden, second_kernel)).astype(jnp.bfloat16)

    back_hidden = conv_back(cot12, second_kernel)
    back_mixed = back_hidden * (sig * (1.0 + mixed * (1.0 - sig)))
    back_first = jnp.where(inside, back_mixed * scale, 0.0).astype(jnp.bfloat16)
    input_grad = (cotangent.astype(jnp.float32) + conv_back(back_first, first_kernel)).astype(
        jnp.bfloat16
    )

    own = slice(1, count + 1)
    second_terms = kernel_terms(hidden, cotangent)
    first_terms = kernel_terms(input12[own.start : count + 3], back_first[own])
    level_terms = jnp.stack(
        [
            jnp.sum(back_mixed[own] * first[own], axis=(0, 1)),
            jnp.sum(back_mixed[own], axis=(0, 1)),
        ]
    )
    second_sum = butterfly_sum(second_terms.reshape(-1))
    rest = butterfly_sum(jnp.concatenate([first_terms.reshape(-1), level_terms.reshape(-1)]))
    split = first_terms.size
    norm = 1.0 / math.sqrt(total_rows * width)
    first_sum = rest[:split].reshape(first_terms.shape)
    level_sum = rest[split:].reshape(level_terms.shape)
    return (outputs, input_grad, first_sum * norm, second_sum.reshape(second_terms.shape) * norm, level_sum * norm)


def solution(mesh):
    return jax.shard_map(
        local,
        mesh=mesh,
        in_specs=(
            P(("groups", "rows"), None, None),
            P(("groups", "rows"), None, None),
            P(),
            P(),
            P(),
            P("groups"),
        ),
        out_specs=(
            P(("groups", "rows"), None, None),
            P(("groups", "rows"), None, None),
            P("groups", None, None),
            P("groups", None, None),
            P("groups", None),
        ),
        check_vma=False,
    )
```

```python
import math

import jax
import jax.numpy as jnp
from jax import lax
from jax.experimental import pallas as pl
from jax.experimental.pallas import tpu as pltpu
from jax.sharding import PartitionSpec as P


def forward_matrix(kernel):
    c, o = kernel.shape[1], kernel.shape[2]
    return kernel.reshape(3, 3, c, o).transpose(0, 2, 1, 3).reshape(3 * c, 3 * o)


def back_matrix(kernel):
    c, o = kernel.shape[1], kernel.shape[2]
    flipped = kernel.reshape(3, 3, c, o)[::-1, ::-1]
    return flipped.transpose(0, 3, 1, 2).reshape(3 * o, 3 * c)


def taps_from_matrix(matrix, c, o):
    return matrix.reshape(3, c, 3, o).transpose(0, 2, 1, 3).reshape(9, c, o)


def section_kernel(edge_ref, ss_ref, x_ref, c_ref, k1f_ref, k2f_ref, k2b_ref, k1b_ref,
                   out_ref, ig_ref, g1_ref, g2_ref, lv_ref, hid_ref, bf_ref):
    count = out_ref.shape[0]
    width = out_ref.shape[1]
    ch = out_ref.shape[2]
    col = lax.broadcasted_iota(jnp.int32, (width, ch), 0)
    not_first = col > 0
    not_last = col < width - 1
    scale = ss_ref[0:1, :]
    shift = ss_ref[1:2, :]
    top = edge_ref[0] > 0
    bottom = edge_ref[1] > 0

    def combine(y):
        left = pltpu.roll(y[:, 0:ch], 1, 0)
        right = pltpu.roll(y[:, 2 * ch:3 * ch], width - 1, 0)
        return y[:, ch:2 * ch] + jnp.where(not_first, left, 0.0) + jnp.where(not_last, right, 0.0)

    def conv_row(ref, r, matrix_ref):
        rows = jnp.concatenate([ref[r], ref[r + 1], ref[r + 2]], axis=1)
        y = jnp.dot(rows, matrix_ref[...], preferred_element_type=jnp.float32)
        return combine(y)

    def shifted(g):
        g32 = g.astype(jnp.float32)
        g0 = jnp.where(not_last, pltpu.roll(g32, width - 1, 0), 0.0)
        g2 = jnp.where(not_first, pltpu.roll(g32, 1, 0), 0.0)
        return jnp.concatenate([g0.astype(g.dtype), g, g2.astype(g.dtype)], axis=1)

    def phase_one(r, carry):
        lv0, lv1 = carry
        valid = jnp.logical_and(jnp.logical_or(r > 0, top), jnp.logical_or(r < count + 1, bottom))
        first = conv_row(x_ref, r, k1f_ref)
        mixed = first * scale + shift
        sig = 1.0 / (1.0 + jnp.exp(-mixed))
        hid_ref[r] = jnp.where(valid, mixed * sig, 0.0).astype(hid_ref.dtype)
        back_hidden = conv_row(c_ref, r, k2b_ref)
        back_mixed = back_hidden * (sig * (1.0 + mixed * (1.0 - sig)))
        bf_ref[r] = jnp.where(valid, back_mixed * scale, 0.0).astype(bf_ref.dtype)
        own = jnp.logical_and(r >= 1, r <= count)
        lv0 = lv0 + jnp.where(own, jnp.sum(back_mixed * first, axis=0, keepdims=True), 0.0)
        lv1 = lv1 + jnp.where(own, jnp.sum(back_mixed, axis=0, keepdims=True), 0.0)
        return lv0, lv1

    zero = jnp.zeros((1, ch), jnp.float32)
    lv0, lv1 = lax.fori_loop(0, count + 2, phase_one, (zero, zero))
    lv_ref[0:1, :] = lv0
    lv_ref[1:2, :] = lv1
    g1_ref[...] = jnp.zeros_like(g1_ref)
    g2_ref[...] = jnp.zeros_like(g2_ref)

    def phase_two(i, carry):
        out_ref[i] = (x_ref[i + 2].astype(jnp.float32) + conv_row(hid_ref, i, k2f_ref)).astype(out_ref.dtype)
        ig_ref[i] = (c_ref[i + 2].astype(jnp.float32) + conv_row(bf_ref, i, k1b_ref)).astype(ig_ref.dtype)
        xs = jnp.concatenate([x_ref[i + 1], x_ref[i + 2], x_ref[i + 3]], axis=1)
        gs = shifted(bf_ref[i + 1])
        g1_ref[...] += lax.dot_general(xs, gs, (((0,), (0,)), ((), ())), preferred_element_type=jnp.float32)
        hs = jnp.concatenate([hid_ref[i], hid_ref[i + 1], hid_ref[i + 2]], axis=1)
        cs = shifted(c_ref[i + 2])
        g2_ref[...] += lax.dot_general(hs, cs, (((0,), (0,)), ((), ())), preferred_element_type=jnp.float32)
        return carry

    lax.fori_loop(0, count, phase_two, 0)


def section(edge, ss, x12, c12, k1f, k2f, k2b, k1b):
    ext, width, ch = x12.shape
    count = ext - 4
    vmem = pltpu.MemorySpace.VMEM if hasattr(pltpu, "MemorySpace") else pltpu.VMEM
    spec = pl.BlockSpec(memory_space=vmem)
    flops = 2 * (count + 2) * width * (3 * ch) * (3 * ch) * 2 + 4 * count * width * (3 * ch) * (3 * ch) * 2
    return pl.pallas_call(
        section_kernel,
        out_shape=(
            jax.ShapeDtypeStruct((count, width, ch), jnp.bfloat16),
            jax.ShapeDtypeStruct((count, width, ch), jnp.bfloat16),
            jax.ShapeDtypeStruct((3 * ch, 3 * ch), jnp.float32),
            jax.ShapeDtypeStruct((3 * ch, 3 * ch), jnp.float32),
            jax.ShapeDtypeStruct((2, ch), jnp.float32),
        ),
        in_specs=[pl.BlockSpec(memory_space=pltpu.SMEM)] + [spec] * 7,
        out_specs=(spec,) * 5,
        scratch_shapes=[
            pltpu.VMEM((count + 2, width, ch), jnp.bfloat16),
            pltpu.VMEM((count + 2, width, ch), jnp.bfloat16),
        ],
        compiler_params=pltpu.CompilerParams(vmem_limit_bytes=60 * 1024 * 1024),
        cost_estimate=pl.CostEstimate(
            flops=flops, transcendentals=(count + 2) * width * ch, bytes_accessed=8 * ext * width * ch
        ),
    )(edge, ss, x12, c12, k1f, k2f, k2b, k1b)


def butterfly_sum(block):
    n = lax.axis_size("rows")
    me = lax.axis_index("rows")
    steps = []
    k = 1
    while k < n:
        steps.append(k)
        k *= 2
    piece = block
    for k in steps:
        half = piece.shape[0] // 2
        low = (me // k) % 2 == 0
        lo, hi = piece[:half], piece[half:]
        keep = jnp.where(low, lo, hi)
        send = jnp.where(low, hi, lo)
        got = lax.ppermute(send, "rows", [(i, i ^ k) for i in range(n)])
        piece = keep + got
    for k in reversed(steps):
        low = (me // k) % 2 == 0
        got = lax.ppermute(piece, "rows", [(i, i ^ k) for i in range(n)])
        piece = jnp.where(low, jnp.concatenate([piece, got]), jnp.concatenate([got, piece]))
    return piece


def local(inputs, cotangent, first_kernel, second_kernel, level_table, level_index):
    count = inputs.shape[0]
    width = inputs.shape[1]
    ch = inputs.shape[2]
    size = lax.axis_size("rows")
    me = lax.axis_index("rows")
    total_rows = count * size
    selected = lax.dynamic_index_in_dim(level_table, level_index[0], 0, keepdims=False)
    ss = jnp.stack([1.0 + selected[0], selected[1]])

    up = [(i, i + 1) for i in range(size - 1)]
    down = [(i + 1, i) for i in range(size - 1)]
    before = lax.ppermute(jnp.concatenate([inputs[-2:], cotangent[-2:]]), "rows", up)
    after = lax.ppermute(jnp.concatenate([inputs[:2], cotangent[:2]]), "rows", down)
    x12 = jnp.concatenate([before[:2], inputs, after[:2]])
    c12 = jnp.concatenate([before[2:], cotangent, after[2:]])
    edge = jnp.stack([me > 0, me < size - 1]).astype(jnp.int32)

    outputs, input_grad, g1, g2, lv = section(
        edge, ss, x12, c12,
        forward_matrix(first_kernel), forward_matrix(second_kernel),
        back_matrix(second_kernel), back_matrix(first_kernel),
    )
    used = 2 * (g1.size // ch) + 2
    pad = jnp.zeros((-used % size, ch), jnp.float32)
    packed = jnp.concatenate([g1.reshape(-1, ch), g2.reshape(-1, ch), lv, pad])
    total = butterfly_sum(packed)
    norm = 1.0 / math.sqrt(total_rows * width)
    n1 = g1.size // ch
    first_sum = taps_from_matrix(total[:n1].reshape(g1.shape), ch, ch)
    second_sum = taps_from_matrix(total[n1 : 2 * n1].reshape(g2.shape), ch, ch)
    level_sum = total[2 * n1 : 2 * n1 + 2]
    return (outputs, input_grad, first_sum * norm, second_sum * norm, level_sum * norm)


def solution(mesh):
    return jax.shard_map(
        local,
        mesh=mesh,
        in_specs=(
            P(("groups", "rows"), None, None),
            P(("groups", "rows"), None, None),
            P(),
            P(),
            P(),
            P("groups"),
        ),
        out_specs=(
            P(("groups", "rows"), None, None),
            P(("groups", "rows"), None, None),
            P("groups", None, None),
            P("groups", None, None),
            P("groups", None),
        ),
        check_vma=False,
    )
```

```python
import functools
import math

import jax
import jax.numpy as jnp
from jax import lax
from jax.experimental import pallas as pl
from jax.experimental.pallas import tpu as pltpu
from jax.sharding import PartitionSpec as P


def section_kernel(norm, idx_ref, lt_ref, x_hbm, c_hbm, before_hbm, after_hbm, k1_ref, k2_ref,
                   out_ref, ig_ref, grad_ref,
                   x_ref, c_ref, hid_ref, bf_ref, k1f_ref, k2f_ref, k2b_ref, k1b_ref, acc1, acc2, sems):
    count = out_ref.shape[0]
    width = out_ref.shape[1]
    ch = out_ref.shape[2]
    copies = [
        pltpu.make_async_copy(before_hbm.at[0:2], x_ref.at[0:2], sems.at[0]),
        pltpu.make_async_copy(x_hbm, x_ref.at[2 : count + 2], sems.at[1]),
        pltpu.make_async_copy(after_hbm.at[0:2], x_ref.at[count + 2 : count + 4], sems.at[2]),
        pltpu.make_async_copy(before_hbm.at[2:4], c_ref.at[0:2], sems.at[3]),
        pltpu.make_async_copy(c_hbm, c_ref.at[2 : count + 2], sems.at[4]),
        pltpu.make_async_copy(after_hbm.at[2:4], c_ref.at[count + 2 : count + 4], sems.at[5]),
    ]
    for cp in copies:
        cp.start()

    for a in range(3):
        for b in range(3):
            rows = slice(a * ch, (a + 1) * ch)
            cols = slice(b * ch, (b + 1) * ch)
            k1f_ref[rows, cols] = k1_ref[3 * a + b]
            k2f_ref[rows, cols] = k2_ref[3 * a + b]
            flip = 3 * (2 - a) + (2 - b)
            k2b_ref[rows, cols] = k2_ref[flip].astype(jnp.float32).T.astype(k2b_ref.dtype)
            k1b_ref[rows, cols] = k1_ref[flip].astype(jnp.float32).T.astype(k1b_ref.dtype)

    me = lax.axis_index("rows")
    size = lax.axis_size("rows")
    top = me > 0
    bottom = me < size - 1
    level = lt_ref[idx_ref[0]]
    scale = level[0:1, :] + 1.0
    shift = level[1:2, :]
    col = lax.broadcasted_iota(jnp.int32, (width, ch), 0)
    not_first = col > 0
    not_last = col < width - 1

    def combine(y):
        left = pltpu.roll(y[:, 0:ch], 1, 0)
        right = pltpu.roll(y[:, 2 * ch:3 * ch], width - 1, 0)
        return y[:, ch:2 * ch] + jnp.where(not_first, left, 0.0) + jnp.where(not_last, right, 0.0)

    def conv_row(ref, r, matrix_ref):
        rows = jnp.concatenate([ref[r], ref[r + 1], ref[r + 2]], axis=1)
        y = jnp.dot(rows, matrix_ref[...], preferred_element_type=jnp.float32)
        return combine(y)

    def shifted(g):
        g32 = g.astype(jnp.float32)
        g0 = jnp.where(not_last, pltpu.roll(g32, width - 1, 0), 0.0)
        g2 = jnp.where(not_first, pltpu.roll(g32, 1, 0), 0.0)
        return jnp.concatenate([g0.astype(g.dtype), g, g2.astype(g.dtype)], axis=1)

    for cp in copies:
        cp.wait()

    def phase_one(r, carry):
        lv0, lv1 = carry
        valid = jnp.logical_and(jnp.logical_or(r > 0, top), jnp.logical_or(r < count + 1, bottom))
        first = conv_row(x_ref, r, k1f_ref)
        mixed = first * scale + shift
        sig = 1.0 / (1.0 + jnp.exp(-mixed))
        hid_ref[r] = jnp.where(valid, mixed * sig, 0.0).astype(hid_ref.dtype)
        back_hidden = conv_row(c_ref, r, k2b_ref)
        back_mixed = back_hidden * (sig * (1.0 + mixed * (1.0 - sig)))
        bf_ref[r] = jnp.where(valid, back_mixed * scale, 0.0).astype(bf_ref.dtype)
        own = jnp.logical_and(r >= 1, r <= count)
        lv0 = lv0 + jnp.where(own, jnp.sum(back_mixed * first, axis=0, keepdims=True), 0.0)
        lv1 = lv1 + jnp.where(own, jnp.sum(back_mixed, axis=0, keepdims=True), 0.0)
        return lv0, lv1

    zero = jnp.zeros((1, ch), jnp.float32)
    lv0, lv1 = lax.fori_loop(0, count + 2, phase_one, (zero, zero))
    acc1[...] = jnp.zeros_like(acc1)
    acc2[...] = jnp.zeros_like(acc2)

    def phase_two(i, carry):
        out_ref[i] = (x_ref[i + 2].astype(jnp.float32) + conv_row(hid_ref, i, k2f_ref)).astype(out_ref.dtype)
        ig_ref[i] = (c_ref[i + 2].astype(jnp.float32) + conv_row(bf_ref, i, k1b_ref)).astype(ig_ref.dtype)
        xs = jnp.concatenate([x_ref[i + 1], x_ref[i + 2], x_ref[i + 3]], axis=1)
        gs = shifted(bf_ref[i + 1])
        acc1[...] += lax.dot_general(xs, gs, (((0,), (0,)), ((), ())), preferred_element_type=jnp.float32)
        hs = jnp.concatenate([hid_ref[i], hid_ref[i + 1], hid_ref[i + 2]], axis=1)
        cs = shifted(c_ref[i + 2])
        acc2[...] += lax.dot_general(hs, cs, (((0,), (0,)), ((), ())), preferred_element_type=jnp.float32)
        return carry

    lax.fori_loop(0, count, phase_two, 0)

    for a in range(3):
        for b in range(3):
            t = 3 * a + b
            blk = (slice(a * ch, (a + 1) * ch), slice(b * ch, (b + 1) * ch))
            grad_ref[t * ch : (t + 1) * ch, :] = acc1[blk] * norm
            grad_ref[(9 + t) * ch : (10 + t) * ch, :] = acc2[blk] * norm
    base = 18 * ch
    tail = grad_ref.shape[0] - base
    grad_ref[base:, :] = jnp.zeros((tail, ch), jnp.float32)
    grad_ref[base : base + 1, :] = lv0 * norm
    grad_ref[base + 1 : base + 2, :] = lv1 * norm


def section(norm, packed_rows, level_index, level_table, inputs, cotangent, before, after, k1, k2):
    count, width, ch = inputs.shape
    vmem = pltpu.MemorySpace.VMEM if hasattr(pltpu, "MemorySpace") else pltpu.VMEM
    spec = pl.BlockSpec(memory_space=vmem)
    anywhere = pl.BlockSpec(memory_space=pl.ANY)
    big = 3 * ch
    flops = 2 * (count + 2) * width * big * big * 2 + 4 * count * width * big * big * 2
    return pl.pallas_call(
        functools.partial(section_kernel, norm),
        out_shape=(
            jax.ShapeDtypeStruct((count, width, ch), jnp.bfloat16),
            jax.ShapeDtypeStruct((count, width, ch), jnp.bfloat16),
            jax.ShapeDtypeStruct((packed_rows, ch), jnp.float32),
        ),
        in_specs=[pl.BlockSpec(memory_space=pltpu.SMEM), spec] + [anywhere] * 4 + [spec] * 2,
        out_specs=(spec,) * 3,
        scratch_shapes=[
            pltpu.VMEM((count + 4, width, ch), jnp.bfloat16),
            pltpu.VMEM((count + 4, width, ch), jnp.bfloat16),
            pltpu.VMEM((count + 2, width, ch), jnp.bfloat16),
            pltpu.VMEM((count + 2, width, ch), jnp.bfloat16),
            pltpu.VMEM((big, big), jnp.bfloat16),
            pltpu.VMEM((big, big), jnp.bfloat16),
            pltpu.VMEM((big, big), jnp.bfloat16),
            pltpu.VMEM((big, big), jnp.bfloat16),
            pltpu.VMEM((big, big), jnp.float32),
            pltpu.VMEM((big, big), jnp.float32),
            pltpu.SemaphoreType.DMA((6,)),
        ],
        compiler_params=pltpu.CompilerParams(vmem_limit_bytes=60 * 1024 * 1024),
        cost_estimate=pl.CostEstimate(
            flops=flops, transcendentals=(count + 2) * width * ch, bytes_accessed=6 * count * width * ch
        ),
    )(level_index, level_table, inputs, cotangent, before, after, k1, k2)


def butterfly_sum(block):
    n = lax.axis_size("rows")
    me = lax.axis_index("rows")
    steps = []
    k = 1
    while k < n:
        steps.append(k)
        k *= 2
    if len(steps) > 2:
        steps = steps[:1] + steps[2:] + steps[1:2]
    piece = block
    for k in steps:
        half = piece.shape[0] // 2
        low = (me // k) % 2 == 0
        lo, hi = piece[:half], piece[half:]
        keep = jnp.where(low, lo, hi)
        send = jnp.where(low, hi, lo)
        got = lax.ppermute(send, "rows", [(i, i ^ k) for i in range(n)])
        piece = keep + got
    for k in reversed(steps):
        low = (me // k) % 2 == 0
        got = lax.ppermute(piece, "rows", [(i, i ^ k) for i in range(n)])
        piece = jnp.where(low, jnp.concatenate([piece, got]), jnp.concatenate([got, piece]))
    return piece


def local(inputs, cotangent, first_kernel, second_kernel, level_table, level_index):
    count = inputs.shape[0]
    width = inputs.shape[1]
    ch = inputs.shape[2]
    size = lax.axis_size("rows")
    total_rows = count * size
    norm = 1.0 / math.sqrt(total_rows * width)

    up = [(i, i + 1) for i in range(size - 1)]
    down = [(i + 1, i) for i in range(size - 1)]
    before = lax.ppermute(jnp.concatenate([inputs[-2:], cotangent[-2:]]), "rows", up)
    after = lax.ppermute(jnp.concatenate([inputs[:2], cotangent[:2]]), "rows", down)

    used = 18 * ch + 2
    packed_rows = used + (-used % size)
    outputs, input_grad, packed = section(
        norm, packed_rows, level_index, level_table, inputs, cotangent, before, after,
        first_kernel, second_kernel,
    )
    total = butterfly_sum(packed)
    first_sum = total[: 9 * ch].reshape(9, ch, ch)
    second_sum = total[9 * ch : 18 * ch].reshape(9, ch, ch)
    level_sum = total[18 * ch : 18 * ch + 2]
    return (outputs, input_grad, first_sum, second_sum, level_sum)


def solution(mesh):
    return jax.shard_map(
        local,
        mesh=mesh,
        in_specs=(
            P(("groups", "rows"), None, None),
            P(("groups", "rows"), None, None),
            P(),
            P(),
            P(),
            P("groups"),
        ),
        out_specs=(
            P(("groups", "rows"), None, None),
            P(("groups", "rows"), None, None),
            P("groups", None, None),
            P("groups", None, None),
            P("groups", None),
        ),
        check_vma=False,
    )
```

```python
import functools
import math

import jax
import jax.numpy as jnp
from jax import lax
from jax.experimental import pallas as pl
from jax.experimental.pallas import tpu as pltpu
from jax.sharding import PartitionSpec as P


def section_kernel(norm, idx_ref, lt_ref, x_hbm, c_hbm, before_hbm, after_hbm, k1_ref, k2_ref,
                   out_ref, ig_ref, grad_ref,
                   x_ref, c_ref, hid_ref, bf_ref, k1f_ref, k2f_ref, k2b_ref, k1b_ref, acc1, acc2, sems):
    count = out_ref.shape[0]
    width = out_ref.shape[1]
    ch = out_ref.shape[2]
    copies = [
        pltpu.make_async_copy(before_hbm.at[0:2], x_ref.at[0:2], sems.at[0]),
        pltpu.make_async_copy(x_hbm, x_ref.at[2 : count + 2], sems.at[1]),
        pltpu.make_async_copy(after_hbm.at[0:2], x_ref.at[count + 2 : count + 4], sems.at[2]),
        pltpu.make_async_copy(before_hbm.at[2:4], c_ref.at[0:2], sems.at[3]),
        pltpu.make_async_copy(c_hbm, c_ref.at[2 : count + 2], sems.at[4]),
        pltpu.make_async_copy(after_hbm.at[2:4], c_ref.at[count + 2 : count + 4], sems.at[5]),
    ]
    for cp in copies:
        cp.start()

    for a in range(3):
        for b in range(3):
            rows = slice(a * ch, (a + 1) * ch)
            cols = slice(b * ch, (b + 1) * ch)
            k1f_ref[rows, cols] = k1_ref[3 * a + b]
            k2f_ref[rows, cols] = k2_ref[3 * a + b]
            flip = 3 * (2 - a) + (2 - b)
            k2b_ref[rows, cols] = k2_ref[flip].astype(jnp.float32).T.astype(k2b_ref.dtype)
            k1b_ref[rows, cols] = k1_ref[flip].astype(jnp.float32).T.astype(k1b_ref.dtype)

    me = lax.axis_index("rows")
    size = lax.axis_size("rows")
    top = me > 0
    bottom = me < size - 1
    level = lt_ref[idx_ref[0]]
    scale = level[0:1, :] + 1.0
    shift = level[1:2, :]
    col = lax.broadcasted_iota(jnp.int32, (width, ch), 0)
    not_first = col > 0
    not_last = col < width - 1

    def combine(y):
        left = pltpu.roll(y[:, 0:ch], 1, 0)
        right = pltpu.roll(y[:, 2 * ch:3 * ch], width - 1, 0)
        return y[:, ch:2 * ch] + jnp.where(not_first, left, 0.0) + jnp.where(not_last, right, 0.0)

    def conv_row(ref, r, matrix_ref):
        rows = jnp.concatenate([ref[r], ref[r + 1], ref[r + 2]], axis=1)
        y = jnp.dot(rows, matrix_ref[...], preferred_element_type=jnp.float32)
        return combine(y)

    def shifted(g):
        g32 = g.astype(jnp.float32)
        g0 = jnp.where(not_last, pltpu.roll(g32, width - 1, 0), 0.0)
        g2 = jnp.where(not_first, pltpu.roll(g32, 1, 0), 0.0)
        return jnp.concatenate([g0.astype(g.dtype), g, g2.astype(g.dtype)], axis=1)

    for cp in copies:
        cp.wait()

    def phase_one(r, carry):
        lv0, lv1 = carry
        valid = jnp.logical_and(jnp.logical_or(r > 0, top), jnp.logical_or(r < count + 1, bottom))
        first = conv_row(x_ref, r, k1f_ref)
        mixed = first * scale + shift
        sig = 1.0 / (1.0 + jnp.exp(-mixed))
        hid_ref[r] = jnp.where(valid, mixed * sig, 0.0).astype(hid_ref.dtype)
        back_hidden = conv_row(c_ref, r, k2b_ref)
        back_mixed = back_hidden * (sig * (1.0 + mixed * (1.0 - sig)))
        bf_ref[r] = jnp.where(valid, back_mixed * scale, 0.0).astype(bf_ref.dtype)
        own = jnp.logical_and(r >= 1, r <= count)
        lv0 = lv0 + jnp.where(own, jnp.sum(back_mixed * first, axis=0, keepdims=True), 0.0)
        lv1 = lv1 + jnp.where(own, jnp.sum(back_mixed, axis=0, keepdims=True), 0.0)
        return lv0, lv1

    zero = jnp.zeros((1, ch), jnp.float32)
    lv0, lv1 = lax.fori_loop(0, count + 2, phase_one, (zero, zero))
    acc1[...] = jnp.zeros_like(acc1)
    acc2[...] = jnp.zeros_like(acc2)

    def phase_two(i, carry):
        out_ref[i] = (x_ref[i + 2].astype(jnp.float32) + conv_row(hid_ref, i, k2f_ref)).astype(out_ref.dtype)
        ig_ref[i] = (c_ref[i + 2].astype(jnp.float32) + conv_row(bf_ref, i, k1b_ref)).astype(ig_ref.dtype)
        xs = jnp.concatenate([x_ref[i + 1], x_ref[i + 2], x_ref[i + 3]], axis=1)
        gs = shifted(bf_ref[i + 1])
        acc1[...] += lax.dot_general(xs, gs, (((0,), (0,)), ((), ())), preferred_element_type=jnp.float32)
        hs = jnp.concatenate([hid_ref[i], hid_ref[i + 1], hid_ref[i + 2]], axis=1)
        cs = shifted(c_ref[i + 2])
        acc2[...] += lax.dot_general(hs, cs, (((0,), (0,)), ((), ())), preferred_element_type=jnp.float32)
        return carry

    lax.fori_loop(0, count, phase_two, 0)

    for a in range(3):
        for b in range(3):
            t = 3 * a + b
            blk = (slice(a * ch, (a + 1) * ch), slice(b * ch, (b + 1) * ch))
            grad_ref[t * ch : (t + 1) * ch, :] = acc1[blk] * norm
            grad_ref[(9 + t) * ch : (10 + t) * ch, :] = acc2[blk] * norm
    base = 18 * ch
    tail = grad_ref.shape[0] - base
    grad_ref[base:, :] = jnp.zeros((tail, ch), jnp.float32)
    grad_ref[base : base + 1, :] = lv0 * norm
    grad_ref[base + 1 : base + 2, :] = lv1 * norm


def section(norm, packed_rows, level_index, level_table, inputs, cotangent, before, after, k1, k2):
    count, width, ch = inputs.shape
    vmem = pltpu.MemorySpace.VMEM if hasattr(pltpu, "MemorySpace") else pltpu.VMEM
    spec = pl.BlockSpec(memory_space=vmem)
    anywhere = pl.BlockSpec(memory_space=pl.ANY)
    big = 3 * ch
    flops = 2 * (count + 2) * width * big * big * 2 + 4 * count * width * big * big * 2
    return pl.pallas_call(
        functools.partial(section_kernel, norm),
        out_shape=(
            jax.ShapeDtypeStruct((count, width, ch), jnp.bfloat16),
            jax.ShapeDtypeStruct((count, width, ch), jnp.bfloat16),
            jax.ShapeDtypeStruct((packed_rows, ch), jnp.float32),
        ),
        in_specs=[pl.BlockSpec(memory_space=pltpu.SMEM), spec] + [anywhere] * 4 + [spec] * 2,
        out_specs=(spec,) * 3,
        scratch_shapes=[
            pltpu.VMEM((count + 4, width, ch), jnp.bfloat16),
            pltpu.VMEM((count + 4, width, ch), jnp.bfloat16),
            pltpu.VMEM((count + 2, width, ch), jnp.bfloat16),
            pltpu.VMEM((count + 2, width, ch), jnp.bfloat16),
            pltpu.VMEM((big, big), jnp.bfloat16),
            pltpu.VMEM((big, big), jnp.bfloat16),
            pltpu.VMEM((big, big), jnp.bfloat16),
            pltpu.VMEM((big, big), jnp.bfloat16),
            pltpu.VMEM((big, big), jnp.float32),
            pltpu.VMEM((big, big), jnp.float32),
            pltpu.SemaphoreType.DMA((6,)),
        ],
        compiler_params=pltpu.CompilerParams(vmem_limit_bytes=60 * 1024 * 1024),
        cost_estimate=pl.CostEstimate(
            flops=flops, transcendentals=(count + 2) * width * ch, bytes_accessed=6 * count * width * ch
        ),
    )(level_index, level_table, inputs, cotangent, before, after, k1, k2)


def butterfly_sum(block):
    n = lax.axis_size("rows")
    me = lax.axis_index("rows")
    bits = []
    k = 1
    while k < n:
        bits.append(k)
        k *= 2
    other = list(bits)
    if len(bits) > 2:
        other[1], other[2] = bits[2], bits[1]
    orders = list(zip(bits, other))
    even = me % 2 == 0

    def step_of(k0, k1):
        perm = [(i, i ^ (k0 if i % 2 == 0 else k1)) for i in range(n)]
        low = jnp.where(even, (me // k0) % 2, (me // k1) % 2) == 0
        return perm, low

    piece = block
    for k0, k1 in orders:
        perm, low = step_of(k0, k1)
        half = piece.shape[0] // 2
        lo, hi = piece[:half], piece[half:]
        keep = jnp.where(low, lo, hi)
        send = jnp.where(low, hi, lo)
        got = lax.ppermute(send, "rows", perm)
        piece = keep + got
    for k0, k1 in reversed(orders):
        perm, low = step_of(k0, k1)
        got = lax.ppermute(piece, "rows", perm)
        piece = jnp.where(low, jnp.concatenate([piece, got]), jnp.concatenate([got, piece]))
    return piece


def local(inputs, cotangent, first_kernel, second_kernel, level_table, level_index):
    count = inputs.shape[0]
    width = inputs.shape[1]
    ch = inputs.shape[2]
    size = lax.axis_size("rows")
    total_rows = count * size
    norm = 1.0 / math.sqrt(total_rows * width)

    up = [(i, i + 1) for i in range(size - 1)]
    down = [(i + 1, i) for i in range(size - 1)]
    before = lax.ppermute(jnp.concatenate([inputs[-2:], cotangent[-2:]]), "rows", up)
    after = lax.ppermute(jnp.concatenate([inputs[:2], cotangent[:2]]), "rows", down)

    used = 18 * ch + 2
    packed_rows = used + (-used % size)
    outputs, input_grad, packed = section(
        norm, packed_rows, level_index, level_table, inputs, cotangent, before, after,
        first_kernel, second_kernel,
    )
    total = butterfly_sum(packed)
    first_sum = total[: 9 * ch].reshape(9, ch, ch)
    second_sum = total[9 * ch : 18 * ch].reshape(9, ch, ch)
    level_sum = total[18 * ch : 18 * ch + 2]
    return (outputs, input_grad, first_sum, second_sum, level_sum)


def solution(mesh):
    return jax.shard_map(
        local,
        mesh=mesh,
        in_specs=(
            P(("groups", "rows"), None, None),
            P(("groups", "rows"), None, None),
            P(),
            P(),
            P(),
            P("groups"),
        ),
        out_specs=(
            P(("groups", "rows"), None, None),
            P(("groups", "rows"), None, None),
            P("groups", None, None),
            P("groups", None, None),
            P("groups", None),
        ),
        check_vma=False,
    )
```

```python
import functools
import math

import jax
import jax.numpy as jnp
from jax import lax
from jax.experimental import pallas as pl
from jax.experimental.pallas import tpu as pltpu
from jax.sharding import PartitionSpec as P


def section_kernel(norm, idx_ref, lt_ref, x_hbm, c_hbm, before_hbm, after_hbm, k1_ref, k2_ref,
                   out_ref, ig_ref, grad_ref,
                   x_ref, c_ref, hid_ref, bf_ref, xt_ref, hidt_ref, k1f_ref, k2f_ref, k2b_ref, k1b_ref, acc1, acc2, sems):
    count = out_ref.shape[0]
    width = out_ref.shape[1]
    ch = out_ref.shape[2]
    copies = [
        pltpu.make_async_copy(before_hbm.at[0:2], x_ref.at[0:2], sems.at[0]),
        pltpu.make_async_copy(x_hbm, x_ref.at[2 : count + 2], sems.at[1]),
        pltpu.make_async_copy(after_hbm.at[0:2], x_ref.at[count + 2 : count + 4], sems.at[2]),
        pltpu.make_async_copy(before_hbm.at[2:4], c_ref.at[0:2], sems.at[3]),
        pltpu.make_async_copy(c_hbm, c_ref.at[2 : count + 2], sems.at[4]),
        pltpu.make_async_copy(after_hbm.at[2:4], c_ref.at[count + 2 : count + 4], sems.at[5]),
    ]
    for cp in copies:
        cp.start()

    for a in range(3):
        for b in range(3):
            rows = slice(a * ch, (a + 1) * ch)
            cols = slice(b * ch, (b + 1) * ch)
            k1f_ref[rows, cols] = k1_ref[3 * a + b]
            k2f_ref[rows, cols] = k2_ref[3 * a + b]
            flip = 3 * (2 - a) + (2 - b)
            k2b_ref[rows, cols] = k2_ref[flip].astype(jnp.float32).T.astype(k2b_ref.dtype)
            k1b_ref[rows, cols] = k1_ref[flip].astype(jnp.float32).T.astype(k1b_ref.dtype)

    me = lax.axis_index("rows")
    size = lax.axis_size("rows")
    top = me > 0
    bottom = me < size - 1
    level = lt_ref[idx_ref[0]]
    scale = level[0:1, :] + 1.0
    shift = level[1:2, :]
    col = lax.broadcasted_iota(jnp.int32, (width, ch), 0)
    not_first = col > 0
    not_last = col < width - 1

    def combine(y):
        left = pltpu.roll(y[:, 0:ch], 1, 0)
        right = pltpu.roll(y[:, 2 * ch:3 * ch], width - 1, 0)
        return y[:, ch:2 * ch] + jnp.where(not_first, left, 0.0) + jnp.where(not_last, right, 0.0)

    def conv_row(ref, r, matrix_ref):
        rows = jnp.concatenate([ref[r], ref[r + 1], ref[r + 2]], axis=1)
        y = jnp.dot(rows, matrix_ref[...], preferred_element_type=jnp.float32)
        return combine(y)

    def shifted(g):
        g32 = g.astype(jnp.float32)
        g0 = jnp.where(not_last, pltpu.roll(g32, width - 1, 0), 0.0)
        g2 = jnp.where(not_first, pltpu.roll(g32, 1, 0), 0.0)
        return jnp.concatenate([g0.astype(g.dtype), g, g2.astype(g.dtype)], axis=1)

    for cp in copies:
        cp.wait()

    def phase_one(r, carry):
        lv0, lv1 = carry
        valid = jnp.logical_and(jnp.logical_or(r > 0, top), jnp.logical_or(r < count + 1, bottom))
        first = conv_row(x_ref, r, k1f_ref)
        mixed = first * scale + shift
        sig = 0.5 + 0.5 * jnp.tanh(0.5 * mixed)
        hidden = jnp.where(valid, mixed * sig, 0.0)
        hid_ref[r] = hidden.astype(hid_ref.dtype)
        hidt_ref[r] = hidden.T.astype(hidt_ref.dtype)
        back_hidden = conv_row(c_ref, r, k2b_ref)
        back_mixed = back_hidden * (sig * (1.0 + mixed * (1.0 - sig)))
        bf_ref[r] = jnp.where(valid, back_mixed * scale, 0.0).astype(bf_ref.dtype)
        own = jnp.logical_and(r >= 1, r <= count)
        lv0 = lv0 + jnp.where(own, jnp.sum(back_mixed * first, axis=0, keepdims=True), 0.0)
        lv1 = lv1 + jnp.where(own, jnp.sum(back_mixed, axis=0, keepdims=True), 0.0)
        return lv0, lv1

    zero = jnp.zeros((1, ch), jnp.float32)
    lv0, lv1 = lax.fori_loop(0, count + 2, phase_one, (zero, zero))

    def transpose_rows(r, carry):
        xt_ref[r] = x_ref[r].astype(jnp.float32).T.astype(xt_ref.dtype)
        return carry

    lax.fori_loop(1, count + 3, transpose_rows, 0)
    acc1[...] = jnp.zeros_like(acc1)
    acc2[...] = jnp.zeros_like(acc2)

    def phase_two(i, carry):
        out_ref[i] = (x_ref[i + 2].astype(jnp.float32) + conv_row(hid_ref, i, k2f_ref)).astype(out_ref.dtype)
        ig_ref[i] = (c_ref[i + 2].astype(jnp.float32) + conv_row(bf_ref, i, k1b_ref)).astype(ig_ref.dtype)
        xs = jnp.concatenate([xt_ref[i + 1], xt_ref[i + 2], xt_ref[i + 3]], axis=0)
        gs = shifted(bf_ref[i + 1])
        acc1[...] += jnp.dot(xs, gs, preferred_element_type=jnp.float32)
        hs = jnp.concatenate([hidt_ref[i], hidt_ref[i + 1], hidt_ref[i + 2]], axis=0)
        cs = shifted(c_ref[i + 2])
        acc2[...] += jnp.dot(hs, cs, preferred_element_type=jnp.float32)
        return carry

    lax.fori_loop(0, count, phase_two, 0)

    for a in range(3):
        for b in range(3):
            t = 3 * a + b
            blk = (slice(a * ch, (a + 1) * ch), slice(b * ch, (b + 1) * ch))
            grad_ref[t * ch : (t + 1) * ch, :] = acc1[blk] * norm
            grad_ref[(9 + t) * ch : (10 + t) * ch, :] = acc2[blk] * norm
    base = 18 * ch
    tail = grad_ref.shape[0] - base
    grad_ref[base:, :] = jnp.zeros((tail, ch), jnp.float32)
    grad_ref[base : base + 1, :] = lv0 * norm
    grad_ref[base + 1 : base + 2, :] = lv1 * norm


def section(norm, packed_rows, level_index, level_table, inputs, cotangent, before, after, k1, k2):
    count, width, ch = inputs.shape
    vmem = pltpu.MemorySpace.VMEM if hasattr(pltpu, "MemorySpace") else pltpu.VMEM
    spec = pl.BlockSpec(memory_space=vmem)
    anywhere = pl.BlockSpec(memory_space=pl.ANY)
    big = 3 * ch
    flops = 2 * (count + 2) * width * big * big * 2 + 4 * count * width * big * big * 2
    return pl.pallas_call(
        functools.partial(section_kernel, norm),
        out_shape=(
            jax.ShapeDtypeStruct((count, width, ch), jnp.bfloat16),
            jax.ShapeDtypeStruct((count, width, ch), jnp.bfloat16),
            jax.ShapeDtypeStruct((packed_rows, ch), jnp.float32),
        ),
        in_specs=[pl.BlockSpec(memory_space=pltpu.SMEM), spec] + [anywhere] * 4 + [spec] * 2,
        out_specs=(spec,) * 3,
        scratch_shapes=[
            pltpu.VMEM((count + 4, width, ch), jnp.bfloat16),
            pltpu.VMEM((count + 4, width, ch), jnp.bfloat16),
            pltpu.VMEM((count + 2, width, ch), jnp.bfloat16),
            pltpu.VMEM((count + 2, width, ch), jnp.bfloat16),
            pltpu.VMEM((count + 4, ch, width), jnp.bfloat16),
            pltpu.VMEM((count + 2, ch, width), jnp.bfloat16),
            pltpu.VMEM((big, big), jnp.bfloat16),
            pltpu.VMEM((big, big), jnp.bfloat16),
            pltpu.VMEM((big, big), jnp.bfloat16),
            pltpu.VMEM((big, big), jnp.bfloat16),
            pltpu.VMEM((big, big), jnp.float32),
            pltpu.VMEM((big, big), jnp.float32),
            pltpu.SemaphoreType.DMA((6,)),
        ],
        compiler_params=pltpu.CompilerParams(vmem_limit_bytes=60 * 1024 * 1024),
        cost_estimate=pl.CostEstimate(
            flops=flops, transcendentals=(count + 2) * width * ch, bytes_accessed=6 * count * width * ch
        ),
    )(level_index, level_table, inputs, cotangent, before, after, k1, k2)


def butterfly_sum(block):
    n = lax.axis_size("rows")
    me = lax.axis_index("rows")
    bits = []
    k = 1
    while k < n:
        bits.append(k)
        k *= 2
    other = list(bits)
    if len(bits) > 2:
        other[1], other[2] = bits[2], bits[1]
    orders = list(zip(bits, other))
    even = me % 2 == 0

    def step_of(k0, k1):
        perm = [(i, i ^ (k0 if i % 2 == 0 else k1)) for i in range(n)]
        low = jnp.where(even, (me // k0) % 2, (me // k1) % 2) == 0
        return perm, low

    piece = block
    for k0, k1 in orders:
        perm, low = step_of(k0, k1)
        half = piece.shape[0] // 2
        lo, hi = piece[:half], piece[half:]
        keep = jnp.where(low, lo, hi)
        send = jnp.where(low, hi, lo)
        got = lax.ppermute(send, "rows", perm)
        piece = keep + got
    for k0, k1 in reversed(orders):
        perm, low = step_of(k0, k1)
        got = lax.ppermute(piece, "rows", perm)
        piece = jnp.where(low, jnp.concatenate([piece, got]), jnp.concatenate([got, piece]))
    return piece


def local(inputs, cotangent, first_kernel, second_kernel, level_table, level_index):
    count = inputs.shape[0]
    width = inputs.shape[1]
    ch = inputs.shape[2]
    size = lax.axis_size("rows")
    total_rows = count * size
    norm = 1.0 / math.sqrt(total_rows * width)

    up = [(i, i + 1) for i in range(size - 1)]
    down = [(i + 1, i) for i in range(size - 1)]
    before = lax.ppermute(jnp.concatenate([inputs[-2:], cotangent[-2:]]), "rows", up)
    after = lax.ppermute(jnp.concatenate([inputs[:2], cotangent[:2]]), "rows", down)

    used = 18 * ch + 2
    packed_rows = used + (-used % size)
    outputs, input_grad, packed = section(
        norm, packed_rows, level_index, level_table, inputs, cotangent, before, after,
        first_kernel, second_kernel,
    )
    total = butterfly_sum(packed)
    first_sum = total[: 9 * ch].reshape(9, ch, ch)
    second_sum = total[9 * ch : 18 * ch].reshape(9, ch, ch)
    level_sum = total[18 * ch : 18 * ch + 2]
    return (outputs, input_grad, first_sum, second_sum, level_sum)


def solution(mesh):
    return jax.shard_map(
        local,
        mesh=mesh,
        in_specs=(
            P(("groups", "rows"), None, None),
            P(("groups", "rows"), None, None),
            P(),
            P(),
            P(),
            P("groups"),
        ),
        out_specs=(
            P(("groups", "rows"), None, None),
            P(("groups", "rows"), None, None),
            P("groups", None, None),
            P("groups", None, None),
            P("groups", None),
        ),
        check_vma=False,
    )
```

```python
import functools
import math

import jax
import jax.numpy as jnp
from jax import lax
from jax.experimental import pallas as pl
from jax.experimental.pallas import tpu as pltpu
from jax.sharding import PartitionSpec as P


def row_ops(width, ch, scale, shift, top, bottom, count):
    col = lax.broadcasted_iota(jnp.int32, (width, ch), 0)
    not_first = col > 0
    not_last = col < width - 1

    def combine(y):
        left = pltpu.roll(y[:, 0:ch], 1, 0)
        right = pltpu.roll(y[:, 2 * ch:3 * ch], width - 1, 0)
        return y[:, ch:2 * ch] + jnp.where(not_first, left, 0.0) + jnp.where(not_last, right, 0.0)

    def conv_row(ref, r, matrix_ref):
        rows = jnp.concatenate([ref[r], ref[r + 1], ref[r + 2]], axis=1)
        y = jnp.dot(rows, matrix_ref[...], preferred_element_type=jnp.float32)
        return combine(y)

    def shifted(g):
        g32 = g.astype(jnp.float32)
        g0 = jnp.where(not_last, pltpu.roll(g32, width - 1, 0), 0.0)
        g2 = jnp.where(not_first, pltpu.roll(g32, 1, 0), 0.0)
        return jnp.concatenate([g0.astype(g.dtype), g, g2.astype(g.dtype)], axis=1)

    def phase_one(r, x_ref, c_ref, hid_ref, hidt_ref, bf_ref, k1f_ref, k2b_ref, carry):
        lv0, lv1 = carry
        valid = jnp.logical_and(jnp.logical_or(r > 0, top), jnp.logical_or(r < count + 1, bottom))
        first = conv_row(x_ref, r, k1f_ref)
        mixed = first * scale + shift
        sig = 0.5 + 0.5 * jnp.tanh(0.5 * mixed)
        hidden = jnp.where(valid, mixed * sig, 0.0)
        hid_ref[r] = hidden.astype(hid_ref.dtype)
        hidt_ref[r] = hidden.T.astype(hidt_ref.dtype)
        back_hidden = conv_row(c_ref, r, k2b_ref)
        back_mixed = back_hidden * (sig * (1.0 + mixed * (1.0 - sig)))
        bf_ref[r] = jnp.where(valid, back_mixed * scale, 0.0).astype(bf_ref.dtype)
        own = jnp.logical_and(r >= 1, r <= count)
        lv0 = lv0 + jnp.where(own, jnp.sum(back_mixed * first, axis=0, keepdims=True), 0.0)
        lv1 = lv1 + jnp.where(own, jnp.sum(back_mixed, axis=0, keepdims=True), 0.0)
        return lv0, lv1

    def out_row(i, x_ref, c_ref, hid_ref, bf_ref, k2f_ref, k1b_ref, out_ref, ig_ref):
        out_ref[i] = (x_ref[i + 2].astype(jnp.float32) + conv_row(hid_ref, i, k2f_ref)).astype(out_ref.dtype)
        ig_ref[i] = (c_ref[i + 2].astype(jnp.float32) + conv_row(bf_ref, i, k1b_ref)).astype(ig_ref.dtype)

    def g1_row(i, xt_ref, bf_ref, acc1):
        xs = jnp.concatenate([xt_ref[i + 1], xt_ref[i + 2], xt_ref[i + 3]], axis=0)
        acc1[...] += jnp.dot(xs, shifted(bf_ref[i + 1]), preferred_element_type=jnp.float32)

    def g2_row(i, hidt_ref, c_ref, acc2):
        hs = jnp.concatenate([hidt_ref[i], hidt_ref[i + 1], hidt_ref[i + 2]], axis=0)
        acc2[...] += jnp.dot(hs, shifted(c_ref[i + 2]), preferred_element_type=jnp.float32)

    return phase_one, out_row, g1_row, g2_row


def level_and_edges(idx_ref, lt_ref):
    me = lax.axis_index("rows")
    size = lax.axis_size("rows")
    level = lt_ref[idx_ref[0]]
    return level[0:1, :] + 1.0, level[1:2, :], me > 0, me < size - 1


def interior_kernel(idx_ref, lt_ref, x_hbm, c_hbm, k1_ref, k2_ref,
                    out_ref, ig_ref, hid_ref, bf_ref, hidt_ref, acc1, acc2, lv_ref, mats_ref,
                    x_ref, c_ref, xt_ref, sems):
    count, width, ch = out_ref.shape
    copies = [
        pltpu.make_async_copy(x_hbm, x_ref.at[2 : count + 2], sems.at[0]),
        pltpu.make_async_copy(c_hbm, c_ref.at[2 : count + 2], sems.at[1]),
    ]
    for cp in copies:
        cp.start()
    for a in range(3):
        for b in range(3):
            rows = slice(a * ch, (a + 1) * ch)
            cols = slice(b * ch, (b + 1) * ch)
            flip = 3 * (2 - a) + (2 - b)
            mats_ref[0, rows, cols] = k1_ref[3 * a + b]
            mats_ref[1, rows, cols] = k2_ref[3 * a + b]
            mats_ref[2, rows, cols] = k2_ref[flip].astype(jnp.float32).T.astype(mats_ref.dtype)
            mats_ref[3, rows, cols] = k1_ref[flip].astype(jnp.float32).T.astype(mats_ref.dtype)
    scale, shift, top, bottom = level_and_edges(idx_ref, lt_ref)
    phase_one, out_row, g1_row, g2_row = row_ops(width, ch, scale, shift, top, bottom, count)
    k1f, k2f, k2b, k1b = (mats_ref.at[t] for t in range(4))
    for cp in copies:
        cp.wait()

    zero = jnp.zeros((1, ch), jnp.float32)
    lv0, lv1 = lax.fori_loop(
        2, count, lambda r, cr: phase_one(r, x_ref, c_ref, hid_ref, hidt_ref, bf_ref, k1f, k2b, cr), (zero, zero)
    )
    lv_ref[0:1, :] = lv0
    lv_ref[1:2, :] = lv1

    def transpose_rows(r, carry):
        xt_ref[r] = x_ref[r].astype(jnp.float32).T.astype(xt_ref.dtype)
        return carry

    lax.fori_loop(2, count + 2, transpose_rows, 0)
    acc1[...] = jnp.zeros_like(acc1)
    acc2[...] = jnp.zeros_like(acc2)

    def middle(i, carry):
        out_row(i, x_ref, c_ref, hid_ref, bf_ref, k2f, k1b, out_ref, ig_ref)
        g2_row(i, hidt_ref, c_ref, acc2)
        return carry

    lax.fori_loop(2, count - 2, middle, 0)

    def g1_middle(i, carry):
        g1_row(i, xt_ref, bf_ref, acc1)
        return carry

    lax.fori_loop(1, count - 1, g1_middle, 0)


def edge_kernel(norm, idx_ref, lt_ref, x_hbm, c_hbm, before_hbm, after_hbm, hida_hbm, bfa_hbm, hidta_hbm,
                acc1a_ref, acc2a_ref, lva_ref, mats_ref, outa_ref, iga_ref,
                out_ref, ig_ref, grad_ref,
                x_ref, c_ref, hid_ref, bf_ref, hidt_ref, xt_ref, acc1, acc2, sems):
    count, width, ch = out_ref.shape
    out_ref[2 : count - 2] = outa_ref[2 : count - 2]
    ig_ref[2 : count - 2] = iga_ref[2 : count - 2]
    copies = [
        pltpu.make_async_copy(before_hbm.at[0:2], x_ref.at[0:2], sems.at[0]),
        pltpu.make_async_copy(x_hbm, x_ref.at[2 : count + 2], sems.at[1]),
        pltpu.make_async_copy(after_hbm.at[0:2], x_ref.at[count + 2 : count + 4], sems.at[2]),
        pltpu.make_async_copy(before_hbm.at[2:4], c_ref.at[0:2], sems.at[3]),
        pltpu.make_async_copy(c_hbm, c_ref.at[2 : count + 2], sems.at[4]),
        pltpu.make_async_copy(after_hbm.at[2:4], c_ref.at[count + 2 : count + 4], sems.at[5]),
        pltpu.make_async_copy(hida_hbm, hid_ref, sems.at[6]),
        pltpu.make_async_copy(bfa_hbm, bf_ref, sems.at[7]),
        pltpu.make_async_copy(hidta_hbm, hidt_ref, sems.at[8]),
    ]
    for cp in copies:
        cp.start()
    scale, shift, top, bottom = level_and_edges(idx_ref, lt_ref)
    phase_one, out_row, g1_row, g2_row = row_ops(width, ch, scale, shift, top, bottom, count)
    k1f, k2f, k2b, k1b = (mats_ref.at[t] for t in range(4))
    acc1[...] = acc1a_ref[...]
    acc2[...] = acc2a_ref[...]
    for cp in copies:
        cp.wait()

    carry = (lva_ref[0:1, :], lva_ref[1:2, :])
    for r in (0, 1, count, count + 1):
        carry = phase_one(r, x_ref, c_ref, hid_ref, hidt_ref, bf_ref, k1f, k2b, carry)
    lv0, lv1 = carry
    for r in (1, 2, 3, count, count + 1, count + 2):
        xt_ref[r] = x_ref[r].astype(jnp.float32).T.astype(xt_ref.dtype)
    for i in (0, 1, count - 2, count - 1):
        out_row(i, x_ref, c_ref, hid_ref, bf_ref, k2f, k1b, out_ref, ig_ref)
        g2_row(i, hidt_ref, c_ref, acc2)
    for i in (0, count - 1):
        g1_row(i, xt_ref, bf_ref, acc1)

    for a in range(3):
        for b in range(3):
            t = 3 * a + b
            blk = (slice(a * ch, (a + 1) * ch), slice(b * ch, (b + 1) * ch))
            grad_ref[t * ch : (t + 1) * ch, :] = acc1[blk] * norm
            grad_ref[(9 + t) * ch : (10 + t) * ch, :] = acc2[blk] * norm
    base = 18 * ch
    tail = grad_ref.shape[0] - base
    grad_ref[base:, :] = jnp.zeros((tail, ch), jnp.float32)
    grad_ref[base : base + 1, :] = lv0 * norm
    grad_ref[base + 1 : base + 2, :] = lv1 * norm


def section(norm, packed_rows, level_index, level_table, inputs, cotangent, before_fn, k1, k2):
    count, width, ch = inputs.shape
    vmem = pltpu.MemorySpace.VMEM if hasattr(pltpu, "MemorySpace") else pltpu.VMEM
    spec = pl.BlockSpec(memory_space=vmem)
    anywhere = pl.BlockSpec(memory_space=pl.ANY)
    smem = pl.BlockSpec(memory_space=pltpu.SMEM)
    big = 3 * ch
    unit = width * big * big * 2
    field = jax.ShapeDtypeStruct((count, width, ch), jnp.bfloat16)
    frame = jax.ShapeDtypeStruct((count + 2, width, ch), jnp.bfloat16)
    frame_t = jax.ShapeDtypeStruct((count + 2, ch, width), jnp.bfloat16)
    square = jax.ShapeDtypeStruct((big, big), jnp.float32)
    params = pltpu.CompilerParams(vmem_limit_bytes=60 * 1024 * 1024)
    out, ig, hid, bf, hidt, acc1, acc2, lv, mats = pl.pallas_call(
        interior_kernel,
        out_shape=(field, field, frame, frame, frame_t, square, square,
                   jax.ShapeDtypeStruct((2, ch), jnp.float32), jax.ShapeDtypeStruct((4, big, big), jnp.bfloat16)),
        in_specs=[smem, spec, anywhere, anywhere, spec, spec],
        out_specs=(spec,) * 9,
        scratch_shapes=[
            pltpu.VMEM((count + 4, width, ch), jnp.bfloat16),
            pltpu.VMEM((count + 4, width, ch), jnp.bfloat16),
            pltpu.VMEM((count + 4, ch, width), jnp.bfloat16),
            pltpu.SemaphoreType.DMA((2,)),
        ],
        compiler_params=params,
        cost_estimate=pl.CostEstimate(
            flops=(5 * count - 8) * unit, transcendentals=count * width * ch, bytes_accessed=8 * count * width * ch
        ),
    )(level_index, level_table, inputs, cotangent, k1, k2)
    before, after = before_fn()
    return pl.pallas_call(
        functools.partial(edge_kernel, norm),
        out_shape=(field, field, jax.ShapeDtypeStruct((packed_rows, ch), jnp.float32)),
        in_specs=[smem, spec] + [anywhere] * 7 + [spec] * 6,
        out_specs=(spec,) * 3,
        scratch_shapes=[
            pltpu.VMEM((count + 4, width, ch), jnp.bfloat16),
            pltpu.VMEM((count + 4, width, ch), jnp.bfloat16),
            pltpu.VMEM((count + 2, width, ch), jnp.bfloat16),
            pltpu.VMEM((count + 2, width, ch), jnp.bfloat16),
            pltpu.VMEM((count + 2, ch, width), jnp.bfloat16),
            pltpu.VMEM((count + 4, ch, width), jnp.bfloat16),
            pltpu.VMEM((big, big), jnp.float32),
            pltpu.VMEM((big, big), jnp.float32),
            pltpu.SemaphoreType.DMA((9,)),
        ],
        compiler_params=params,
        cost_estimate=pl.CostEstimate(
            flops=22 * unit, transcendentals=4 * width * ch, bytes_accessed=10 * count * width * ch
        ),
    )(level_index, level_table, inputs, cotangent, before, after, hid, bf, hidt, acc1, acc2, lv, mats, out, ig)


def butterfly_sum(block):
    n = lax.axis_size("rows")
    me = lax.axis_index("rows")
    bits = []
    k = 1
    while k < n:
        bits.append(k)
        k *= 2
    other = list(bits)
    if len(bits) > 2:
        other[1], other[2] = bits[2], bits[1]
    orders = list(zip(bits, other))
    even = me % 2 == 0

    def step_of(k0, k1):
        perm = [(i, i ^ (k0 if i % 2 == 0 else k1)) for i in range(n)]
        low = jnp.where(even, (me // k0) % 2, (me // k1) % 2) == 0
        return perm, low

    piece = block
    for k0, k1 in orders:
        perm, low = step_of(k0, k1)
        half = piece.shape[0] // 2
        lo, hi = piece[:half], piece[half:]
        keep = jnp.where(low, lo, hi)
        send = jnp.where(low, hi, lo)
        got = lax.ppermute(send, "rows", perm)
        piece = keep + got
    for k0, k1 in reversed(orders):
        perm, low = step_of(k0, k1)
        got = lax.ppermute(piece, "rows", perm)
        piece = jnp.where(low, jnp.concatenate([piece, got]), jnp.concatenate([got, piece]))
    return piece


def local(inputs, cotangent, first_kernel, second_kernel, level_table, level_index):
    count = inputs.shape[0]
    width = inputs.shape[1]
    ch = inputs.shape[2]
    size = lax.axis_size("rows")
    total_rows = count * size
    norm = 1.0 / math.sqrt(total_rows * width)

    up = [(i, i + 1) for i in range(size - 1)]
    down = [(i + 1, i) for i in range(size - 1)]
    before = lax.ppermute(jnp.concatenate([inputs[-2:], cotangent[-2:]]), "rows", up)
    after = lax.ppermute(jnp.concatenate([inputs[:2], cotangent[:2]]), "rows", down)
    halo = lambda: (before, after)

    used = 18 * ch + 2
    packed_rows = used + (-used % size)
    outputs, input_grad, packed = section(
        norm, packed_rows, level_index, level_table, inputs, cotangent, halo,
        first_kernel, second_kernel,
    )
    total = butterfly_sum(packed)
    first_sum = total[: 9 * ch].reshape(9, ch, ch)
    second_sum = total[9 * ch : 18 * ch].reshape(9, ch, ch)
    level_sum = total[18 * ch : 18 * ch + 2]
    return (outputs, input_grad, first_sum, second_sum, level_sum)


def solution(mesh):
    return jax.shard_map(
        local,
        mesh=mesh,
        in_specs=(
            P(("groups", "rows"), None, None),
            P(("groups", "rows"), None, None),
            P(),
            P(),
            P(),
            P("groups"),
        ),
        out_specs=(
            P(("groups", "rows"), None, None),
            P(("groups", "rows"), None, None),
            P("groups", None, None),
            P("groups", None, None),
            P("groups", None),
        ),
        check_vma=False,
    )
```

```python
import functools
import math

import jax
import jax.numpy as jnp
from jax import lax
from jax.experimental import pallas as pl
from jax.experimental.pallas import tpu as pltpu
from jax.sharding import PartitionSpec as P


def row_ops(width, ch, scale, shift, top, bottom, count):
    col = lax.broadcasted_iota(jnp.int32, (width, ch), 0)
    not_first = col > 0
    not_last = col < width - 1

    def combine(y):
        left = pltpu.roll(y[:, 0:ch], 1, 0)
        right = pltpu.roll(y[:, 2 * ch:3 * ch], width - 1, 0)
        return y[:, ch:2 * ch] + jnp.where(not_first, left, 0.0) + jnp.where(not_last, right, 0.0)

    def conv_row(ref, r, matrix_ref):
        rows = jnp.concatenate([ref[r], ref[r + 1], ref[r + 2]], axis=1)
        y = jnp.dot(rows, matrix_ref[...], preferred_element_type=jnp.float32)
        return combine(y)

    def shifted(g):
        g32 = g.astype(jnp.float32)
        g0 = jnp.where(not_last, pltpu.roll(g32, width - 1, 0), 0.0)
        g2 = jnp.where(not_first, pltpu.roll(g32, 1, 0), 0.0)
        return jnp.concatenate([g0.astype(g.dtype), g, g2.astype(g.dtype)], axis=1)

    def phase_one(r, x_ref, c_ref, hid_ref, hidt_ref, bf_ref, k1f_ref, k2b_ref, carry):
        lv0, lv1 = carry
        valid = jnp.logical_and(jnp.logical_or(r > 0, top), jnp.logical_or(r < count + 1, bottom))
        first = conv_row(x_ref, r, k1f_ref)
        mixed = first * scale + shift
        sig = 0.5 + 0.5 * jnp.tanh(0.5 * mixed)
        hidden = jnp.where(valid, mixed * sig, 0.0)
        hid_ref[r] = hidden.astype(hid_ref.dtype)
        hidt_ref[r] = hidden.T.astype(hidt_ref.dtype)
        back_hidden = conv_row(c_ref, r, k2b_ref)
        back_mixed = back_hidden * (sig * (1.0 + mixed * (1.0 - sig)))
        bf_ref[r] = jnp.where(valid, back_mixed * scale, 0.0).astype(bf_ref.dtype)
        own = jnp.logical_and(r >= 1, r <= count)
        lv0 = lv0 + jnp.where(own, jnp.sum(back_mixed * first, axis=0, keepdims=True), 0.0)
        lv1 = lv1 + jnp.where(own, jnp.sum(back_mixed, axis=0, keepdims=True), 0.0)
        return lv0, lv1

    def out_row(i, x_ref, c_ref, hid_ref, bf_ref, k2f_ref, k1b_ref, out_ref, ig_ref):
        out_ref[i] = (x_ref[i + 2].astype(jnp.float32) + conv_row(hid_ref, i, k2f_ref)).astype(out_ref.dtype)
        ig_ref[i] = (c_ref[i + 2].astype(jnp.float32) + conv_row(bf_ref, i, k1b_ref)).astype(ig_ref.dtype)

    def g1_row(i, xt_ref, bf_ref, acc1):
        xs = jnp.concatenate([xt_ref[i + 1], xt_ref[i + 2], xt_ref[i + 3]], axis=0)
        acc1[...] += jnp.dot(xs, shifted(bf_ref[i + 1]), preferred_element_type=jnp.float32)

    def g2_row(i, hidt_ref, c_ref, acc2):
        hs = jnp.concatenate([hidt_ref[i], hidt_ref[i + 1], hidt_ref[i + 2]], axis=0)
        acc2[...] += jnp.dot(hs, shifted(c_ref[i + 2]), preferred_element_type=jnp.float32)

    return phase_one, out_row, g1_row, g2_row


def level_and_edges(idx_ref, lt_ref):
    me = lax.axis_index("rows")
    size = lax.axis_size("rows")
    level = lt_ref[idx_ref[0]]
    return level[0:1, :] + 1.0, level[1:2, :], me > 0, me < size - 1


def interior_kernel(idx_ref, lt_ref, x_hbm, c_hbm, k1_ref, k2_ref,
                    hid_ref, bf_ref, hidt_ref, acc1, acc2, lv_ref, k1f, k2f, k2b, k1b,
                    x_ref, c_ref, xt_ref, sems):
    count = hid_ref.shape[0] - 2
    width, ch = hid_ref.shape[1], hid_ref.shape[2]
    copies = [
        pltpu.make_async_copy(x_hbm, x_ref.at[2 : count + 2], sems.at[0]),
        pltpu.make_async_copy(c_hbm, c_ref.at[2 : count + 2], sems.at[1]),
    ]
    for cp in copies:
        cp.start()
    for a in range(3):
        for b in range(3):
            rows = slice(a * ch, (a + 1) * ch)
            cols = slice(b * ch, (b + 1) * ch)
            flip = 3 * (2 - a) + (2 - b)
            k1f[rows, cols] = k1_ref[3 * a + b]
            k2f[rows, cols] = k2_ref[3 * a + b]
            k2b[rows, cols] = k2_ref[flip].astype(jnp.float32).T.astype(k2b.dtype)
            k1b[rows, cols] = k1_ref[flip].astype(jnp.float32).T.astype(k1b.dtype)
    scale, shift, top, bottom = level_and_edges(idx_ref, lt_ref)
    phase_one, out_row, g1_row, g2_row = row_ops(width, ch, scale, shift, top, bottom, count)
    for cp in copies:
        cp.wait()

    zero = jnp.zeros((1, ch), jnp.float32)
    lv0, lv1 = lax.fori_loop(
        2, count, lambda r, cr: phase_one(r, x_ref, c_ref, hid_ref, hidt_ref, bf_ref, k1f, k2b, cr), (zero, zero)
    )
    lv_ref[0:1, :] = lv0
    lv_ref[1:2, :] = lv1

    def transpose_rows(r, carry):
        xt_ref[r] = x_ref[r].astype(jnp.float32).T.astype(xt_ref.dtype)
        return carry

    lax.fori_loop(2, count + 2, transpose_rows, 0)
    acc1[...] = jnp.zeros_like(acc1)
    acc2[...] = jnp.zeros_like(acc2)

    def middle(i, carry):
        g2_row(i, hidt_ref, c_ref, acc2)
        return carry

    lax.fori_loop(2, count - 2, middle, 0)

    def g1_middle(i, carry):
        g1_row(i, xt_ref, bf_ref, acc1)
        return carry

    lax.fori_loop(1, count - 1, g1_middle, 0)


def edge_kernel(norm, idx_ref, lt_ref, x_hbm, c_hbm, before_hbm, after_hbm, hida_hbm, bfa_hbm, hidta_hbm,
                acc1a_ref, acc2a_ref, lva_ref, k1f, k2b,
                grad_ref, hid_ref, bf_ref,
                x_ref, c_ref, hidt_ref, xt_ref, acc1, acc2, sems):
    count = hid_ref.shape[0] - 2
    width, ch = hid_ref.shape[1], hid_ref.shape[2]
    copies = [
        pltpu.make_async_copy(before_hbm.at[0:2], x_ref.at[0:2], sems.at[0]),
        pltpu.make_async_copy(x_hbm, x_ref.at[2 : count + 2], sems.at[1]),
        pltpu.make_async_copy(after_hbm.at[0:2], x_ref.at[count + 2 : count + 4], sems.at[2]),
        pltpu.make_async_copy(before_hbm.at[2:4], c_ref.at[0:2], sems.at[3]),
        pltpu.make_async_copy(c_hbm, c_ref.at[2 : count + 2], sems.at[4]),
        pltpu.make_async_copy(after_hbm.at[2:4], c_ref.at[count + 2 : count + 4], sems.at[5]),
        pltpu.make_async_copy(hida_hbm, hid_ref, sems.at[6]),
        pltpu.make_async_copy(bfa_hbm, bf_ref, sems.at[7]),
        pltpu.make_async_copy(hidta_hbm, hidt_ref, sems.at[8]),
    ]
    for cp in copies:
        cp.start()
    scale, shift, top, bottom = level_and_edges(idx_ref, lt_ref)
    phase_one, out_row, g1_row, g2_row = row_ops(width, ch, scale, shift, top, bottom, count)
    acc1[...] = acc1a_ref[...]
    acc2[...] = acc2a_ref[...]
    for cp in copies:
        cp.wait()

    carry = (lva_ref[0:1, :], lva_ref[1:2, :])
    for r in (0, 1, count, count + 1):
        carry = phase_one(r, x_ref, c_ref, hid_ref, hidt_ref, bf_ref, k1f, k2b, carry)
    lv0, lv1 = carry
    for r in (1, 2, 3, count, count + 1, count + 2):
        xt_ref[r] = x_ref[r].astype(jnp.float32).T.astype(xt_ref.dtype)
    for i in (0, 1, count - 2, count - 1):
        g2_row(i, hidt_ref, c_ref, acc2)
    for i in (0, count - 1):
        g1_row(i, xt_ref, bf_ref, acc1)

    for a in range(3):
        for b in range(3):
            t = 3 * a + b
            blk = (slice(a * ch, (a + 1) * ch), slice(b * ch, (b + 1) * ch))
            grad_ref[t * ch : (t + 1) * ch, :] = acc1[blk] * norm
            grad_ref[(9 + t) * ch : (10 + t) * ch, :] = acc2[blk] * norm
    base = 18 * ch
    tail = grad_ref.shape[0] - base
    grad_ref[base:, :] = jnp.zeros((tail, ch), jnp.float32)
    grad_ref[base : base + 1, :] = lv0 * norm
    grad_ref[base + 1 : base + 2, :] = lv1 * norm


def out_kernel(first_row, x_hbm, c_hbm, hid_hbm, bf_hbm, k2f, k1b, out_ref, ig_ref,
               x_ref, c_ref, hid_ref, bf_ref, sems):
    n, width, ch = out_ref.shape
    copies = [
        pltpu.make_async_copy(x_hbm.at[first_row : first_row + n], x_ref.at[2 : n + 2], sems.at[0]),
        pltpu.make_async_copy(c_hbm.at[first_row : first_row + n], c_ref.at[2 : n + 2], sems.at[1]),
        pltpu.make_async_copy(hid_hbm.at[first_row : first_row + n + 2], hid_ref, sems.at[2]),
        pltpu.make_async_copy(bf_hbm.at[first_row : first_row + n + 2], bf_ref, sems.at[3]),
    ]
    for cp in copies:
        cp.start()
    one = jnp.ones((1, ch), jnp.float32)
    out_row = row_ops(width, ch, one, one, True, True, n)[1]
    for cp in copies:
        cp.wait()
    for i in range(n):
        out_row(i, x_ref, c_ref, hid_ref, bf_ref, k2f, k1b, out_ref, ig_ref)


def section(norm, packed_rows, level_index, level_table, inputs, cotangent, before_fn, k1, k2):
    count, width, ch = inputs.shape
    vmem = pltpu.MemorySpace.VMEM if hasattr(pltpu, "MemorySpace") else pltpu.VMEM
    spec = pl.BlockSpec(memory_space=vmem)
    anywhere = pl.BlockSpec(memory_space=pl.ANY)
    smem = pl.BlockSpec(memory_space=pltpu.SMEM)
    big = 3 * ch
    unit = width * big * big * 2
    field = jax.ShapeDtypeStruct((count, width, ch), jnp.bfloat16)
    frame = jax.ShapeDtypeStruct((count + 2, width, ch), jnp.bfloat16)
    frame_t = jax.ShapeDtypeStruct((count + 2, ch, width), jnp.bfloat16)
    square = jax.ShapeDtypeStruct((big, big), jnp.float32)
    params = pltpu.CompilerParams(vmem_limit_bytes=60 * 1024 * 1024)
    matrix = jax.ShapeDtypeStruct((big, big), jnp.bfloat16)
    hid, bf, hidt, acc1, acc2, lv, k1f, k2f, k2b, k1b = pl.pallas_call(
        interior_kernel,
        out_shape=(frame, frame, frame_t, square, square,
                   jax.ShapeDtypeStruct((2, ch), jnp.float32), matrix, matrix, matrix, matrix),
        in_specs=[smem, spec, anywhere, anywhere, spec, spec],
        out_specs=(spec,) * 10,
        scratch_shapes=[
            pltpu.VMEM((count + 4, width, ch), jnp.bfloat16),
            pltpu.VMEM((count + 4, width, ch), jnp.bfloat16),
            pltpu.VMEM((count + 4, ch, width), jnp.bfloat16),
            pltpu.SemaphoreType.DMA((2,)),
        ],
        compiler_params=params,
        cost_estimate=pl.CostEstimate(
            flops=(4 * count - 6) * unit, transcendentals=count * width * ch, bytes_accessed=8 * count * width * ch
        ),
    )(level_index, level_table, inputs, cotangent, k1, k2)
    before, after = before_fn()
    packed, hid, bf = pl.pallas_call(
        functools.partial(edge_kernel, norm),
        out_shape=(jax.ShapeDtypeStruct((packed_rows, ch), jnp.float32), frame, frame),
        in_specs=[smem, spec] + [anywhere] * 7 + [spec] * 5,
        out_specs=(spec, spec, spec),
        scratch_shapes=[
            pltpu.VMEM((count + 4, width, ch), jnp.bfloat16),
            pltpu.VMEM((count + 4, width, ch), jnp.bfloat16),
            pltpu.VMEM((count + 2, ch, width), jnp.bfloat16),
            pltpu.VMEM((count + 4, ch, width), jnp.bfloat16),
            pltpu.VMEM((big, big), jnp.float32),
            pltpu.VMEM((big, big), jnp.float32),
            pltpu.SemaphoreType.DMA((9,)),
        ],
        compiler_params=params,
        cost_estimate=pl.CostEstimate(
            flops=14 * unit, transcendentals=4 * width * ch, bytes_accessed=10 * count * width * ch
        ),
    )(level_index, level_table, inputs, cotangent, before, after, hid, bf, hidt, acc1, acc2, lv, k1f, k2b)
    step = 2 if count % 2 == 0 else 1
    chunk = jax.ShapeDtypeStruct((step, width, ch), jnp.bfloat16)
    outs, igs = [], []
    for first_row in range(0, count, step):
        o, g = pl.pallas_call(
            functools.partial(out_kernel, first_row),
            out_shape=(chunk, chunk),
            in_specs=[anywhere] * 4 + [spec] * 2,
            out_specs=(spec, spec),
            scratch_shapes=[
                pltpu.VMEM((step + 2, width, ch), jnp.bfloat16),
                pltpu.VMEM((step + 2, width, ch), jnp.bfloat16),
                pltpu.VMEM((step + 2, width, ch), jnp.bfloat16),
                pltpu.VMEM((step + 2, width, ch), jnp.bfloat16),
                pltpu.SemaphoreType.DMA((4,)),
            ],
            compiler_params=params,
            cost_estimate=pl.CostEstimate(
                flops=2 * step * unit, transcendentals=0, bytes_accessed=8 * step * width * ch
            ),
        )(inputs, cotangent, hid, bf, k2f, k1b)
        outs.append((o, g))
    return outs, packed


def butterfly_sum(block, riders=()):
    n = lax.axis_size("rows")
    me = lax.axis_index("rows")
    bits = []
    k = 1
    while k < n:
        bits.append(k)
        k *= 2
    other = list(bits)
    if len(bits) > 2:
        other[1], other[2] = bits[2], bits[1]
    orders = list(zip(bits, other))
    even = me % 2 == 0

    def step_of(k0, k1):
        perm = [(i, i ^ (k0 if i % 2 == 0 else k1)) for i in range(n)]
        low = jnp.where(even, (me // k0) % 2, (me // k1) % 2) == 0
        return perm, low

    riders = list(riders)
    tied = []
    piece = block
    for k0, k1 in orders:
        perm, low = step_of(k0, k1)
        half = piece.shape[0] // 2
        lo, hi = piece[:half], piece[half:]
        keep = jnp.where(low, lo, hi)
        send = jnp.where(low, hi, lo)
        got = lax.ppermute(send, "rows", perm)
        if riders:
            got, rider = lax.optimization_barrier((got, riders.pop(0)))
            tied.append(rider)
        piece = keep + got
    for k0, k1 in reversed(orders):
        perm, low = step_of(k0, k1)
        got = lax.ppermute(piece, "rows", perm)
        if riders:
            got, rider = lax.optimization_barrier((got, riders.pop(0)))
            tied.append(rider)
        piece = jnp.where(low, jnp.concatenate([piece, got]), jnp.concatenate([got, piece]))
    return piece, tied + riders


def local(inputs, cotangent, first_kernel, second_kernel, level_table, level_index):
    count = inputs.shape[0]
    width = inputs.shape[1]
    ch = inputs.shape[2]
    size = lax.axis_size("rows")
    total_rows = count * size
    norm = 1.0 / math.sqrt(total_rows * width)

    up = [(i, i + 1) for i in range(size - 1)]
    down = [(i + 1, i) for i in range(size - 1)]
    before = lax.ppermute(jnp.concatenate([inputs[-2:], cotangent[-2:]]), "rows", up)
    after = lax.ppermute(jnp.concatenate([inputs[:2], cotangent[:2]]), "rows", down)
    halo = lambda: (before, after)

    used = 18 * ch + 2
    packed_rows = used + (-used % size)
    chunks, packed = section(
        norm, packed_rows, level_index, level_table, inputs, cotangent, halo,
        first_kernel, second_kernel,
    )
    total, chunks = butterfly_sum(packed, chunks)
    outputs = jnp.concatenate([o for o, _ in chunks])
    input_grad = jnp.concatenate([g for _, g in chunks])
    first_sum = total[: 9 * ch].reshape(9, ch, ch)
    second_sum = total[9 * ch : 18 * ch].reshape(9, ch, ch)
    level_sum = total[18 * ch : 18 * ch + 2]
    return (outputs, input_grad, first_sum, second_sum, level_sum)


def solution(mesh):
    return jax.shard_map(
        local,
        mesh=mesh,
        in_specs=(
            P(("groups", "rows"), None, None),
            P(("groups", "rows"), None, None),
            P(),
            P(),
            P(),
            P("groups"),
        ),
        out_specs=(
            P(("groups", "rows"), None, None),
            P(("groups", "rows"), None, None),
            P("groups", None, None),
            P("groups", None, None),
            P("groups", None),
        ),
        check_vma=False,
    )
```

```python
import functools
import math

import jax
import jax.numpy as jnp
from jax import lax
from jax.experimental import pallas as pl
from jax.experimental.pallas import tpu as pltpu
from jax.sharding import PartitionSpec as P


def row_ops(width, ch, scale, shift, top, bottom, count):
    col = lax.broadcasted_iota(jnp.int32, (width, ch), 0)
    not_first = col > 0
    not_last = col < width - 1

    def combine(y):
        left = pltpu.roll(y[:, 0:ch], 1, 0)
        right = pltpu.roll(y[:, 2 * ch:3 * ch], width - 1, 0)
        return y[:, ch:2 * ch] + jnp.where(not_first, left, 0.0) + jnp.where(not_last, right, 0.0)

    def conv_row(ref, r, matrix_ref):
        rows = jnp.concatenate([ref[r], ref[r + 1], ref[r + 2]], axis=1)
        y = jnp.dot(rows, matrix_ref[...], preferred_element_type=jnp.float32)
        return combine(y)

    def shifted(g):
        g32 = g.astype(jnp.float32)
        g0 = jnp.where(not_last, pltpu.roll(g32, width - 1, 0), 0.0)
        g2 = jnp.where(not_first, pltpu.roll(g32, 1, 0), 0.0)
        return jnp.concatenate([g0.astype(g.dtype), g, g2.astype(g.dtype)], axis=1)

    def phase_one(r, x_ref, c_ref, hid_ref, hidt_ref, bf_ref, k1f_ref, k2b_ref, carry):
        lv0, lv1 = carry
        valid = jnp.logical_and(jnp.logical_or(r > 0, top), jnp.logical_or(r < count + 1, bottom))
        first = conv_row(x_ref, r, k1f_ref)
        mixed = first * scale + shift
        sig = 0.5 + 0.5 * jnp.tanh(0.5 * mixed)
        hidden = jnp.where(valid, mixed * sig, 0.0)
        hid_ref[r] = hidden.astype(hid_ref.dtype)
        hidt_ref[r] = hidden.T.astype(hidt_ref.dtype)
        back_hidden = conv_row(c_ref, r, k2b_ref)
        back_mixed = back_hidden * (sig * (1.0 + mixed * (1.0 - sig)))
        bf_ref[r] = jnp.where(valid, back_mixed * scale, 0.0).astype(bf_ref.dtype)
        own = jnp.logical_and(r >= 1, r <= count)
        lv0 = lv0 + jnp.where(own, jnp.sum(back_mixed * first, axis=0, keepdims=True), 0.0)
        lv1 = lv1 + jnp.where(own, jnp.sum(back_mixed, axis=0, keepdims=True), 0.0)
        return lv0, lv1

    def out_row(i, x_ref, c_ref, hid_ref, bf_ref, k2f_ref, k1b_ref, out_ref, ig_ref):
        out_ref[i] = (x_ref[i + 2].astype(jnp.float32) + conv_row(hid_ref, i, k2f_ref)).astype(out_ref.dtype)
        ig_ref[i] = (c_ref[i + 2].astype(jnp.float32) + conv_row(bf_ref, i, k1b_ref)).astype(ig_ref.dtype)

    def g1_row(i, xt_ref, bf_ref, acc1):
        xs = jnp.concatenate([xt_ref[i + 1], xt_ref[i + 2], xt_ref[i + 3]], axis=0)
        acc1[...] += jnp.dot(xs, shifted(bf_ref[i + 1]), preferred_element_type=jnp.float32)

    def g2_row(i, hidt_ref, c_ref, acc2):
        hs = jnp.concatenate([hidt_ref[i], hidt_ref[i + 1], hidt_ref[i + 2]], axis=0)
        acc2[...] += jnp.dot(hs, shifted(c_ref[i + 2]), preferred_element_type=jnp.float32)

    return phase_one, out_row, g1_row, g2_row


def level_and_edges(idx_ref, lt_ref):
    me = lax.axis_index("rows")
    size = lax.axis_size("rows")
    level = lt_ref[idx_ref[0]]
    return level[0:1, :] + 1.0, level[1:2, :], me > 0, me < size - 1


def interior_kernel(idx_ref, lt_ref, x_hbm, c_hbm, k1_ref, k2_ref,
                    hid_ref, bf_ref, hidt_ref, acc1, acc2, lv_ref, k1f, k2f, k2b, k1b,
                    x_ref, c_ref, xt_ref, sems):
    count = hid_ref.shape[0] - 2
    width, ch = hid_ref.shape[1], hid_ref.shape[2]
    copies = [
        pltpu.make_async_copy(x_hbm, x_ref.at[2 : count + 2], sems.at[0]),
        pltpu.make_async_copy(c_hbm, c_ref.at[2 : count + 2], sems.at[1]),
    ]
    for cp in copies:
        cp.start()
    for a in range(3):
        for b in range(3):
            rows = slice(a * ch, (a + 1) * ch)
            cols = slice(b * ch, (b + 1) * ch)
            flip = 3 * (2 - a) + (2 - b)
            k1f[rows, cols] = k1_ref[3 * a + b]
            k2f[rows, cols] = k2_ref[3 * a + b]
            k2b[rows, cols] = k2_ref[flip].astype(jnp.float32).T.astype(k2b.dtype)
            k1b[rows, cols] = k1_ref[flip].astype(jnp.float32).T.astype(k1b.dtype)
    scale, shift, top, bottom = level_and_edges(idx_ref, lt_ref)
    phase_one, out_row, g1_row, g2_row = row_ops(width, ch, scale, shift, top, bottom, count)
    for cp in copies:
        cp.wait()

    zero = jnp.zeros((1, ch), jnp.float32)
    lv0, lv1 = lax.fori_loop(
        2, count, lambda r, cr: phase_one(r, x_ref, c_ref, hid_ref, hidt_ref, bf_ref, k1f, k2b, cr), (zero, zero)
    )
    lv_ref[0:1, :] = lv0
    lv_ref[1:2, :] = lv1

    def transpose_rows(r, carry):
        xt_ref[r] = x_ref[r].astype(jnp.float32).T.astype(xt_ref.dtype)
        return carry

    lax.fori_loop(2, count + 2, transpose_rows, 0)
    acc1[...] = jnp.zeros_like(acc1)
    acc2[...] = jnp.zeros_like(acc2)

    def middle(i, carry):
        g2_row(i, hidt_ref, c_ref, acc2)
        return carry

    lax.fori_loop(2, count - 2, middle, 0)

    def g1_middle(i, carry):
        g1_row(i, xt_ref, bf_ref, acc1)
        return carry

    lax.fori_loop(1, count - 1, g1_middle, 0)


def edge_kernel(norm, idx_ref, lt_ref, x_hbm, c_hbm, before_hbm, after_hbm, hida_hbm, bfa_hbm, hidta_hbm,
                acc1a_ref, acc2a_ref, lva_ref, k1f, k2b,
                grad_ref, hid_ref, bf_ref,
                x_ref, c_ref, hidt_ref, xt_ref, acc1, acc2, sems):
    count = hid_ref.shape[0] - 2
    width, ch = hid_ref.shape[1], hid_ref.shape[2]
    copies = [
        pltpu.make_async_copy(before_hbm.at[0:2], x_ref.at[0:2], sems.at[0]),
        pltpu.make_async_copy(x_hbm, x_ref.at[2 : count + 2], sems.at[1]),
        pltpu.make_async_copy(after_hbm.at[0:2], x_ref.at[count + 2 : count + 4], sems.at[2]),
        pltpu.make_async_copy(before_hbm.at[2:4], c_ref.at[0:2], sems.at[3]),
        pltpu.make_async_copy(c_hbm, c_ref.at[2 : count + 2], sems.at[4]),
        pltpu.make_async_copy(after_hbm.at[2:4], c_ref.at[count + 2 : count + 4], sems.at[5]),
        pltpu.make_async_copy(hida_hbm, hid_ref, sems.at[6]),
        pltpu.make_async_copy(bfa_hbm, bf_ref, sems.at[7]),
        pltpu.make_async_copy(hidta_hbm, hidt_ref, sems.at[8]),
    ]
    for cp in copies:
        cp.start()
    scale, shift, top, bottom = level_and_edges(idx_ref, lt_ref)
    phase_one, out_row, g1_row, g2_row = row_ops(width, ch, scale, shift, top, bottom, count)
    acc1[...] = acc1a_ref[...]
    acc2[...] = acc2a_ref[...]
    for cp in copies:
        cp.wait()

    carry = (lva_ref[0:1, :], lva_ref[1:2, :])
    for r in (0, 1, count, count + 1):
        carry = phase_one(r, x_ref, c_ref, hid_ref, hidt_ref, bf_ref, k1f, k2b, carry)
    lv0, lv1 = carry
    for r in (1, 2, 3, count, count + 1, count + 2):
        xt_ref[r] = x_ref[r].astype(jnp.float32).T.astype(xt_ref.dtype)
    for i in (0, 1, count - 2, count - 1):
        g2_row(i, hidt_ref, c_ref, acc2)
    for i in (0, count - 1):
        g1_row(i, xt_ref, bf_ref, acc1)

    for a in range(3):
        for b in range(3):
            t = 3 * a + b
            blk = (slice(a * ch, (a + 1) * ch), slice(b * ch, (b + 1) * ch))
            grad_ref[t * ch : (t + 1) * ch, :] = acc1[blk] * norm
            grad_ref[(9 + t) * ch : (10 + t) * ch, :] = acc2[blk] * norm
    base = 18 * ch
    tail = grad_ref.shape[0] - base
    grad_ref[base:, :] = jnp.zeros((tail, ch), jnp.float32)
    grad_ref[base : base + 1, :] = lv0 * norm
    grad_ref[base + 1 : base + 2, :] = lv1 * norm


def out_kernel(first_row, x_hbm, c_hbm, hid_hbm, bf_hbm, k2f, k1b, outa_hbm, iga_hbm, out_hbm, ig_hbm,
               x_ref, c_ref, hid_ref, bf_ref, o_ref, g_ref, sems):
    del outa_hbm, iga_hbm
    n, width, ch = o_ref.shape
    copies = [
        pltpu.make_async_copy(x_hbm.at[first_row : first_row + n], x_ref.at[2 : n + 2], sems.at[0]),
        pltpu.make_async_copy(c_hbm.at[first_row : first_row + n], c_ref.at[2 : n + 2], sems.at[1]),
        pltpu.make_async_copy(hid_hbm.at[first_row : first_row + n + 2], hid_ref, sems.at[2]),
        pltpu.make_async_copy(bf_hbm.at[first_row : first_row + n + 2], bf_ref, sems.at[3]),
    ]
    for cp in copies:
        cp.start()
    one = jnp.ones((1, ch), jnp.float32)
    out_row = row_ops(width, ch, one, one, True, True, n)[1]
    for cp in copies:
        cp.wait()
    for i in range(n):
        out_row(i, x_ref, c_ref, hid_ref, bf_ref, k2f, k1b, o_ref, g_ref)
    stores = [
        pltpu.make_async_copy(o_ref, out_hbm.at[first_row : first_row + n], sems.at[4]),
        pltpu.make_async_copy(g_ref, ig_hbm.at[first_row : first_row + n], sems.at[5]),
    ]
    for cp in stores:
        cp.start()
    for cp in stores:
        cp.wait()


def section(norm, packed_rows, level_index, level_table, inputs, cotangent, before_fn, k1, k2):
    count, width, ch = inputs.shape
    vmem = pltpu.MemorySpace.VMEM if hasattr(pltpu, "MemorySpace") else pltpu.VMEM
    spec = pl.BlockSpec(memory_space=vmem)
    anywhere = pl.BlockSpec(memory_space=pl.ANY)
    smem = pl.BlockSpec(memory_space=pltpu.SMEM)
    big = 3 * ch
    unit = width * big * big * 2
    field = jax.ShapeDtypeStruct((count, width, ch), jnp.bfloat16)
    frame = jax.ShapeDtypeStruct((count + 2, width, ch), jnp.bfloat16)
    frame_t = jax.ShapeDtypeStruct((count + 2, ch, width), jnp.bfloat16)
    square = jax.ShapeDtypeStruct((big, big), jnp.float32)
    params = pltpu.CompilerParams(vmem_limit_bytes=60 * 1024 * 1024)
    matrix = jax.ShapeDtypeStruct((big, big), jnp.bfloat16)
    hid, bf, hidt, acc1, acc2, lv, k1f, k2f, k2b, k1b = pl.pallas_call(
        interior_kernel,
        out_shape=(frame, frame, frame_t, square, square,
                   jax.ShapeDtypeStruct((2, ch), jnp.float32), matrix, matrix, matrix, matrix),
        in_specs=[smem, spec, anywhere, anywhere, spec, spec],
        out_specs=(spec,) * 10,
        scratch_shapes=[
            pltpu.VMEM((count + 4, width, ch), jnp.bfloat16),
            pltpu.VMEM((count + 4, width, ch), jnp.bfloat16),
            pltpu.VMEM((count + 4, ch, width), jnp.bfloat16),
            pltpu.SemaphoreType.DMA((2,)),
        ],
        compiler_params=params,
        cost_estimate=pl.CostEstimate(
            flops=(4 * count - 6) * unit, transcendentals=count * width * ch, bytes_accessed=8 * count * width * ch
        ),
    )(level_index, level_table, inputs, cotangent, k1, k2)
    before, after = before_fn()
    packed, hid, bf = pl.pallas_call(
        functools.partial(edge_kernel, norm),
        out_shape=(jax.ShapeDtypeStruct((packed_rows, ch), jnp.float32), frame, frame),
        in_specs=[smem, spec] + [anywhere] * 7 + [spec] * 5,
        out_specs=(spec, spec, spec),
        scratch_shapes=[
            pltpu.VMEM((count + 4, width, ch), jnp.bfloat16),
            pltpu.VMEM((count + 4, width, ch), jnp.bfloat16),
            pltpu.VMEM((count + 2, ch, width), jnp.bfloat16),
            pltpu.VMEM((count + 4, ch, width), jnp.bfloat16),
            pltpu.VMEM((big, big), jnp.float32),
            pltpu.VMEM((big, big), jnp.float32),
            pltpu.SemaphoreType.DMA((9,)),
        ],
        compiler_params=params,
        cost_estimate=pl.CostEstimate(
            flops=14 * unit, transcendentals=4 * width * ch, bytes_accessed=10 * count * width * ch
        ),
    )(level_index, level_table, inputs, cotangent, before, after, hid, bf, hidt, acc1, acc2, lv, k1f, k2b)
    step = 1
    whole = jax.ShapeDtypeStruct((count, width, ch), jnp.bfloat16)
    out = jnp.zeros((count, width, ch), jnp.bfloat16)
    ig = jnp.zeros((count, width, ch), jnp.bfloat16)
    chunks = []
    for first_row in range(0, count, step):
        chunks.append(functools.partial(
            pl.pallas_call(
                functools.partial(out_kernel, first_row),
                out_shape=(whole, whole),
                in_specs=[anywhere] * 4 + [spec] * 2 + [anywhere] * 2,
                out_specs=(anywhere, anywhere),
                scratch_shapes=[
                    pltpu.VMEM((step + 2, width, ch), jnp.bfloat16),
                    pltpu.VMEM((step + 2, width, ch), jnp.bfloat16),
                    pltpu.VMEM((step + 2, width, ch), jnp.bfloat16),
                    pltpu.VMEM((step + 2, width, ch), jnp.bfloat16),
                    pltpu.VMEM((step, width, ch), jnp.bfloat16),
                    pltpu.VMEM((step, width, ch), jnp.bfloat16),
                    pltpu.SemaphoreType.DMA((6,)),
                ],
                input_output_aliases={6: 0, 7: 1},
                compiler_params=params,
                cost_estimate=pl.CostEstimate(
                    flops=2 * step * unit, transcendentals=0, bytes_accessed=8 * step * width * ch
                ),
            ),
            inputs, cotangent, hid, bf, k2f, k1b,
        ))
    return (out, ig), chunks, packed


def butterfly_sum(block, state, riders=()):
    n = lax.axis_size("rows")
    me = lax.axis_index("rows")
    bits = []
    k = 1
    while k < n:
        bits.append(k)
        k *= 2
    other = list(bits)
    if len(bits) > 2:
        other[1], other[2] = bits[2], bits[1]
    orders = list(zip(bits, other))
    even = me % 2 == 0

    def step_of(k0, k1):
        perm = [(i, i ^ (k0 if i % 2 == 0 else k1)) for i in range(n)]
        low = jnp.where(even, (me // k0) % 2, (me // k1) % 2) == 0
        return perm, low

    riders = list(riders)
    piece = block
    for k0, k1 in orders:
        perm, low = step_of(k0, k1)
        half = piece.shape[0] // 2
        lo, hi = piece[:half], piece[half:]
        keep = jnp.where(low, lo, hi)
        send = jnp.where(low, hi, lo)
        got = lax.ppermute(send, "rows", perm)
        if riders:
            got, state = lax.optimization_barrier((got, riders.pop(0)(*state)))
        piece = keep + got
    for k0, k1 in reversed(orders):
        perm, low = step_of(k0, k1)
        got = lax.ppermute(piece, "rows", perm)
        if riders:
            got, state = lax.optimization_barrier((got, riders.pop(0)(*state)))
        piece = jnp.where(low, jnp.concatenate([piece, got]), jnp.concatenate([got, piece]))
    for rider in riders:
        state = rider(*state)
    return piece, state


def local(inputs, cotangent, first_kernel, second_kernel, level_table, level_index):
    count = inputs.shape[0]
    width = inputs.shape[1]
    ch = inputs.shape[2]
    size = lax.axis_size("rows")
    total_rows = count * size
    norm = 1.0 / math.sqrt(total_rows * width)

    up = [(i, i + 1) for i in range(size - 1)]
    down = [(i + 1, i) for i in range(size - 1)]
    before = lax.ppermute(jnp.concatenate([inputs[-2:], cotangent[-2:]]), "rows", up)
    after = lax.ppermute(jnp.concatenate([inputs[:2], cotangent[:2]]), "rows", down)
    halo = lambda: (before, after)

    used = 18 * ch + 2
    packed_rows = used + (-used % size)
    state, chunks, packed = section(
        norm, packed_rows, level_index, level_table, inputs, cotangent, halo,
        first_kernel, second_kernel,
    )
    total, (outputs, input_grad) = butterfly_sum(packed, state, chunks)
    first_sum = total[: 9 * ch].reshape(9, ch, ch)
    second_sum = total[9 * ch : 18 * ch].reshape(9, ch, ch)
    level_sum = total[18 * ch : 18 * ch + 2]
    return (outputs, input_grad, first_sum, second_sum, level_sum)


def solution(mesh):
    return jax.shard_map(
        local,
        mesh=mesh,
        in_specs=(
            P(("groups", "rows"), None, None),
            P(("groups", "rows"), None, None),
            P(),
            P(),
            P(),
            P("groups"),
        ),
        out_specs=(
            P(("groups", "rows"), None, None),
            P(("groups", "rows"), None, None),
            P("groups", None, None),
            P("groups", None, None),
            P("groups", None),
        ),
        check_vma=False,
    )
```

```python
import functools
import math

import jax
import jax.numpy as jnp
from jax import lax
from jax.experimental import pallas as pl
from jax.experimental.pallas import tpu as pltpu
from jax.sharding import PartitionSpec as P


def row_ops(width, ch, scale, shift, top, bottom, count):
    col = lax.broadcasted_iota(jnp.int32, (width, ch), 0)
    not_first = col > 0
    not_last = col < width - 1

    def combine(y):
        left = pltpu.roll(y[:, 0:ch], 1, 0)
        right = pltpu.roll(y[:, 2 * ch:3 * ch], width - 1, 0)
        return y[:, ch:2 * ch] + jnp.where(not_first, left, 0.0) + jnp.where(not_last, right, 0.0)

    def conv_row(ref, r, matrix_ref):
        rows = jnp.concatenate([ref[r], ref[r + 1], ref[r + 2]], axis=1)
        y = jnp.dot(rows, matrix_ref[...], preferred_element_type=jnp.float32)
        return combine(y)

    def shifted(g):
        g32 = g.astype(jnp.float32)
        g0 = jnp.where(not_last, pltpu.roll(g32, width - 1, 0), 0.0)
        g2 = jnp.where(not_first, pltpu.roll(g32, 1, 0), 0.0)
        return jnp.concatenate([g0.astype(g.dtype), g, g2.astype(g.dtype)], axis=1)

    def phase_one(r, x_ref, c_ref, hid_ref, hidt_ref, bf_ref, k1f_ref, k2b_ref, carry):
        lv0, lv1 = carry
        valid = jnp.logical_and(jnp.logical_or(r > 0, top), jnp.logical_or(r < count + 1, bottom))
        first = conv_row(x_ref, r, k1f_ref)
        mixed = first * scale + shift
        sig = 0.5 + 0.5 * jnp.tanh(0.5 * mixed)
        hidden = jnp.where(valid, mixed * sig, 0.0)
        hid_ref[r] = hidden.astype(hid_ref.dtype)
        hidt_ref[r] = hidden.T.astype(hidt_ref.dtype)
        back_hidden = conv_row(c_ref, r, k2b_ref)
        back_mixed = back_hidden * (sig * (1.0 + mixed * (1.0 - sig)))
        bf_ref[r] = jnp.where(valid, back_mixed * scale, 0.0).astype(bf_ref.dtype)
        own = jnp.logical_and(r >= 1, r <= count)
        lv0 = lv0 + jnp.where(own, jnp.sum(back_mixed * first, axis=0, keepdims=True), 0.0)
        lv1 = lv1 + jnp.where(own, jnp.sum(back_mixed, axis=0, keepdims=True), 0.0)
        return lv0, lv1

    def out_row(i, x_ref, c_ref, hid_ref, bf_ref, k2f_ref, k1b_ref, out_ref, ig_ref):
        out_ref[i] = (x_ref[i + 2].astype(jnp.float32) + conv_row(hid_ref, i, k2f_ref)).astype(out_ref.dtype)
        ig_ref[i] = (c_ref[i + 2].astype(jnp.float32) + conv_row(bf_ref, i, k1b_ref)).astype(ig_ref.dtype)

    def g1_row(i, xt_ref, bf_ref, acc1):
        xs = jnp.concatenate([xt_ref[i + 1], xt_ref[i + 2], xt_ref[i + 3]], axis=0)
        acc1[...] += jnp.dot(xs, shifted(bf_ref[i + 1]), preferred_element_type=jnp.float32)

    def g2_row(i, hidt_ref, c_ref, acc2):
        hs = jnp.concatenate([hidt_ref[i], hidt_ref[i + 1], hidt_ref[i + 2]], axis=0)
        acc2[...] += jnp.dot(hs, shifted(c_ref[i + 2]), preferred_element_type=jnp.float32)

    return phase_one, out_row, g1_row, g2_row


def level_and_edges(idx_ref, lt_ref):
    me = lax.axis_index("rows")
    size = lax.axis_size("rows")
    level = lt_ref[idx_ref[0]]
    return level[0:1, :] + 1.0, level[1:2, :], me > 0, me < size - 1


def interior_kernel(idx_ref, lt_ref, x_hbm, c_hbm, k1_ref, k2_ref,
                    hid_ref, bf_ref, hidt_ref, acc1, acc2, lv_ref, k1f, k2f, k2b, k1b,
                    x_ref, c_ref, xt_ref, sems):
    count = hid_ref.shape[0] - 2
    width, ch = hid_ref.shape[1], hid_ref.shape[2]
    copies = [
        pltpu.make_async_copy(x_hbm, x_ref.at[2 : count + 2], sems.at[0]),
        pltpu.make_async_copy(c_hbm, c_ref.at[2 : count + 2], sems.at[1]),
    ]
    for cp in copies:
        cp.start()
    for a in range(3):
        for b in range(3):
            rows = slice(a * ch, (a + 1) * ch)
            cols = slice(b * ch, (b + 1) * ch)
            flip = 3 * (2 - a) + (2 - b)
            k1f[rows, cols] = k1_ref[3 * a + b]
            k2f[rows, cols] = k2_ref[3 * a + b]
            k2b[rows, cols] = k2_ref[flip].astype(jnp.float32).T.astype(k2b.dtype)
            k1b[rows, cols] = k1_ref[flip].astype(jnp.float32).T.astype(k1b.dtype)
    scale, shift, top, bottom = level_and_edges(idx_ref, lt_ref)
    phase_one, out_row, g1_row, g2_row = row_ops(width, ch, scale, shift, top, bottom, count)
    for cp in copies:
        cp.wait()

    zero = jnp.zeros((1, ch), jnp.float32)
    lv0, lv1 = lax.fori_loop(
        2, count, lambda r, cr: phase_one(r, x_ref, c_ref, hid_ref, hidt_ref, bf_ref, k1f, k2b, cr), (zero, zero)
    )
    lv_ref[0:1, :] = lv0
    lv_ref[1:2, :] = lv1

    def transpose_rows(r, carry):
        xt_ref[r] = x_ref[r].astype(jnp.float32).T.astype(xt_ref.dtype)
        return carry

    lax.fori_loop(2, count + 2, transpose_rows, 0)
    acc1[...] = jnp.zeros_like(acc1)
    acc2[...] = jnp.zeros_like(acc2)

    def middle(i, carry):
        g2_row(i, hidt_ref, c_ref, acc2)
        return carry

    lax.fori_loop(2, count - 2, middle, 0)

    def g1_middle(i, carry):
        g1_row(i, xt_ref, bf_ref, acc1)
        return carry

    lax.fori_loop(1, count - 1, g1_middle, 0)


def edge_kernel(norm, idx_ref, lt_ref, x_hbm, c_hbm, before_hbm, after_hbm, hida_hbm, bfa_hbm, hidta_hbm,
                acc1a_ref, acc2a_ref, lva_ref, k1f, k2b,
                grad_ref, hid_ref, bf_ref,
                x_ref, c_ref, hidt_ref, xt_ref, acc1, acc2, sems):
    count = hid_ref.shape[0] - 2
    width, ch = hid_ref.shape[1], hid_ref.shape[2]
    copies = [
        pltpu.make_async_copy(before_hbm.at[0:2], x_ref.at[0:2], sems.at[0]),
        pltpu.make_async_copy(x_hbm, x_ref.at[2 : count + 2], sems.at[1]),
        pltpu.make_async_copy(after_hbm.at[0:2], x_ref.at[count + 2 : count + 4], sems.at[2]),
        pltpu.make_async_copy(before_hbm.at[2:4], c_ref.at[0:2], sems.at[3]),
        pltpu.make_async_copy(c_hbm, c_ref.at[2 : count + 2], sems.at[4]),
        pltpu.make_async_copy(after_hbm.at[2:4], c_ref.at[count + 2 : count + 4], sems.at[5]),
        pltpu.make_async_copy(hida_hbm, hid_ref, sems.at[6]),
        pltpu.make_async_copy(bfa_hbm, bf_ref, sems.at[7]),
        pltpu.make_async_copy(hidta_hbm, hidt_ref, sems.at[8]),
    ]
    for cp in copies:
        cp.start()
    scale, shift, top, bottom = level_and_edges(idx_ref, lt_ref)
    phase_one, out_row, g1_row, g2_row = row_ops(width, ch, scale, shift, top, bottom, count)
    acc1[...] = acc1a_ref[...]
    acc2[...] = acc2a_ref[...]
    for cp in copies:
        cp.wait()

    carry = (lva_ref[0:1, :], lva_ref[1:2, :])
    for r in (0, 1, count, count + 1):
        carry = phase_one(r, x_ref, c_ref, hid_ref, hidt_ref, bf_ref, k1f, k2b, carry)
    lv0, lv1 = carry
    for r in (1, 2, 3, count, count + 1, count + 2):
        xt_ref[r] = x_ref[r].astype(jnp.float32).T.astype(xt_ref.dtype)
    for i in (0, 1, count - 2, count - 1):
        g2_row(i, hidt_ref, c_ref, acc2)
    for i in (0, count - 1):
        g1_row(i, xt_ref, bf_ref, acc1)

    for a in range(3):
        for b in range(3):
            t = 3 * a + b
            blk = (slice(a * ch, (a + 1) * ch), slice(b * ch, (b + 1) * ch))
            grad_ref[t * ch : (t + 1) * ch, :] = acc1[blk] * norm
            grad_ref[(9 + t) * ch : (10 + t) * ch, :] = acc2[blk] * norm
    base = 18 * ch
    tail = grad_ref.shape[0] - base
    grad_ref[base:, :] = jnp.zeros((tail, ch), jnp.float32)
    grad_ref[base : base + 1, :] = lv0 * norm
    grad_ref[base + 1 : base + 2, :] = lv1 * norm


def out_kernel(first_row, aliased, x_hbm, c_hbm, hid_hbm, bf_hbm, k2f, k1b, *refs):
    if aliased:
        refs = refs[2:]
    out_hbm, ig_hbm, x_ref, c_ref, hid_ref, bf_ref, o_ref, g_ref, sems = refs
    n, width, ch = o_ref.shape
    copies = [
        pltpu.make_async_copy(x_hbm.at[first_row : first_row + n], x_ref.at[2 : n + 2], sems.at[0]),
        pltpu.make_async_copy(c_hbm.at[first_row : first_row + n], c_ref.at[2 : n + 2], sems.at[1]),
        pltpu.make_async_copy(hid_hbm.at[first_row : first_row + n + 2], hid_ref, sems.at[2]),
        pltpu.make_async_copy(bf_hbm.at[first_row : first_row + n + 2], bf_ref, sems.at[3]),
    ]
    for cp in copies:
        cp.start()
    one = jnp.ones((1, ch), jnp.float32)
    out_row = row_ops(width, ch, one, one, True, True, n)[1]
    for cp in copies:
        cp.wait()
    for i in range(n):
        out_row(i, x_ref, c_ref, hid_ref, bf_ref, k2f, k1b, o_ref, g_ref)
    stores = [
        pltpu.make_async_copy(o_ref, out_hbm.at[first_row : first_row + n], sems.at[4]),
        pltpu.make_async_copy(g_ref, ig_hbm.at[first_row : first_row + n], sems.at[5]),
    ]
    for cp in stores:
        cp.start()
    for cp in stores:
        cp.wait()


def section(norm, packed_rows, level_index, level_table, inputs, cotangent, before_fn, k1, k2):
    count, width, ch = inputs.shape
    vmem = pltpu.MemorySpace.VMEM if hasattr(pltpu, "MemorySpace") else pltpu.VMEM
    spec = pl.BlockSpec(memory_space=vmem)
    anywhere = pl.BlockSpec(memory_space=pl.ANY)
    smem = pl.BlockSpec(memory_space=pltpu.SMEM)
    big = 3 * ch
    unit = width * big * big * 2
    field = jax.ShapeDtypeStruct((count, width, ch), jnp.bfloat16)
    frame = jax.ShapeDtypeStruct((count + 2, width, ch), jnp.bfloat16)
    frame_t = jax.ShapeDtypeStruct((count + 2, ch, width), jnp.bfloat16)
    square = jax.ShapeDtypeStruct((big, big), jnp.float32)
    params = pltpu.CompilerParams(vmem_limit_bytes=60 * 1024 * 1024)
    matrix = jax.ShapeDtypeStruct((big, big), jnp.bfloat16)
    hid, bf, hidt, acc1, acc2, lv, k1f, k2f, k2b, k1b = pl.pallas_call(
        interior_kernel,
        out_shape=(frame, frame, frame_t, square, square,
                   jax.ShapeDtypeStruct((2, ch), jnp.float32), matrix, matrix, matrix, matrix),
        in_specs=[smem, spec, anywhere, anywhere, spec, spec],
        out_specs=(spec,) * 10,
        scratch_shapes=[
            pltpu.VMEM((count + 4, width, ch), jnp.bfloat16),
            pltpu.VMEM((count + 4, width, ch), jnp.bfloat16),
            pltpu.VMEM((count + 4, ch, width), jnp.bfloat16),
            pltpu.SemaphoreType.DMA((2,)),
        ],
        compiler_params=params,
        cost_estimate=pl.CostEstimate(
            flops=(4 * count - 6) * unit, transcendentals=count * width * ch, bytes_accessed=8 * count * width * ch
        ),
    )(level_index, level_table, inputs, cotangent, k1, k2)
    before, after = before_fn()
    packed, hid, bf = pl.pallas_call(
        functools.partial(edge_kernel, norm),
        out_shape=(jax.ShapeDtypeStruct((packed_rows, ch), jnp.float32), frame, frame),
        in_specs=[smem, spec] + [anywhere] * 7 + [spec] * 5,
        out_specs=(spec, spec, spec),
        scratch_shapes=[
            pltpu.VMEM((count + 4, width, ch), jnp.bfloat16),
            pltpu.VMEM((count + 4, width, ch), jnp.bfloat16),
            pltpu.VMEM((count + 2, ch, width), jnp.bfloat16),
            pltpu.VMEM((count + 4, ch, width), jnp.bfloat16),
            pltpu.VMEM((big, big), jnp.float32),
            pltpu.VMEM((big, big), jnp.float32),
            pltpu.SemaphoreType.DMA((9,)),
        ],
        compiler_params=params,
        cost_estimate=pl.CostEstimate(
            flops=14 * unit, transcendentals=4 * width * ch, bytes_accessed=10 * count * width * ch
        ),
    )(level_index, level_table, inputs, cotangent, before, after, hid, bf, hidt, acc1, acc2, lv, k1f, k2b)
    step = count // 2 if count % 2 == 0 else count
    whole = jax.ShapeDtypeStruct((count, width, ch), jnp.bfloat16)
    chunks = []
    for first_row in range(0, count, step):
        aliased = first_row > 0
        chunks.append(functools.partial(
            pl.pallas_call(
                functools.partial(out_kernel, first_row, aliased),
                out_shape=(whole, whole),
                in_specs=[anywhere] * 4 + [spec] * 2 + [anywhere] * (2 if aliased else 0),
                out_specs=(anywhere, anywhere),
                scratch_shapes=[
                    pltpu.VMEM((step + 2, width, ch), jnp.bfloat16),
                    pltpu.VMEM((step + 2, width, ch), jnp.bfloat16),
                    pltpu.VMEM((step + 2, width, ch), jnp.bfloat16),
                    pltpu.VMEM((step + 2, width, ch), jnp.bfloat16),
                    pltpu.VMEM((step, width, ch), jnp.bfloat16),
                    pltpu.VMEM((step, width, ch), jnp.bfloat16),
                    pltpu.SemaphoreType.DMA((6,)),
                ],
                input_output_aliases={6: 0, 7: 1} if aliased else {},
                compiler_params=params,
                cost_estimate=pl.CostEstimate(
                    flops=2 * step * unit, transcendentals=0, bytes_accessed=8 * step * width * ch
                ),
            ),
            inputs, cotangent, hid, bf, k2f, k1b,
        ))
    return chunks, packed


def butterfly_sum(block, riders):
    n = lax.axis_size("rows")
    me = lax.axis_index("rows")
    bits = []
    k = 1
    while k < n:
        bits.append(k)
        k *= 2
    other = list(bits)
    if len(bits) > 2:
        other[1], other[2] = bits[2], bits[1]
    orders = list(zip(bits, other))
    even = me % 2 == 0

    def step_of(k0, k1):
        perm = [(i, i ^ (k0 if i % 2 == 0 else k1)) for i in range(n)]
        low = jnp.where(even, (me // k0) % 2, (me // k1) % 2) == 0
        return perm, low

    state = ()
    count = 0
    piece = block
    for k0, k1 in orders:
        perm, low = step_of(k0, k1)
        half = piece.shape[0] // 2
        lo, hi = piece[:half], piece[half:]
        keep = jnp.where(low, lo, hi)
        send = jnp.where(low, hi, lo)
        got = lax.ppermute(send, "rows", perm)
        if count in riders:
            got, state = lax.optimization_barrier((got, riders[count](*state)))
        count += 1
        piece = keep + got
    for k0, k1 in reversed(orders):
        perm, low = step_of(k0, k1)
        got = lax.ppermute(piece, "rows", perm)
        if count in riders:
            got, state = lax.optimization_barrier((got, riders[count](*state)))
        count += 1
        piece = jnp.where(low, jnp.concatenate([piece, got]), jnp.concatenate([got, piece]))
    return piece, state


def local(inputs, cotangent, first_kernel, second_kernel, level_table, level_index):
    count = inputs.shape[0]
    width = inputs.shape[1]
    ch = inputs.shape[2]
    size = lax.axis_size("rows")
    total_rows = count * size
    norm = 1.0 / math.sqrt(total_rows * width)

    up = [(i, i + 1) for i in range(size - 1)]
    down = [(i + 1, i) for i in range(size - 1)]
    before = lax.ppermute(jnp.concatenate([inputs[-2:], cotangent[-2:]]), "rows", up)
    after = lax.ppermute(jnp.concatenate([inputs[:2], cotangent[:2]]), "rows", down)
    halo = lambda: (before, after)

    used = 18 * ch + 2
    packed_rows = used + (-used % size)
    chunks, packed = section(
        norm, packed_rows, level_index, level_table, inputs, cotangent, halo,
        first_kernel, second_kernel,
    )
    steps = 2 * (size.bit_length() - 1)
    places = [1, steps - 2] if len(chunks) == 2 and steps >= 4 else list(range(len(chunks)))
    total, (outputs, input_grad) = butterfly_sum(packed, dict(zip(places, chunks)))
    first_sum = total[: 9 * ch].reshape(9, ch, ch)
    second_sum = total[9 * ch : 18 * ch].reshape(9, ch, ch)
    level_sum = total[18 * ch : 18 * ch + 2]
    return (outputs, input_grad, first_sum, second_sum, level_sum)


def solution(mesh):
    return jax.shard_map(
        local,
        mesh=mesh,
        in_specs=(
            P(("groups", "rows"), None, None),
            P(("groups", "rows"), None, None),
            P(),
            P(),
            P(),
            P("groups"),
        ),
        out_specs=(
            P(("groups", "rows"), None, None),
            P(("groups", "rows"), None, None),
            P("groups", None, None),
            P("groups", None, None),
            P("groups", None),
        ),
        check_vma=False,
    )
```

```python
import functools
import math

import jax
import jax.numpy as jnp
from jax import lax
from jax.experimental import pallas as pl
from jax.experimental.pallas import tpu as pltpu
from jax.sharding import PartitionSpec as P


def row_ops(width, ch, scale, shift, top, bottom, count):
    col = lax.broadcasted_iota(jnp.int32, (width, ch), 0)
    not_first = col > 0
    not_last = col < width - 1

    def combine(y):
        left = pltpu.roll(y[:, 0:ch], 1, 0)
        right = pltpu.roll(y[:, 2 * ch:3 * ch], width - 1, 0)
        return y[:, ch:2 * ch] + jnp.where(not_first, left, 0.0) + jnp.where(not_last, right, 0.0)

    def conv_row(ref, r, matrix_ref):
        rows = jnp.concatenate([ref[r], ref[r + 1], ref[r + 2]], axis=1)
        y = jnp.dot(rows, matrix_ref[...], preferred_element_type=jnp.float32)
        return combine(y)

    def shifted(g):
        g32 = g.astype(jnp.float32)
        g0 = jnp.where(not_last, pltpu.roll(g32, width - 1, 0), 0.0)
        g2 = jnp.where(not_first, pltpu.roll(g32, 1, 0), 0.0)
        return jnp.concatenate([g0.astype(g.dtype), g, g2.astype(g.dtype)], axis=1)

    def phase_one(r, x_ref, c_ref, hid_ref, hidt_ref, bf_ref, k1f_ref, k2b_ref, carry):
        lv0, lv1 = carry
        valid = jnp.logical_and(jnp.logical_or(r > 0, top), jnp.logical_or(r < count + 1, bottom))
        first = conv_row(x_ref, r, k1f_ref)
        mixed = first * scale + shift
        sig = 0.5 + 0.5 * jnp.tanh(0.5 * mixed)
        hidden = jnp.where(valid, mixed * sig, 0.0)
        hid_ref[r] = hidden.astype(hid_ref.dtype)
        hidt_ref[r] = hidden.T.astype(hidt_ref.dtype)
        back_hidden = conv_row(c_ref, r, k2b_ref)
        back_mixed = back_hidden * (sig * (1.0 + mixed * (1.0 - sig)))
        bf_ref[r] = jnp.where(valid, back_mixed * scale, 0.0).astype(bf_ref.dtype)
        own = jnp.logical_and(r >= 1, r <= count)
        lv0 = lv0 + jnp.where(own, jnp.sum(back_mixed * first, axis=0, keepdims=True), 0.0)
        lv1 = lv1 + jnp.where(own, jnp.sum(back_mixed, axis=0, keepdims=True), 0.0)
        return lv0, lv1

    def out_row(i, x_ref, c_ref, hid_ref, bf_ref, k2f_ref, k1b_ref, out_ref, ig_ref):
        out_ref[i] = (x_ref[i + 2].astype(jnp.float32) + conv_row(hid_ref, i, k2f_ref)).astype(out_ref.dtype)
        ig_ref[i] = (c_ref[i + 2].astype(jnp.float32) + conv_row(bf_ref, i, k1b_ref)).astype(ig_ref.dtype)

    def g1_row(i, xt_ref, bf_ref, acc1):
        xs = jnp.concatenate([xt_ref[i + 1], xt_ref[i + 2], xt_ref[i + 3]], axis=0)
        acc1[...] += jnp.dot(xs, shifted(bf_ref[i + 1]), preferred_element_type=jnp.float32)

    def g2_row(i, hidt_ref, c_ref, acc2):
        hs = jnp.concatenate([hidt_ref[i], hidt_ref[i + 1], hidt_ref[i + 2]], axis=0)
        acc2[...] += jnp.dot(hs, shifted(c_ref[i + 2]), preferred_element_type=jnp.float32)

    return phase_one, out_row, g1_row, g2_row


def level_and_edges(idx_ref, lt_ref):
    me = lax.axis_index("rows")
    size = lax.axis_size("rows")
    level = lt_ref[idx_ref[0]]
    return level[0:1, :] + 1.0, level[1:2, :], me > 0, me < size - 1


def interior_kernel(idx_ref, lt_ref, x_hbm, c_hbm, k1_ref, k2_ref,
                    hid_ref, bf_ref, hidt_ref, acc1, acc2, lv_ref, k1f, k2f, k2b, k1b,
                    x_ref, c_ref, xt_ref, sems):
    count = hid_ref.shape[0] - 2
    width, ch = hid_ref.shape[1], hid_ref.shape[2]
    copies = [
        pltpu.make_async_copy(x_hbm, x_ref.at[2 : count + 2], sems.at[0]),
        pltpu.make_async_copy(c_hbm, c_ref.at[2 : count + 2], sems.at[1]),
    ]
    for cp in copies:
        cp.start()
    for a in range(3):
        for b in range(3):
            rows = slice(a * ch, (a + 1) * ch)
            cols = slice(b * ch, (b + 1) * ch)
            flip = 3 * (2 - a) + (2 - b)
            k1f[rows, cols] = k1_ref[3 * a + b]
            k2f[rows, cols] = k2_ref[3 * a + b]
            k2b[rows, cols] = k2_ref[flip].astype(jnp.float32).T.astype(k2b.dtype)
            k1b[rows, cols] = k1_ref[flip].astype(jnp.float32).T.astype(k1b.dtype)
    scale, shift, top, bottom = level_and_edges(idx_ref, lt_ref)
    phase_one, out_row, g1_row, g2_row = row_ops(width, ch, scale, shift, top, bottom, count)
    for cp in copies:
        cp.wait()

    zero = jnp.zeros((1, ch), jnp.float32)
    lv0, lv1 = lax.fori_loop(
        2, count, lambda r, cr: phase_one(r, x_ref, c_ref, hid_ref, hidt_ref, bf_ref, k1f, k2b, cr), (zero, zero)
    )
    lv_ref[0:1, :] = lv0
    lv_ref[1:2, :] = lv1

    def transpose_rows(r, carry):
        xt_ref[r] = x_ref[r].astype(jnp.float32).T.astype(xt_ref.dtype)
        return carry

    lax.fori_loop(2, count + 2, transpose_rows, 0)
    acc1[...] = jnp.zeros_like(acc1)
    acc2[...] = jnp.zeros_like(acc2)

    def middle(i, carry):
        g2_row(i, hidt_ref, c_ref, acc2)
        return carry

    lax.fori_loop(2, count - 2, middle, 0)

    def g1_middle(i, carry):
        g1_row(i, xt_ref, bf_ref, acc1)
        return carry

    lax.fori_loop(1, count - 1, g1_middle, 0)


def edge_kernel(norm, idx_ref, lt_ref, x_hbm, c_hbm, before_hbm, after_hbm, hida_hbm, bfa_hbm, hidta_hbm,
                acc1a_ref, acc2a_ref, lva_ref, k1f, k2b,
                grad_ref, hid_ref, bf_ref,
                x_ref, c_ref, hidt_ref, xt_ref, acc1, acc2, sems):
    count = hid_ref.shape[0] - 2
    width, ch = hid_ref.shape[1], hid_ref.shape[2]
    copies = [
        pltpu.make_async_copy(before_hbm.at[0:2], x_ref.at[0:2], sems.at[0]),
        pltpu.make_async_copy(x_hbm, x_ref.at[2 : count + 2], sems.at[1]),
        pltpu.make_async_copy(after_hbm.at[0:2], x_ref.at[count + 2 : count + 4], sems.at[2]),
        pltpu.make_async_copy(before_hbm.at[2:4], c_ref.at[0:2], sems.at[3]),
        pltpu.make_async_copy(c_hbm, c_ref.at[2 : count + 2], sems.at[4]),
        pltpu.make_async_copy(after_hbm.at[2:4], c_ref.at[count + 2 : count + 4], sems.at[5]),
        pltpu.make_async_copy(hida_hbm, hid_ref, sems.at[6]),
        pltpu.make_async_copy(bfa_hbm, bf_ref, sems.at[7]),
        pltpu.make_async_copy(hidta_hbm, hidt_ref, sems.at[8]),
    ]
    for cp in copies:
        cp.start()
    scale, shift, top, bottom = level_and_edges(idx_ref, lt_ref)
    phase_one, out_row, g1_row, g2_row = row_ops(width, ch, scale, shift, top, bottom, count)
    acc1[...] = acc1a_ref[...]
    acc2[...] = acc2a_ref[...]
    for cp in copies:
        cp.wait()

    carry = (lva_ref[0:1, :], lva_ref[1:2, :])
    for r in (0, 1, count, count + 1):
        carry = phase_one(r, x_ref, c_ref, hid_ref, hidt_ref, bf_ref, k1f, k2b, carry)
    lv0, lv1 = carry
    for r in (1, 2, 3, count, count + 1, count + 2):
        xt_ref[r] = x_ref[r].astype(jnp.float32).T.astype(xt_ref.dtype)
    for i in (0, 1, count - 2, count - 1):
        g2_row(i, hidt_ref, c_ref, acc2)
    for i in (0, count - 1):
        g1_row(i, xt_ref, bf_ref, acc1)

    for a in range(3):
        for b in range(3):
            t = 3 * a + b
            blk = (slice(a * ch, (a + 1) * ch), slice(b * ch, (b + 1) * ch))
            grad_ref[t * ch : (t + 1) * ch, :] = acc1[blk] * norm
            grad_ref[(9 + t) * ch : (10 + t) * ch, :] = acc2[blk] * norm
    base = 18 * ch
    tail = grad_ref.shape[0] - base
    grad_ref[base:, :] = jnp.zeros((tail, ch), jnp.float32)
    grad_ref[base : base + 1, :] = lv0 * norm
    grad_ref[base + 1 : base + 2, :] = lv1 * norm


def out_kernel(first_row, aliased, x_hbm, c_hbm, hid_hbm, bf_hbm, k2f, k1b, *refs):
    if aliased:
        refs = refs[2:]
    out_hbm, ig_hbm, x_ref, c_ref, hid_ref, bf_ref, o_ref, g_ref, sems = refs
    n, width, ch = o_ref.shape
    copies = [
        pltpu.make_async_copy(x_hbm.at[first_row : first_row + n], x_ref.at[2 : n + 2], sems.at[0]),
        pltpu.make_async_copy(c_hbm.at[first_row : first_row + n], c_ref.at[2 : n + 2], sems.at[1]),
        pltpu.make_async_copy(hid_hbm.at[first_row : first_row + n + 2], hid_ref, sems.at[2]),
        pltpu.make_async_copy(bf_hbm.at[first_row : first_row + n + 2], bf_ref, sems.at[3]),
    ]
    for cp in copies:
        cp.start()
    one = jnp.ones((1, ch), jnp.float32)
    out_row = row_ops(width, ch, one, one, True, True, n)[1]
    for cp in copies:
        cp.wait()
    for i in range(n):
        out_row(i, x_ref, c_ref, hid_ref, bf_ref, k2f, k1b, o_ref, g_ref)
    stores = [
        pltpu.make_async_copy(o_ref, out_hbm.at[first_row : first_row + n], sems.at[4]),
        pltpu.make_async_copy(g_ref, ig_hbm.at[first_row : first_row + n], sems.at[5]),
    ]
    for cp in stores:
        cp.start()
    for cp in stores:
        cp.wait()


def section(norm, packed_rows, level_index, level_table, inputs, cotangent, before_fn, k1, k2):
    count, width, ch = inputs.shape
    vmem = pltpu.MemorySpace.VMEM if hasattr(pltpu, "MemorySpace") else pltpu.VMEM
    spec = pl.BlockSpec(memory_space=vmem)
    anywhere = pl.BlockSpec(memory_space=pl.ANY)
    smem = pl.BlockSpec(memory_space=pltpu.SMEM)
    big = 3 * ch
    unit = width * big * big * 2
    field = jax.ShapeDtypeStruct((count, width, ch), jnp.bfloat16)
    frame = jax.ShapeDtypeStruct((count + 2, width, ch), jnp.bfloat16)
    frame_t = jax.ShapeDtypeStruct((count + 2, ch, width), jnp.bfloat16)
    square = jax.ShapeDtypeStruct((big, big), jnp.float32)
    params = pltpu.CompilerParams(vmem_limit_bytes=60 * 1024 * 1024)
    matrix = jax.ShapeDtypeStruct((big, big), jnp.bfloat16)
    hid, bf, hidt, acc1, acc2, lv, k1f, k2f, k2b, k1b = pl.pallas_call(
        interior_kernel,
        out_shape=(frame, frame, frame_t, square, square,
                   jax.ShapeDtypeStruct((2, ch), jnp.float32), matrix, matrix, matrix, matrix),
        in_specs=[smem, spec, anywhere, anywhere, spec, spec],
        out_specs=(spec,) * 10,
        scratch_shapes=[
            pltpu.VMEM((count + 4, width, ch), jnp.bfloat16),
            pltpu.VMEM((count + 4, width, ch), jnp.bfloat16),
            pltpu.VMEM((count + 4, ch, width), jnp.bfloat16),
            pltpu.SemaphoreType.DMA((2,)),
        ],
        compiler_params=params,
        cost_estimate=pl.CostEstimate(
            flops=(4 * count - 6) * unit, transcendentals=count * width * ch, bytes_accessed=8 * count * width * ch
        ),
    )(level_index, level_table, inputs, cotangent, k1, k2)
    before, after = before_fn()
    packed, hid, bf = pl.pallas_call(
        functools.partial(edge_kernel, norm),
        out_shape=(jax.ShapeDtypeStruct((packed_rows, ch), jnp.float32), frame, frame),
        in_specs=[smem, spec] + [anywhere] * 7 + [spec] * 5,
        out_specs=(spec, spec, spec),
        scratch_shapes=[
            pltpu.VMEM((count + 4, width, ch), jnp.bfloat16),
            pltpu.VMEM((count + 4, width, ch), jnp.bfloat16),
            pltpu.VMEM((count + 2, ch, width), jnp.bfloat16),
            pltpu.VMEM((count + 4, ch, width), jnp.bfloat16),
            pltpu.VMEM((big, big), jnp.float32),
            pltpu.VMEM((big, big), jnp.float32),
            pltpu.SemaphoreType.DMA((9,)),
        ],
        compiler_params=params,
        cost_estimate=pl.CostEstimate(
            flops=14 * unit, transcendentals=4 * width * ch, bytes_accessed=10 * count * width * ch
        ),
    )(level_index, level_table, inputs, cotangent, before, after, hid, bf, hidt, acc1, acc2, lv, k1f, k2b)
    step = 2 if count % 2 == 0 else count
    whole = jax.ShapeDtypeStruct((count, width, ch), jnp.bfloat16)
    chunks = []
    for first_row in range(0, count, step):
        aliased = first_row > 0
        chunks.append(functools.partial(
            pl.pallas_call(
                functools.partial(out_kernel, first_row, aliased),
                out_shape=(whole, whole),
                in_specs=[anywhere] * 4 + [spec] * 2 + [anywhere] * (2 if aliased else 0),
                out_specs=(anywhere, anywhere),
                scratch_shapes=[
                    pltpu.VMEM((step + 2, width, ch), jnp.bfloat16),
                    pltpu.VMEM((step + 2, width, ch), jnp.bfloat16),
                    pltpu.VMEM((step + 2, width, ch), jnp.bfloat16),
                    pltpu.VMEM((step + 2, width, ch), jnp.bfloat16),
                    pltpu.VMEM((step, width, ch), jnp.bfloat16),
                    pltpu.VMEM((step, width, ch), jnp.bfloat16),
                    pltpu.SemaphoreType.DMA((6,)),
                ],
                input_output_aliases={6: 0, 7: 1} if aliased else {},
                compiler_params=params,
                cost_estimate=pl.CostEstimate(
                    flops=2 * step * unit, transcendentals=0, bytes_accessed=8 * step * width * ch
                ),
            ),
            inputs, cotangent, hid, bf, k2f, k1b,
        ))
    return chunks, packed


def butterfly_sum(block, riders):
    n = lax.axis_size("rows")
    me = lax.axis_index("rows")
    bits = []
    k = 1
    while k < n:
        bits.append(k)
        k *= 2
    other = list(bits)
    if len(bits) > 2:
        other[1], other[2] = bits[2], bits[1]
    orders = list(zip(bits, other))
    even = me % 2 == 0

    def step_of(k0, k1):
        perm = [(i, i ^ (k0 if i % 2 == 0 else k1)) for i in range(n)]
        low = jnp.where(even, (me // k0) % 2, (me // k1) % 2) == 0
        return perm, low

    state = ()
    count = 0
    piece = block
    for k0, k1 in orders:
        perm, low = step_of(k0, k1)
        half = piece.shape[0] // 2
        lo, hi = piece[:half], piece[half:]
        keep = jnp.where(low, lo, hi)
        send = jnp.where(low, hi, lo)
        got = lax.ppermute(send, "rows", perm)
        if count in riders:
            got, state = lax.optimization_barrier((got, riders[count](*state)))
        count += 1
        piece = keep + got
    for k0, k1 in reversed(orders):
        perm, low = step_of(k0, k1)
        got = lax.ppermute(piece, "rows", perm)
        if count in riders:
            got, state = lax.optimization_barrier((got, riders[count](*state)))
        count += 1
        if count < 2 * len(orders):
            piece = jnp.where(low, jnp.concatenate([piece, got]), jnp.concatenate([got, piece]))
    return (jnp.where(low, piece, got), jnp.where(low, got, piece)), state


def local(inputs, cotangent, first_kernel, second_kernel, level_table, level_index):
    count = inputs.shape[0]
    width = inputs.shape[1]
    ch = inputs.shape[2]
    size = lax.axis_size("rows")
    total_rows = count * size
    norm = 1.0 / math.sqrt(total_rows * width)

    up = [(i, i + 1) for i in range(size - 1)]
    down = [(i + 1, i) for i in range(size - 1)]
    before = lax.ppermute(jnp.concatenate([inputs[-2:], cotangent[-2:]]), "rows", up)
    after = lax.ppermute(jnp.concatenate([inputs[:2], cotangent[:2]]), "rows", down)
    halo = lambda: (before, after)

    used = 18 * ch + 2
    packed_rows = used + (-used % size)
    chunks, packed = section(
        norm, packed_rows, level_index, level_table, inputs, cotangent, halo,
        first_kernel, second_kernel,
    )
    steps = 2 * (size.bit_length() - 1)
    if len(chunks) == 4 and steps >= 8:
        places = [1, 2, steps - 3, steps - 2]
    elif len(chunks) == 2 and steps >= 4:
        places = [1, steps - 2]
    else:
        places = list(range(len(chunks)))
    (lower, upper), (outputs, input_grad) = butterfly_sum(packed, dict(zip(places, chunks)))
    half = lower.shape[0]

    def rows(a, b):
        parts = []
        if a < half:
            parts.append(lower[a : min(b, half)])
        if b > half:
            parts.append(upper[max(a, half) - half : b - half])
        return parts[0] if len(parts) == 1 else jnp.concatenate(parts)

    first_sum = rows(0, 9 * ch).reshape(9, ch, ch)
    second_sum = rows(9 * ch, 18 * ch).reshape(9, ch, ch)
    level_sum = rows(18 * ch, 18 * ch + 2)
    return (outputs, input_grad, first_sum, second_sum, level_sum)


def solution(mesh):
    return jax.shard_map(
        local,
        mesh=mesh,
        in_specs=(
            P(("groups", "rows"), None, None),
            P(("groups", "rows"), None, None),
            P(),
            P(),
            P(),
            P("groups"),
        ),
        out_specs=(
            P(("groups", "rows"), None, None),
            P(("groups", "rows"), None, None),
            P("groups", None, None),
            P("groups", None, None),
            P("groups", None),
        ),
        check_vma=False,
    )
```

```python
import functools
import math

import jax
import jax.numpy as jnp
from jax import lax
from jax.experimental import pallas as pl
from jax.experimental.pallas import tpu as pltpu
from jax.sharding import PartitionSpec as P


def row_ops(width, ch, scale, shift, top, bottom, count):
    col = lax.broadcasted_iota(jnp.int32, (width, ch), 0)
    not_first = col > 0
    not_last = col < width - 1

    def combine(y):
        left = pltpu.roll(y[:, 0:ch], 1, 0)
        right = pltpu.roll(y[:, 2 * ch:3 * ch], width - 1, 0)
        return y[:, ch:2 * ch] + jnp.where(not_first, left, 0.0) + jnp.where(not_last, right, 0.0)

    def conv_row(ref, r, matrix_ref):
        rows = jnp.concatenate([ref[r], ref[r + 1], ref[r + 2]], axis=1)
        y = jnp.dot(rows, matrix_ref[...], preferred_element_type=jnp.float32)
        return combine(y)

    def shifted(g):
        g32 = g.astype(jnp.float32)
        g0 = jnp.where(not_last, pltpu.roll(g32, width - 1, 0), 0.0)
        g2 = jnp.where(not_first, pltpu.roll(g32, 1, 0), 0.0)
        return jnp.concatenate([g0.astype(g.dtype), g, g2.astype(g.dtype)], axis=1)

    def phase_one(r, x_ref, c_ref, hid_ref, hidt_ref, bf_ref, k1f_ref, k2b_ref, carry):
        lv0, lv1 = carry
        valid = jnp.logical_and(jnp.logical_or(r > 0, top), jnp.logical_or(r < count + 1, bottom))
        first = conv_row(x_ref, r, k1f_ref)
        mixed = first * scale + shift
        sig = 0.5 + 0.5 * jnp.tanh(0.5 * mixed)
        hidden = jnp.where(valid, mixed * sig, 0.0)
        hid_ref[r] = hidden.astype(hid_ref.dtype)
        hidt_ref[r] = hidden.T.astype(hidt_ref.dtype)
        back_hidden = conv_row(c_ref, r, k2b_ref)
        back_mixed = back_hidden * (sig * (1.0 + mixed * (1.0 - sig)))
        bf_ref[r] = jnp.where(valid, back_mixed * scale, 0.0).astype(bf_ref.dtype)
        own = jnp.logical_and(r >= 1, r <= count)
        lv0 = lv0 + jnp.where(own, jnp.sum(back_mixed * first, axis=0, keepdims=True), 0.0)
        lv1 = lv1 + jnp.where(own, jnp.sum(back_mixed, axis=0, keepdims=True), 0.0)
        return lv0, lv1

    def out_row(i, x_ref, c_ref, hid_ref, bf_ref, k2f_ref, k1b_ref, out_ref, ig_ref):
        out_ref[i] = (x_ref[i + 2].astype(jnp.float32) + conv_row(hid_ref, i, k2f_ref)).astype(out_ref.dtype)
        ig_ref[i] = (c_ref[i + 2].astype(jnp.float32) + conv_row(bf_ref, i, k1b_ref)).astype(ig_ref.dtype)

    def g1_row(i, xt_ref, bf_ref, acc1):
        xs = jnp.concatenate([xt_ref[i + 1], xt_ref[i + 2], xt_ref[i + 3]], axis=0)
        acc1[...] += jnp.dot(xs, shifted(bf_ref[i + 1]), preferred_element_type=jnp.float32)

    def g2_row(i, hidt_ref, c_ref, acc2):
        hs = jnp.concatenate([hidt_ref[i], hidt_ref[i + 1], hidt_ref[i + 2]], axis=0)
        acc2[...] += jnp.dot(hs, shifted(c_ref[i + 2]), preferred_element_type=jnp.float32)

    return phase_one, out_row, g1_row, g2_row


def level_and_edges(idx_ref, lt_ref):
    me = lax.axis_index("rows")
    size = lax.axis_size("rows")
    level = lt_ref[idx_ref[0]]
    return level[0:1, :] + 1.0, level[1:2, :], me > 0, me < size - 1


def interior_kernel(idx_ref, lt_ref, x_hbm, c_hbm, k1_ref, k2_ref,
                    hid_ref, bf_ref, hidt_ref, acc1, acc2, lv_ref, k1f, k2f, k2b, k1b,
                    x_ref, c_ref, xt_ref, sems):
    count = hid_ref.shape[0] - 2
    width, ch = hid_ref.shape[1], hid_ref.shape[2]
    copies = [
        pltpu.make_async_copy(x_hbm, x_ref.at[2 : count + 2], sems.at[0]),
        pltpu.make_async_copy(c_hbm, c_ref.at[2 : count + 2], sems.at[1]),
    ]
    for cp in copies:
        cp.start()
    for a in range(3):
        for b in range(3):
            rows = slice(a * ch, (a + 1) * ch)
            cols = slice(b * ch, (b + 1) * ch)
            flip = 3 * (2 - a) + (2 - b)
            k1f[rows, cols] = k1_ref[3 * a + b]
            k2f[rows, cols] = k2_ref[3 * a + b]
            k2b[rows, cols] = k2_ref[flip].astype(jnp.float32).T.astype(k2b.dtype)
            k1b[rows, cols] = k1_ref[flip].astype(jnp.float32).T.astype(k1b.dtype)
    scale, shift, top, bottom = level_and_edges(idx_ref, lt_ref)
    phase_one, out_row, g1_row, g2_row = row_ops(width, ch, scale, shift, top, bottom, count)
    for cp in copies:
        cp.wait()

    zero = jnp.zeros((1, ch), jnp.float32)
    lv0, lv1 = lax.fori_loop(
        2, count, lambda r, cr: phase_one(r, x_ref, c_ref, hid_ref, hidt_ref, bf_ref, k1f, k2b, cr), (zero, zero),
        unroll=True,
    )
    lv_ref[0:1, :] = lv0
    lv_ref[1:2, :] = lv1

    def transpose_rows(r, carry):
        xt_ref[r] = x_ref[r].astype(jnp.float32).T.astype(xt_ref.dtype)
        return carry

    lax.fori_loop(2, count + 2, transpose_rows, 0, unroll=True)
    acc1[...] = jnp.zeros_like(acc1)
    acc2[...] = jnp.zeros_like(acc2)

    def middle(i, carry):
        g2_row(i, hidt_ref, c_ref, acc2)
        return carry

    lax.fori_loop(2, count - 2, middle, 0, unroll=True)

    def g1_middle(i, carry):
        g1_row(i, xt_ref, bf_ref, acc1)
        return carry

    lax.fori_loop(1, count - 1, g1_middle, 0, unroll=True)


def edge_kernel(norm, idx_ref, lt_ref, x_hbm, c_hbm, before_hbm, after_hbm, hida_hbm, bfa_hbm, hidta_hbm,
                acc1a_ref, acc2a_ref, lva_ref, k1f, k2b,
                grad_ref, hid_ref, bf_ref,
                x_ref, c_ref, hidt_ref, xt_ref, acc1, acc2, sems):
    count = hid_ref.shape[0] - 2
    width, ch = hid_ref.shape[1], hid_ref.shape[2]
    copies = [
        pltpu.make_async_copy(before_hbm.at[0:2], x_ref.at[0:2], sems.at[0]),
        pltpu.make_async_copy(x_hbm, x_ref.at[2 : count + 2], sems.at[1]),
        pltpu.make_async_copy(after_hbm.at[0:2], x_ref.at[count + 2 : count + 4], sems.at[2]),
        pltpu.make_async_copy(before_hbm.at[2:4], c_ref.at[0:2], sems.at[3]),
        pltpu.make_async_copy(c_hbm, c_ref.at[2 : count + 2], sems.at[4]),
        pltpu.make_async_copy(after_hbm.at[2:4], c_ref.at[count + 2 : count + 4], sems.at[5]),
        pltpu.make_async_copy(hida_hbm, hid_ref, sems.at[6]),
        pltpu.make_async_copy(bfa_hbm, bf_ref, sems.at[7]),
        pltpu.make_async_copy(hidta_hbm, hidt_ref, sems.at[8]),
    ]
    for cp in copies:
        cp.start()
    scale, shift, top, bottom = level_and_edges(idx_ref, lt_ref)
    phase_one, out_row, g1_row, g2_row = row_ops(width, ch, scale, shift, top, bottom, count)
    acc1[...] = acc1a_ref[...]
    acc2[...] = acc2a_ref[...]
    for cp in copies:
        cp.wait()

    carry = (lva_ref[0:1, :], lva_ref[1:2, :])
    for r in (0, 1, count, count + 1):
        carry = phase_one(r, x_ref, c_ref, hid_ref, hidt_ref, bf_ref, k1f, k2b, carry)
    lv0, lv1 = carry
    for r in (1, 2, 3, count, count + 1, count + 2):
        xt_ref[r] = x_ref[r].astype(jnp.float32).T.astype(xt_ref.dtype)
    for i in (0, 1, count - 2, count - 1):
        g2_row(i, hidt_ref, c_ref, acc2)
    for i in (0, count - 1):
        g1_row(i, xt_ref, bf_ref, acc1)

    for a in range(3):
        for b in range(3):
            t = 3 * a + b
            blk = (slice(a * ch, (a + 1) * ch), slice(b * ch, (b + 1) * ch))
            grad_ref[t * ch : (t + 1) * ch, :] = acc1[blk] * norm
            grad_ref[(9 + t) * ch : (10 + t) * ch, :] = acc2[blk] * norm
    base = 18 * ch
    tail = grad_ref.shape[0] - base
    grad_ref[base:, :] = jnp.zeros((tail, ch), jnp.float32)
    grad_ref[base : base + 1, :] = lv0 * norm
    grad_ref[base + 1 : base + 2, :] = lv1 * norm


def out_kernel(first_row, aliased, x_hbm, c_hbm, hid_hbm, bf_hbm, k2f, k1b, *refs):
    if aliased:
        refs = refs[2:]
    out_hbm, ig_hbm, x_ref, c_ref, hid_ref, bf_ref, o_ref, g_ref, sems = refs
    n, width, ch = o_ref.shape
    copies = [
        pltpu.make_async_copy(x_hbm.at[first_row : first_row + n], x_ref.at[2 : n + 2], sems.at[0]),
        pltpu.make_async_copy(c_hbm.at[first_row : first_row + n], c_ref.at[2 : n + 2], sems.at[1]),
        pltpu.make_async_copy(hid_hbm.at[first_row : first_row + n + 2], hid_ref, sems.at[2]),
        pltpu.make_async_copy(bf_hbm.at[first_row : first_row + n + 2], bf_ref, sems.at[3]),
    ]
    for cp in copies:
        cp.start()
    one = jnp.ones((1, ch), jnp.float32)
    out_row = row_ops(width, ch, one, one, True, True, n)[1]
    for cp in copies:
        cp.wait()
    for i in range(n):
        out_row(i, x_ref, c_ref, hid_ref, bf_ref, k2f, k1b, o_ref, g_ref)
    stores = [
        pltpu.make_async_copy(o_ref, out_hbm.at[first_row : first_row + n], sems.at[4]),
        pltpu.make_async_copy(g_ref, ig_hbm.at[first_row : first_row + n], sems.at[5]),
    ]
    for cp in stores:
        cp.start()
    for cp in stores:
        cp.wait()


def section(norm, packed_rows, level_index, level_table, inputs, cotangent, before_fn, k1, k2):
    count, width, ch = inputs.shape
    vmem = pltpu.MemorySpace.VMEM if hasattr(pltpu, "MemorySpace") else pltpu.VMEM
    spec = pl.BlockSpec(memory_space=vmem)
    anywhere = pl.BlockSpec(memory_space=pl.ANY)
    smem = pl.BlockSpec(memory_space=pltpu.SMEM)
    big = 3 * ch
    unit = width * big * big * 2
    field = jax.ShapeDtypeStruct((count, width, ch), jnp.bfloat16)
    frame = jax.ShapeDtypeStruct((count + 2, width, ch), jnp.bfloat16)
    frame_t = jax.ShapeDtypeStruct((count + 2, ch, width), jnp.bfloat16)
    square = jax.ShapeDtypeStruct((big, big), jnp.float32)
    params = pltpu.CompilerParams(vmem_limit_bytes=60 * 1024 * 1024)
    matrix = jax.ShapeDtypeStruct((big, big), jnp.bfloat16)
    hid, bf, hidt, acc1, acc2, lv, k1f, k2f, k2b, k1b = pl.pallas_call(
        interior_kernel,
        out_shape=(frame, frame, frame_t, square, square,
                   jax.ShapeDtypeStruct((2, ch), jnp.float32), matrix, matrix, matrix, matrix),
        in_specs=[smem, spec, anywhere, anywhere, spec, spec],
        out_specs=(spec,) * 10,
        scratch_shapes=[
            pltpu.VMEM((count + 4, width, ch), jnp.bfloat16),
            pltpu.VMEM((count + 4, width, ch), jnp.bfloat16),
            pltpu.VMEM((count + 4, ch, width), jnp.bfloat16),
            pltpu.SemaphoreType.DMA((2,)),
        ],
        compiler_params=params,
        cost_estimate=pl.CostEstimate(
            flops=(4 * count - 6) * unit, transcendentals=count * width * ch, bytes_accessed=8 * count * width * ch
        ),
    )(level_index, level_table, inputs, cotangent, k1, k2)
    before, after = before_fn()
    packed, hid, bf = pl.pallas_call(
        functools.partial(edge_kernel, norm),
        out_shape=(jax.ShapeDtypeStruct((packed_rows, ch), jnp.float32), frame, frame),
        in_specs=[smem, spec] + [anywhere] * 7 + [spec] * 5,
        out_specs=(spec, spec, spec),
        scratch_shapes=[
            pltpu.VMEM((count + 4, width, ch), jnp.bfloat16),
            pltpu.VMEM((count + 4, width, ch), jnp.bfloat16),
            pltpu.VMEM((count + 2, ch, width), jnp.bfloat16),
            pltpu.VMEM((count + 4, ch, width), jnp.bfloat16),
            pltpu.VMEM((big, big), jnp.float32),
            pltpu.VMEM((big, big), jnp.float32),
            pltpu.SemaphoreType.DMA((9,)),
        ],
        compiler_params=params,
        cost_estimate=pl.CostEstimate(
            flops=14 * unit, transcendentals=4 * width * ch, bytes_accessed=10 * count * width * ch
        ),
    )(level_index, level_table, inputs, cotangent, before, after, hid, bf, hidt, acc1, acc2, lv, k1f, k2b)
    step = count // 2 if count % 2 == 0 else count
    whole = jax.ShapeDtypeStruct((count, width, ch), jnp.bfloat16)
    chunks = []
    for first_row in range(0, count, step):
        aliased = first_row > 0
        chunks.append(functools.partial(
            pl.pallas_call(
                functools.partial(out_kernel, first_row, aliased),
                out_shape=(whole, whole),
                in_specs=[anywhere] * 4 + [spec] * 2 + [anywhere] * (2 if aliased else 0),
                out_specs=(anywhere, anywhere),
                scratch_shapes=[
                    pltpu.VMEM((step + 2, width, ch), jnp.bfloat16),
                    pltpu.VMEM((step + 2, width, ch), jnp.bfloat16),
                    pltpu.VMEM((step + 2, width, ch), jnp.bfloat16),
                    pltpu.VMEM((step + 2, width, ch), jnp.bfloat16),
                    pltpu.VMEM((step, width, ch), jnp.bfloat16),
                    pltpu.VMEM((step, width, ch), jnp.bfloat16),
                    pltpu.SemaphoreType.DMA((6,)),
                ],
                input_output_aliases={6: 0, 7: 1} if aliased else {},
                compiler_params=params,
                cost_estimate=pl.CostEstimate(
                    flops=2 * step * unit, transcendentals=0, bytes_accessed=8 * step * width * ch
                ),
            ),
            inputs, cotangent, hid, bf, k2f, k1b,
        ))
    return chunks, packed


def butterfly_sum(block, riders):
    n = lax.axis_size("rows")
    me = lax.axis_index("rows")
    bits = []
    k = 1
    while k < n:
        bits.append(k)
        k *= 2
    other = list(bits)
    if len(bits) > 2:
        other[1], other[2] = bits[2], bits[1]
    orders = list(zip(bits, other))
    even = me % 2 == 0

    def step_of(k0, k1):
        perm = [(i, i ^ (k0 if i % 2 == 0 else k1)) for i in range(n)]
        low = jnp.where(even, (me // k0) % 2, (me // k1) % 2) == 0
        return perm, low

    state = ()
    count = 0
    piece = block
    for k0, k1 in orders:
        perm, low = step_of(k0, k1)
        half = piece.shape[0] // 2
        lo, hi = piece[:half], piece[half:]
        keep = jnp.where(low, lo, hi)
        send = jnp.where(low, hi, lo)
        got = lax.ppermute(send, "rows", perm)
        if count in riders:
            got, state = lax.optimization_barrier((got, riders[count](*state)))
        count += 1
        piece = keep + got
    for k0, k1 in reversed(orders):
        perm, low = step_of(k0, k1)
        got = lax.ppermute(piece, "rows", perm)
        if count in riders:
            got, state = lax.optimization_barrier((got, riders[count](*state)))
        count += 1
        piece = jnp.where(low, jnp.concatenate([piece, got]), jnp.concatenate([got, piece]))
    return piece, state


def local(inputs, cotangent, first_kernel, second_kernel, level_table, level_index):
    count = inputs.shape[0]
    width = inputs.shape[1]
    ch = inputs.shape[2]
    size = lax.axis_size("rows")
    total_rows = count * size
    norm = 1.0 / math.sqrt(total_rows * width)

    up = [(i, i + 1) for i in range(size - 1)]
    down = [(i + 1, i) for i in range(size - 1)]
    before = lax.ppermute(jnp.concatenate([inputs[-2:], cotangent[-2:]]), "rows", up)
    after = lax.ppermute(jnp.concatenate([inputs[:2], cotangent[:2]]), "rows", down)
    halo = lambda: (before, after)

    used = 18 * ch + 2
    packed_rows = used + (-used % size)
    chunks, packed = section(
        norm, packed_rows, level_index, level_table, inputs, cotangent, halo,
        first_kernel, second_kernel,
    )
    steps = 2 * (size.bit_length() - 1)
    places = [1, steps - 2] if len(chunks) == 2 and steps >= 4 else list(range(len(chunks)))
    total, (outputs, input_grad) = butterfly_sum(packed, dict(zip(places, chunks)))
    first_sum = total[: 9 * ch].reshape(9, ch, ch)
    second_sum = total[9 * ch : 18 * ch].reshape(9, ch, ch)
    level_sum = total[18 * ch : 18 * ch + 2]
    return (outputs, input_grad, first_sum, second_sum, level_sum)


def solution(mesh):
    return jax.shard_map(
        local,
        mesh=mesh,
        in_specs=(
            P(("groups", "rows"), None, None),
            P(("groups", "rows"), None, None),
            P(),
            P(),
            P(),
            P("groups"),
        ),
        out_specs=(
            P(("groups", "rows"), None, None),
            P(("groups", "rows"), None, None),
            P("groups", None, None),
            P("groups", None, None),
            P("groups", None),
        ),
        check_vma=False,
    )
```

```python
import functools
import math

import jax
import jax.numpy as jnp
from jax import lax
from jax.experimental import pallas as pl
from jax.experimental.pallas import tpu as pltpu
from jax.sharding import PartitionSpec as P


def row_ops(width, ch, scale, shift, top, bottom, count):
    col = lax.broadcasted_iota(jnp.int32, (width, ch), 0)
    not_first = col > 0
    not_last = col < width - 1

    def combine(y):
        left = pltpu.roll(y[:, 0:ch], 1, 0)
        right = pltpu.roll(y[:, 2 * ch:3 * ch], width - 1, 0)
        return y[:, ch:2 * ch] + jnp.where(not_first, left, 0.0) + jnp.where(not_last, right, 0.0)

    def conv_row(ref, r, matrix_ref):
        rows = jnp.concatenate([ref[r], ref[r + 1], ref[r + 2]], axis=1)
        y = jnp.dot(rows, matrix_ref[...], preferred_element_type=jnp.float32)
        return combine(y)

    def shifted(g):
        g32 = g.astype(jnp.float32)
        g0 = jnp.where(not_last, pltpu.roll(g32, width - 1, 0), 0.0)
        g2 = jnp.where(not_first, pltpu.roll(g32, 1, 0), 0.0)
        return jnp.concatenate([g0.astype(g.dtype), g, g2.astype(g.dtype)], axis=1)

    def phase_one(r, x_ref, c_ref, hid_ref, hidt_ref, bf_ref, k1f_ref, k2b_ref, carry):
        lv0, lv1 = carry
        valid = jnp.logical_and(jnp.logical_or(r > 0, top), jnp.logical_or(r < count + 1, bottom))
        first = conv_row(x_ref, r, k1f_ref)
        mixed = first * scale + shift
        sig = 0.5 + 0.5 * jnp.tanh(0.5 * mixed)
        hidden = jnp.where(valid, mixed * sig, 0.0)
        hid_ref[r] = hidden.astype(hid_ref.dtype)
        hidt_ref[r] = hidden.T.astype(hidt_ref.dtype)
        back_hidden = conv_row(c_ref, r, k2b_ref)
        back_mixed = back_hidden * (sig * (1.0 + mixed * (1.0 - sig)))
        bf_ref[r] = jnp.where(valid, back_mixed * scale, 0.0).astype(bf_ref.dtype)
        own = jnp.logical_and(r >= 1, r <= count)
        lv0 = lv0 + jnp.where(own, jnp.sum(back_mixed * first, axis=0, keepdims=True), 0.0)
        lv1 = lv1 + jnp.where(own, jnp.sum(back_mixed, axis=0, keepdims=True), 0.0)
        return lv0, lv1

    def out_row(i, x_ref, c_ref, hid_ref, bf_ref, k2f_ref, k1b_ref, out_ref, ig_ref):
        out_ref[i] = (x_ref[i + 2].astype(jnp.float32) + conv_row(hid_ref, i, k2f_ref)).astype(out_ref.dtype)
        ig_ref[i] = (c_ref[i + 2].astype(jnp.float32) + conv_row(bf_ref, i, k1b_ref)).astype(ig_ref.dtype)

    def g1_row(i, xt_ref, bf_ref, acc1):
        xs = jnp.concatenate([xt_ref[i + 1], xt_ref[i + 2], xt_ref[i + 3]], axis=0)
        acc1[...] += jnp.dot(xs, shifted(bf_ref[i + 1]), preferred_element_type=jnp.float32)

    def g2_row(i, hidt_ref, c_ref, acc2):
        hs = jnp.concatenate([hidt_ref[i], hidt_ref[i + 1], hidt_ref[i + 2]], axis=0)
        acc2[...] += jnp.dot(hs, shifted(c_ref[i + 2]), preferred_element_type=jnp.float32)

    return phase_one, out_row, g1_row, g2_row


def level_and_edges(idx_ref, lt_ref):
    me = lax.axis_index("rows")
    size = lax.axis_size("rows")
    level = lt_ref[idx_ref[0]]
    return level[0:1, :] + 1.0, level[1:2, :], me > 0, me < size - 1


def interior_kernel(idx_ref, lt_ref, x_hbm, c_hbm, k1_ref, k2_ref,
                    hid_ref, bf_ref, hidt_ref, acc1, acc2, lv_ref, k1f, k2f, k2b, k1b,
                    x_ref, c_ref, xt_ref, sems):
    count = hid_ref.shape[0] - 2
    width, ch = hid_ref.shape[1], hid_ref.shape[2]
    copies = [
        pltpu.make_async_copy(x_hbm, x_ref.at[2 : count + 2], sems.at[0]),
        pltpu.make_async_copy(c_hbm, c_ref.at[2 : count + 2], sems.at[1]),
    ]
    for cp in copies:
        cp.start()
    for a in range(3):
        for b in range(3):
            rows = slice(a * ch, (a + 1) * ch)
            cols = slice(b * ch, (b + 1) * ch)
            flip = 3 * (2 - a) + (2 - b)
            k1f[rows, cols] = k1_ref[3 * a + b]
            k2f[rows, cols] = k2_ref[3 * a + b]
            k2b[rows, cols] = k2_ref[flip].astype(jnp.float32).T.astype(k2b.dtype)
            k1b[rows, cols] = k1_ref[flip].astype(jnp.float32).T.astype(k1b.dtype)
    scale, shift, top, bottom = level_and_edges(idx_ref, lt_ref)
    phase_one, out_row, g1_row, g2_row = row_ops(width, ch, scale, shift, top, bottom, count)
    for cp in copies:
        cp.wait()

    zero = jnp.zeros((1, ch), jnp.float32)
    lv0, lv1 = lax.fori_loop(
        2, count, lambda r, cr: phase_one(r, x_ref, c_ref, hid_ref, hidt_ref, bf_ref, k1f, k2b, cr), (zero, zero),
        unroll=True,
    )
    lv_ref[0:1, :] = lv0
    lv_ref[1:2, :] = lv1

    def transpose_rows(r, carry):
        xt_ref[r] = x_ref[r].astype(jnp.float32).T.astype(xt_ref.dtype)
        return carry

    lax.fori_loop(2, count + 2, transpose_rows, 0, unroll=True)
    acc1[...] = jnp.zeros_like(acc1)
    acc2[...] = jnp.zeros_like(acc2)

    def middle(i, carry):
        g2_row(i, hidt_ref, c_ref, acc2)
        return carry

    lax.fori_loop(2, count - 2, middle, 0, unroll=True)

    def g1_middle(i, carry):
        g1_row(i, xt_ref, bf_ref, acc1)
        return carry

    lax.fori_loop(1, count - 1, g1_middle, 0, unroll=True)


def edge_kernel(norm, idx_ref, lt_ref, x_hbm, c_hbm, before_hbm, after_hbm, hida_hbm, bfa_hbm, hidta_hbm,
                acc1a_ref, acc2a_ref, lva_ref, k1f, k2b,
                grad_ref, hid_ref, bf_ref,
                x_ref, c_ref, hidt_ref, xt_ref, acc1, acc2, sems):
    count = hid_ref.shape[0] - 2
    width, ch = hid_ref.shape[1], hid_ref.shape[2]
    copies = [
        pltpu.make_async_copy(before_hbm.at[0:2], x_ref.at[0:2], sems.at[0]),
        pltpu.make_async_copy(x_hbm, x_ref.at[2 : count + 2], sems.at[1]),
        pltpu.make_async_copy(after_hbm.at[0:2], x_ref.at[count + 2 : count + 4], sems.at[2]),
        pltpu.make_async_copy(before_hbm.at[2:4], c_ref.at[0:2], sems.at[3]),
        pltpu.make_async_copy(c_hbm, c_ref.at[2 : count + 2], sems.at[4]),
        pltpu.make_async_copy(after_hbm.at[2:4], c_ref.at[count + 2 : count + 4], sems.at[5]),
    ]
    inner = [
        pltpu.make_async_copy(hida_hbm.at[2:count], hid_ref.at[2:count], sems.at[6]),
        pltpu.make_async_copy(bfa_hbm.at[2:count], bf_ref.at[2:count], sems.at[7]),
        pltpu.make_async_copy(hidta_hbm.at[2:count], hidt_ref.at[2:count], sems.at[8]),
    ]
    for cp in copies + inner:
        cp.start()
    scale, shift, top, bottom = level_and_edges(idx_ref, lt_ref)
    phase_one, out_row, g1_row, g2_row = row_ops(width, ch, scale, shift, top, bottom, count)
    acc1[...] = acc1a_ref[...]
    acc2[...] = acc2a_ref[...]
    for cp in copies:
        cp.wait()

    carry = (lva_ref[0:1, :], lva_ref[1:2, :])
    for r in (0, 1, count, count + 1):
        carry = phase_one(r, x_ref, c_ref, hid_ref, hidt_ref, bf_ref, k1f, k2b, carry)
    lv0, lv1 = carry
    for cp in inner:
        cp.wait()
    for r in (1, 2, 3, count, count + 1, count + 2):
        xt_ref[r] = x_ref[r].astype(jnp.float32).T.astype(xt_ref.dtype)
    for i in (0, 1, count - 2, count - 1):
        g2_row(i, hidt_ref, c_ref, acc2)
    for i in (0, count - 1):
        g1_row(i, xt_ref, bf_ref, acc1)

    for a in range(3):
        for b in range(3):
            t = 3 * a + b
            blk = (slice(a * ch, (a + 1) * ch), slice(b * ch, (b + 1) * ch))
            grad_ref[t * ch : (t + 1) * ch, :] = acc1[blk] * norm
            grad_ref[(9 + t) * ch : (10 + t) * ch, :] = acc2[blk] * norm
    base = 18 * ch
    tail = grad_ref.shape[0] - base
    grad_ref[base:, :] = jnp.zeros((tail, ch), jnp.float32)
    grad_ref[base : base + 1, :] = lv0 * norm
    grad_ref[base + 1 : base + 2, :] = lv1 * norm


def out_kernel(first_row, aliased, x_hbm, c_hbm, hid_hbm, bf_hbm, k2f, k1b, *refs):
    if aliased:
        refs = refs[2:]
    out_hbm, ig_hbm, x_ref, c_ref, hid_ref, bf_ref, o_ref, g_ref, sems = refs
    n, width, ch = o_ref.shape
    copies = [
        pltpu.make_async_copy(x_hbm.at[first_row : first_row + n], x_ref.at[2 : n + 2], sems.at[0]),
        pltpu.make_async_copy(c_hbm.at[first_row : first_row + n], c_ref.at[2 : n + 2], sems.at[1]),
        pltpu.make_async_copy(hid_hbm.at[first_row : first_row + n + 2], hid_ref, sems.at[2]),
        pltpu.make_async_copy(bf_hbm.at[first_row : first_row + n + 2], bf_ref, sems.at[3]),
    ]
    for cp in copies:
        cp.start()
    one = jnp.ones((1, ch), jnp.float32)
    out_row = row_ops(width, ch, one, one, True, True, n)[1]
    for cp in copies:
        cp.wait()
    for i in range(n):
        out_row(i, x_ref, c_ref, hid_ref, bf_ref, k2f, k1b, o_ref, g_ref)
    stores = [
        pltpu.make_async_copy(o_ref, out_hbm.at[first_row : first_row + n], sems.at[4]),
        pltpu.make_async_copy(g_ref, ig_hbm.at[first_row : first_row + n], sems.at[5]),
    ]
    for cp in stores:
        cp.start()
    for cp in stores:
        cp.wait()


def section(norm, packed_rows, level_index, level_table, inputs, cotangent, before_fn, k1, k2):
    count, width, ch = inputs.shape
    vmem = pltpu.MemorySpace.VMEM if hasattr(pltpu, "MemorySpace") else pltpu.VMEM
    spec = pl.BlockSpec(memory_space=vmem)
    anywhere = pl.BlockSpec(memory_space=pl.ANY)
    smem = pl.BlockSpec(memory_space=pltpu.SMEM)
    big = 3 * ch
    unit = width * big * big * 2
    field = jax.ShapeDtypeStruct((count, width, ch), jnp.bfloat16)
    frame = jax.ShapeDtypeStruct((count + 2, width, ch), jnp.bfloat16)
    frame_t = jax.ShapeDtypeStruct((count + 2, ch, width), jnp.bfloat16)
    square = jax.ShapeDtypeStruct((big, big), jnp.float32)
    params = pltpu.CompilerParams(vmem_limit_bytes=60 * 1024 * 1024)
    matrix = jax.ShapeDtypeStruct((big, big), jnp.bfloat16)
    hid, bf, hidt, acc1, acc2, lv, k1f, k2f, k2b, k1b = pl.pallas_call(
        interior_kernel,
        out_shape=(frame, frame, frame_t, square, square,
                   jax.ShapeDtypeStruct((2, ch), jnp.float32), matrix, matrix, matrix, matrix),
        in_specs=[smem, spec, anywhere, anywhere, spec, spec],
        out_specs=(spec,) * 10,
        scratch_shapes=[
            pltpu.VMEM((count + 4, width, ch), jnp.bfloat16),
            pltpu.VMEM((count + 4, width, ch), jnp.bfloat16),
            pltpu.VMEM((count + 4, ch, width), jnp.bfloat16),
            pltpu.SemaphoreType.DMA((2,)),
        ],
        compiler_params=params,
        cost_estimate=pl.CostEstimate(
            flops=(4 * count - 6) * unit, transcendentals=count * width * ch, bytes_accessed=8 * count * width * ch
        ),
    )(level_index, level_table, inputs, cotangent, k1, k2)
    before, after = before_fn()
    packed, hid, bf = pl.pallas_call(
        functools.partial(edge_kernel, norm),
        out_shape=(jax.ShapeDtypeStruct((packed_rows, ch), jnp.float32), frame, frame),
        in_specs=[smem, spec] + [anywhere] * 7 + [spec] * 5,
        out_specs=(spec, spec, spec),
        scratch_shapes=[
            pltpu.VMEM((count + 4, width, ch), jnp.bfloat16),
            pltpu.VMEM((count + 4, width, ch), jnp.bfloat16),
            pltpu.VMEM((count + 2, ch, width), jnp.bfloat16),
            pltpu.VMEM((count + 4, ch, width), jnp.bfloat16),
            pltpu.VMEM((big, big), jnp.float32),
            pltpu.VMEM((big, big), jnp.float32),
            pltpu.SemaphoreType.DMA((9,)),
        ],
        compiler_params=params,
        cost_estimate=pl.CostEstimate(
            flops=14 * unit, transcendentals=4 * width * ch, bytes_accessed=10 * count * width * ch
        ),
    )(level_index, level_table, inputs, cotangent, before, after, hid, bf, hidt, acc1, acc2, lv, k1f, k2b)
    step = count // 2 if count % 2 == 0 else count
    whole = jax.ShapeDtypeStruct((count, width, ch), jnp.bfloat16)
    chunks = []
    for first_row in range(0, count, step):
        aliased = first_row > 0
        chunks.append(functools.partial(
            pl.pallas_call(
                functools.partial(out_kernel, first_row, aliased),
                out_shape=(whole, whole),
                in_specs=[anywhere] * 4 + [spec] * 2 + [anywhere] * (2 if aliased else 0),
                out_specs=(anywhere, anywhere),
                scratch_shapes=[
                    pltpu.VMEM((step + 2, width, ch), jnp.bfloat16),
                    pltpu.VMEM((step + 2, width, ch), jnp.bfloat16),
                    pltpu.VMEM((step + 2, width, ch), jnp.bfloat16),
                    pltpu.VMEM((step + 2, width, ch), jnp.bfloat16),
                    pltpu.VMEM((step, width, ch), jnp.bfloat16),
                    pltpu.VMEM((step, width, ch), jnp.bfloat16),
                    pltpu.SemaphoreType.DMA((6,)),
                ],
                input_output_aliases={6: 0, 7: 1} if aliased else {},
                compiler_params=params,
                cost_estimate=pl.CostEstimate(
                    flops=2 * step * unit, transcendentals=0, bytes_accessed=8 * step * width * ch
                ),
            ),
            inputs, cotangent, hid, bf, k2f, k1b,
        ))
    return chunks, packed


def butterfly_sum(block, riders):
    n = lax.axis_size("rows")
    me = lax.axis_index("rows")
    bits = []
    k = 1
    while k < n:
        bits.append(k)
        k *= 2
    other = list(bits)
    if len(bits) > 2:
        other[1], other[2] = bits[2], bits[1]
    orders = list(zip(bits, other))
    even = me % 2 == 0

    def step_of(k0, k1):
        perm = [(i, i ^ (k0 if i % 2 == 0 else k1)) for i in range(n)]
        low = jnp.where(even, (me // k0) % 2, (me // k1) % 2) == 0
        return perm, low

    state = ()
    count = 0
    piece = block
    for k0, k1 in orders:
        perm, low = step_of(k0, k1)
        half = piece.shape[0] // 2
        lo, hi = piece[:half], piece[half:]
        keep = jnp.where(low, lo, hi)
        send = jnp.where(low, hi, lo)
        got = lax.ppermute(send, "rows", perm)
        if count in riders:
            got, state = lax.optimization_barrier((got, riders[count](*state)))
        count += 1
        piece = keep + got
    for k0, k1 in reversed(orders):
        perm, low = step_of(k0, k1)
        got = lax.ppermute(piece, "rows", perm)
        if count in riders:
            got, state = lax.optimization_barrier((got, riders[count](*state)))
        count += 1
        piece = jnp.where(low, jnp.concatenate([piece, got]), jnp.concatenate([got, piece]))
    return piece, state


def local(inputs, cotangent, first_kernel, second_kernel, level_table, level_index):
    count = inputs.shape[0]
    width = inputs.shape[1]
    ch = inputs.shape[2]
    size = lax.axis_size("rows")
    total_rows = count * size
    norm = 1.0 / math.sqrt(total_rows * width)

    up = [(i, i + 1) for i in range(size - 1)]
    down = [(i + 1, i) for i in range(size - 1)]
    before = lax.ppermute(jnp.concatenate([inputs[-2:], cotangent[-2:]]), "rows", up)
    after = lax.ppermute(jnp.concatenate([inputs[:2], cotangent[:2]]), "rows", down)
    halo = lambda: (before, after)

    used = 18 * ch + 2
    packed_rows = used + (-used % size)
    chunks, packed = section(
        norm, packed_rows, level_index, level_table, inputs, cotangent, halo,
        first_kernel, second_kernel,
    )
    steps = 2 * (size.bit_length() - 1)
    places = [1, steps - 2] if len(chunks) == 2 and steps >= 4 else list(range(len(chunks)))
    total, (outputs, input_grad) = butterfly_sum(packed, dict(zip(places, chunks)))
    first_sum = total[: 9 * ch].reshape(9, ch, ch)
    second_sum = total[9 * ch : 18 * ch].reshape(9, ch, ch)
    level_sum = total[18 * ch : 18 * ch + 2]
    return (outputs, input_grad, first_sum, second_sum, level_sum)


def solution(mesh):
    return jax.shard_map(
        local,
        mesh=mesh,
        in_specs=(
            P(("groups", "rows"), None, None),
            P(("groups", "rows"), None, None),
            P(),
            P(),
            P(),
            P("groups"),
        ),
        out_specs=(
            P(("groups", "rows"), None, None),
            P(("groups", "rows"), None, None),
            P("groups", None, None),
            P("groups", None, None),
            P("groups", None),
        ),
        check_vma=False,
    )
```

```python
import functools
import math

import jax
import jax.numpy as jnp
from jax import lax
from jax.experimental import pallas as pl
from jax.experimental.pallas import tpu as pltpu
from jax.sharding import PartitionSpec as P


def row_ops(width, ch, scale, shift, top, bottom, count):
    col = lax.broadcasted_iota(jnp.int32, (width, ch), 0)
    not_first = col > 0
    not_last = col < width - 1

    def combine(y):
        left = pltpu.roll(y[:, 0:ch], 1, 0)
        right = pltpu.roll(y[:, 2 * ch:3 * ch], width - 1, 0)
        return y[:, ch:2 * ch] + jnp.where(not_first, left, 0.0) + jnp.where(not_last, right, 0.0)

    def conv_row(ref, r, matrix_ref):
        rows = jnp.concatenate([ref[r], ref[r + 1], ref[r + 2]], axis=1)
        y = jnp.dot(rows, matrix_ref[...], preferred_element_type=jnp.float32)
        return combine(y)

    def shifted(g):
        g32 = g.astype(jnp.float32)
        g0 = jnp.where(not_last, pltpu.roll(g32, width - 1, 0), 0.0)
        g2 = jnp.where(not_first, pltpu.roll(g32, 1, 0), 0.0)
        return jnp.concatenate([g0.astype(g.dtype), g, g2.astype(g.dtype)], axis=1)

    def phase_one(r, x_ref, c_ref, hid_ref, hidt_ref, bf_ref, k1f_ref, k2b_ref, carry):
        lv0, lv1 = carry
        valid = jnp.logical_and(jnp.logical_or(r > 0, top), jnp.logical_or(r < count + 1, bottom))
        first = conv_row(x_ref, r, k1f_ref)
        mixed = first * scale + shift
        sig = 0.5 + 0.5 * jnp.tanh(0.5 * mixed)
        hidden = jnp.where(valid, mixed * sig, 0.0)
        hid_ref[r] = hidden.astype(hid_ref.dtype)
        hidt_ref[r] = hidden.T.astype(hidt_ref.dtype)
        back_hidden = conv_row(c_ref, r, k2b_ref)
        back_mixed = back_hidden * (sig * (1.0 + mixed * (1.0 - sig)))
        bf_ref[r] = jnp.where(valid, back_mixed * scale, 0.0).astype(bf_ref.dtype)
        own = jnp.logical_and(r >= 1, r <= count)
        lv0 = lv0 + jnp.where(own, jnp.sum(back_mixed * first, axis=0, keepdims=True), 0.0)
        lv1 = lv1 + jnp.where(own, jnp.sum(back_mixed, axis=0, keepdims=True), 0.0)
        return lv0, lv1

    def out_row(i, x_ref, c_ref, hid_ref, bf_ref, k2f_ref, k1b_ref, out_ref, ig_ref):
        out_ref[i] = (x_ref[i + 2].astype(jnp.float32) + conv_row(hid_ref, i, k2f_ref)).astype(out_ref.dtype)
        ig_ref[i] = (c_ref[i + 2].astype(jnp.float32) + conv_row(bf_ref, i, k1b_ref)).astype(ig_ref.dtype)

    def g1_row(i, xt_ref, bf_ref, acc1):
        xs = jnp.concatenate([xt_ref[i + 1], xt_ref[i + 2], xt_ref[i + 3]], axis=0)
        acc1[...] += jnp.dot(xs, shifted(bf_ref[i + 1]), preferred_element_type=jnp.float32)

    def g2_row(i, hidt_ref, c_ref, acc2):
        hs = jnp.concatenate([hidt_ref[i], hidt_ref[i + 1], hidt_ref[i + 2]], axis=0)
        acc2[...] += jnp.dot(hs, shifted(c_ref[i + 2]), preferred_element_type=jnp.float32)

    return phase_one, out_row, g1_row, g2_row, conv_row


def level_and_edges(idx_ref, lt_ref):
    me = lax.axis_index("rows")
    size = lax.axis_size("rows")
    level = lt_ref[idx_ref[0]]
    return level[0:1, :] + 1.0, level[1:2, :], me > 0, me < size - 1


def interior_kernel(idx_ref, lt_ref, x_hbm, c_hbm, k1_ref, k2_ref,
                    hid_ref, bf_ref, hidt_ref, acc1, acc2, lv_ref, k1f, k2f, k2b, k1b,
                    x_ref, c_ref, xt_ref, sems):
    count = hid_ref.shape[0] - 2
    width, ch = hid_ref.shape[1], hid_ref.shape[2]
    copies = [
        pltpu.make_async_copy(x_hbm, x_ref.at[2 : count + 2], sems.at[0]),
        pltpu.make_async_copy(c_hbm, c_ref.at[2 : count + 2], sems.at[1]),
    ]
    for cp in copies:
        cp.start()
    for a in range(3):
        for b in range(3):
            rows = slice(a * ch, (a + 1) * ch)
            cols = slice(b * ch, (b + 1) * ch)
            flip = 3 * (2 - a) + (2 - b)
            k1f[rows, cols] = k1_ref[3 * a + b]
            k2f[rows, cols] = k2_ref[3 * a + b]
            k2b[rows, cols] = k2_ref[flip].astype(jnp.float32).T.astype(k2b.dtype)
            k1b[rows, cols] = k1_ref[flip].astype(jnp.float32).T.astype(k1b.dtype)
    scale, shift, top, bottom = level_and_edges(idx_ref, lt_ref)
    phase_one, out_row, g1_row, g2_row, _ = row_ops(width, ch, scale, shift, top, bottom, count)
    for cp in copies:
        cp.wait()

    zero = jnp.zeros((1, ch), jnp.float32)
    lv0, lv1 = lax.fori_loop(
        2, count, lambda r, cr: phase_one(r, x_ref, c_ref, hid_ref, hidt_ref, bf_ref, k1f, k2b, cr), (zero, zero),
        unroll=True,
    )
    lv_ref[0:1, :] = lv0
    lv_ref[1:2, :] = lv1

    def transpose_rows(r, carry):
        xt_ref[r] = x_ref[r].astype(jnp.float32).T.astype(xt_ref.dtype)
        return carry

    lax.fori_loop(2, count + 2, transpose_rows, 0, unroll=True)
    acc1[...] = jnp.zeros_like(acc1)
    acc2[...] = jnp.zeros_like(acc2)

    def middle(i, carry):
        g2_row(i, hidt_ref, c_ref, acc2)
        return carry

    lax.fori_loop(2, count - 2, middle, 0, unroll=True)

    def g1_middle(i, carry):
        g1_row(i, xt_ref, bf_ref, acc1)
        return carry

    lax.fori_loop(1, count - 1, g1_middle, 0, unroll=True)


def edge_kernel(norm, idx_ref, lt_ref, x_hbm, c_hbm, before_hbm, after_hbm, hida_hbm, bfa_hbm, hidta_hbm,
                acc1a_ref, acc2a_ref, lva_ref, k1f, k2b,
                grad_ref, hid_ref, bf_ref,
                x_ref, c_ref, hidt_ref, xt_ref, acc1, acc2, sems):
    count = hid_ref.shape[0] - 2
    width, ch = hid_ref.shape[1], hid_ref.shape[2]
    copies = [
        pltpu.make_async_copy(before_hbm.at[0:2], x_ref.at[0:2], sems.at[0]),
        pltpu.make_async_copy(x_hbm, x_ref.at[2 : count + 2], sems.at[1]),
        pltpu.make_async_copy(after_hbm.at[0:2], x_ref.at[count + 2 : count + 4], sems.at[2]),
        pltpu.make_async_copy(before_hbm.at[2:4], c_ref.at[0:2], sems.at[3]),
        pltpu.make_async_copy(c_hbm, c_ref.at[2 : count + 2], sems.at[4]),
        pltpu.make_async_copy(after_hbm.at[2:4], c_ref.at[count + 2 : count + 4], sems.at[5]),
    ]
    inner = [
        pltpu.make_async_copy(hida_hbm.at[2:count], hid_ref.at[2:count], sems.at[6]),
        pltpu.make_async_copy(bfa_hbm.at[2:count], bf_ref.at[2:count], sems.at[7]),
        pltpu.make_async_copy(hidta_hbm.at[2:count], hidt_ref.at[2:count], sems.at[8]),
    ]
    for cp in copies + inner:
        cp.start()
    scale, shift, top, bottom = level_and_edges(idx_ref, lt_ref)
    phase_one, out_row, g1_row, g2_row, _ = row_ops(width, ch, scale, shift, top, bottom, count)
    acc1[...] = acc1a_ref[...]
    acc2[...] = acc2a_ref[...]
    for cp in copies:
        cp.wait()

    carry = (lva_ref[0:1, :], lva_ref[1:2, :])
    for r in (0, 1, count, count + 1):
        carry = phase_one(r, x_ref, c_ref, hid_ref, hidt_ref, bf_ref, k1f, k2b, carry)
    lv0, lv1 = carry
    for cp in inner:
        cp.wait()
    for r in (1, 2, 3, count, count + 1, count + 2):
        xt_ref[r] = x_ref[r].astype(jnp.float32).T.astype(xt_ref.dtype)
    for i in (0, 1, count - 2, count - 1):
        g2_row(i, hidt_ref, c_ref, acc2)
    for i in (0, count - 1):
        g1_row(i, xt_ref, bf_ref, acc1)

    for a in range(3):
        for b in range(3):
            t = 3 * a + b
            blk = (slice(a * ch, (a + 1) * ch), slice(b * ch, (b + 1) * ch))
            grad_ref[t * ch : (t + 1) * ch, :] = acc1[blk] * norm
            grad_ref[(9 + t) * ch : (10 + t) * ch, :] = acc2[blk] * norm
    base = 18 * ch
    tail = grad_ref.shape[0] - base
    grad_ref[base:, :] = jnp.zeros((tail, ch), jnp.float32)
    grad_ref[base : base + 1, :] = lv0 * norm
    grad_ref[base + 1 : base + 2, :] = lv1 * norm


def out_kernel(first_row, aliased, x_hbm, c_hbm, hid_hbm, bf_hbm, k2f, k1b, *refs):
    if aliased:
        refs = refs[2:]
    out_hbm, ig_hbm, x_ref, c_ref, hid_ref, bf_ref, o_ref, g_ref, sems = refs
    n, width, ch = o_ref.shape
    copies = [
        pltpu.make_async_copy(x_hbm.at[first_row : first_row + n], x_ref.at[2 : n + 2], sems.at[0]),
        pltpu.make_async_copy(c_hbm.at[first_row : first_row + n], c_ref.at[2 : n + 2], sems.at[1]),
        pltpu.make_async_copy(hid_hbm.at[first_row : first_row + n + 2], hid_ref, sems.at[2]),
        pltpu.make_async_copy(bf_hbm.at[first_row : first_row + n + 2], bf_ref, sems.at[3]),
    ]
    for cp in copies:
        cp.start()
    one = jnp.ones((1, ch), jnp.float32)
    conv_row = row_ops(width, ch, one, one, True, True, n)[4]
    copies[0].wait()
    copies[2].wait()
    for i in range(n):
        o_ref[i] = (x_ref[i + 2].astype(jnp.float32) + conv_row(hid_ref, i, k2f)).astype(o_ref.dtype)
    copies[1].wait()
    copies[3].wait()
    for i in range(n):
        g_ref[i] = (c_ref[i + 2].astype(jnp.float32) + conv_row(bf_ref, i, k1b)).astype(g_ref.dtype)
    stores = [
        pltpu.make_async_copy(o_ref, out_hbm.at[first_row : first_row + n], sems.at[4]),
        pltpu.make_async_copy(g_ref, ig_hbm.at[first_row : first_row + n], sems.at[5]),
    ]
    for cp in stores:
        cp.start()
    for cp in stores:
        cp.wait()


def section(norm, packed_rows, level_index, level_table, inputs, cotangent, before_fn, k1, k2):
    count, width, ch = inputs.shape
    vmem = pltpu.MemorySpace.VMEM if hasattr(pltpu, "MemorySpace") else pltpu.VMEM
    spec = pl.BlockSpec(memory_space=vmem)
    anywhere = pl.BlockSpec(memory_space=pl.ANY)
    smem = pl.BlockSpec(memory_space=pltpu.SMEM)
    big = 3 * ch
    unit = width * big * big * 2
    field = jax.ShapeDtypeStruct((count, width, ch), jnp.bfloat16)
    frame = jax.ShapeDtypeStruct((count + 2, width, ch), jnp.bfloat16)
    frame_t = jax.ShapeDtypeStruct((count + 2, ch, width), jnp.bfloat16)
    square = jax.ShapeDtypeStruct((big, big), jnp.float32)
    params = pltpu.CompilerParams(vmem_limit_bytes=60 * 1024 * 1024)
    matrix = jax.ShapeDtypeStruct((big, big), jnp.bfloat16)
    hid, bf, hidt, acc1, acc2, lv, k1f, k2f, k2b, k1b = pl.pallas_call(
        interior_kernel,
        out_shape=(frame, frame, frame_t, square, square,
                   jax.ShapeDtypeStruct((2, ch), jnp.float32), matrix, matrix, matrix, matrix),
        in_specs=[smem, spec, anywhere, anywhere, spec, spec],
        out_specs=(spec,) * 10,
        scratch_shapes=[
            pltpu.VMEM((count + 4, width, ch), jnp.bfloat16),
            pltpu.VMEM((count + 4, width, ch), jnp.bfloat16),
            pltpu.VMEM((count + 4, ch, width), jnp.bfloat16),
            pltpu.SemaphoreType.DMA((2,)),
        ],
        compiler_params=params,
        cost_estimate=pl.CostEstimate(
            flops=(4 * count - 6) * unit, transcendentals=count * width * ch, bytes_accessed=8 * count * width * ch
        ),
    )(level_index, level_table, inputs, cotangent, k1, k2)
    before, after = before_fn()
    packed, hid, bf = pl.pallas_call(
        functools.partial(edge_kernel, norm),
        out_shape=(jax.ShapeDtypeStruct((packed_rows, ch), jnp.float32), frame, frame),
        in_specs=[smem, spec] + [anywhere] * 7 + [spec] * 5,
        out_specs=(spec, spec, spec),
        scratch_shapes=[
            pltpu.VMEM((count + 4, width, ch), jnp.bfloat16),
            pltpu.VMEM((count + 4, width, ch), jnp.bfloat16),
            pltpu.VMEM((count + 2, ch, width), jnp.bfloat16),
            pltpu.VMEM((count + 4, ch, width), jnp.bfloat16),
            pltpu.VMEM((big, big), jnp.float32),
            pltpu.VMEM((big, big), jnp.float32),
            pltpu.SemaphoreType.DMA((9,)),
        ],
        compiler_params=params,
        cost_estimate=pl.CostEstimate(
            flops=14 * unit, transcendentals=4 * width * ch, bytes_accessed=10 * count * width * ch
        ),
    )(level_index, level_table, inputs, cotangent, before, after, hid, bf, hidt, acc1, acc2, lv, k1f, k2b)
    step = 2 if count % 2 == 0 else count
    whole = jax.ShapeDtypeStruct((count, width, ch), jnp.bfloat16)
    chunks = []
    for first_row in range(0, count, step):
        aliased = first_row > 0
        chunks.append(functools.partial(
            pl.pallas_call(
                functools.partial(out_kernel, first_row, aliased),
                out_shape=(whole, whole),
                in_specs=[anywhere] * 4 + [spec] * 2 + [anywhere] * (2 if aliased else 0),
                out_specs=(anywhere, anywhere),
                scratch_shapes=[
                    pltpu.VMEM((step + 2, width, ch), jnp.bfloat16),
                    pltpu.VMEM((step + 2, width, ch), jnp.bfloat16),
                    pltpu.VMEM((step + 2, width, ch), jnp.bfloat16),
                    pltpu.VMEM((step + 2, width, ch), jnp.bfloat16),
                    pltpu.VMEM((step, width, ch), jnp.bfloat16),
                    pltpu.VMEM((step, width, ch), jnp.bfloat16),
                    pltpu.SemaphoreType.DMA((6,)),
                ],
                input_output_aliases={6: 0, 7: 1} if aliased else {},
                compiler_params=params,
                cost_estimate=pl.CostEstimate(
                    flops=2 * step * unit, transcendentals=0, bytes_accessed=8 * step * width * ch
                ),
            ),
            inputs, cotangent, hid, bf, k2f, k1b,
        ))
    return chunks, packed


def butterfly_sum(block, riders):
    n = lax.axis_size("rows")
    me = lax.axis_index("rows")
    bits = []
    k = 1
    while k < n:
        bits.append(k)
        k *= 2
    other = list(bits)
    if len(bits) > 2:
        other[1], other[2] = bits[2], bits[1]
    orders = list(zip(bits, other))
    even = me % 2 == 0

    def step_of(k0, k1):
        perm = [(i, i ^ (k0 if i % 2 == 0 else k1)) for i in range(n)]
        low = jnp.where(even, (me // k0) % 2, (me // k1) % 2) == 0
        return perm, low

    state = ()
    count = 0
    piece = block
    for k0, k1 in orders:
        perm, low = step_of(k0, k1)
        half = piece.shape[0] // 2
        lo, hi = piece[:half], piece[half:]
        keep = jnp.where(low, lo, hi)
        send = jnp.where(low, hi, lo)
        got = lax.ppermute(send, "rows", perm)
        if count in riders:
            got, state = lax.optimization_barrier((got, riders[count](*state)))
        count += 1
        piece = keep + got
    for k0, k1 in reversed(orders):
        perm, low = step_of(k0, k1)
        got = lax.ppermute(piece, "rows", perm)
        if count in riders:
            got, state = lax.optimization_barrier((got, riders[count](*state)))
        count += 1
        piece = jnp.where(low, jnp.concatenate([piece, got]), jnp.concatenate([got, piece]))
    return piece, state


def local(inputs, cotangent, first_kernel, second_kernel, level_table, level_index):
    count = inputs.shape[0]
    width = inputs.shape[1]
    ch = inputs.shape[2]
    size = lax.axis_size("rows")
    total_rows = count * size
    norm = 1.0 / math.sqrt(total_rows * width)

    up = [(i, i + 1) for i in range(size - 1)]
    down = [(i + 1, i) for i in range(size - 1)]
    before = lax.ppermute(jnp.concatenate([inputs[-2:], cotangent[-2:]]), "rows", up)
    after = lax.ppermute(jnp.concatenate([inputs[:2], cotangent[:2]]), "rows", down)
    halo = lambda: (before, after)

    used = 18 * ch + 2
    packed_rows = used + (-used % size)
    chunks, packed = section(
        norm, packed_rows, level_index, level_table, inputs, cotangent, halo,
        first_kernel, second_kernel,
    )
    steps = 2 * (size.bit_length() - 1)
    if len(chunks) == 4 and steps >= 8:
        places = [1, 2, steps - 3, steps - 2]
    elif len(chunks) == 2 and steps >= 4:
        places = [1, steps - 2]
    else:
        places = list(range(len(chunks)))
    total, (outputs, input_grad) = butterfly_sum(packed, dict(zip(places, chunks)))
    first_sum = total[: 9 * ch].reshape(9, ch, ch)
    second_sum = total[9 * ch : 18 * ch].reshape(9, ch, ch)
    level_sum = total[18 * ch : 18 * ch + 2]
    return (outputs, input_grad, first_sum, second_sum, level_sum)


def solution(mesh):
    return jax.shard_map(
        local,
        mesh=mesh,
        in_specs=(
            P(("groups", "rows"), None, None),
            P(("groups", "rows"), None, None),
            P(),
            P(),
            P(),
            P("groups"),
        ),
        out_specs=(
            P(("groups", "rows"), None, None),
            P(("groups", "rows"), None, None),
            P("groups", None, None),
            P("groups", None, None),
            P("groups", None),
        ),
        check_vma=False,
    )
```

```python
import functools
import math

import jax
import jax.numpy as jnp
from jax import lax
from jax.experimental import pallas as pl
from jax.experimental.pallas import tpu as pltpu
from jax.sharding import PartitionSpec as P


def row_ops(width, ch, scale, shift, top, bottom, count):
    col = lax.broadcasted_iota(jnp.int32, (width, ch), 0)
    not_first = col > 0
    not_last = col < width - 1

    def combine(y):
        left = pltpu.roll(y[:, 0:ch], 1, 0)
        right = pltpu.roll(y[:, 2 * ch:3 * ch], width - 1, 0)
        return y[:, ch:2 * ch] + jnp.where(not_first, left, 0.0) + jnp.where(not_last, right, 0.0)

    def conv_row(ref, r, matrix_ref):
        rows = jnp.concatenate([ref[r], ref[r + 1], ref[r + 2]], axis=1)
        y = jnp.dot(rows, matrix_ref[...], preferred_element_type=jnp.float32)
        return combine(y)

    def shifted(g):
        g32 = g.astype(jnp.float32)
        g0 = jnp.where(not_last, pltpu.roll(g32, width - 1, 0), 0.0)
        g2 = jnp.where(not_first, pltpu.roll(g32, 1, 0), 0.0)
        return jnp.concatenate([g0.astype(g.dtype), g, g2.astype(g.dtype)], axis=1)

    def phase_one(r, x_ref, c_ref, hid_ref, hidt_ref, bf_ref, k1f_ref, k2b_ref, carry):
        lv0, lv1 = carry
        valid = jnp.logical_and(jnp.logical_or(r > 0, top), jnp.logical_or(r < count + 1, bottom))
        first = conv_row(x_ref, r, k1f_ref)
        mixed = first * scale + shift
        sig = 0.5 + 0.5 * jnp.tanh(0.5 * mixed)
        hidden = jnp.where(valid, mixed * sig, 0.0)
        hid_ref[r] = hidden.astype(hid_ref.dtype)
        hidt_ref[r] = hidden.T.astype(hidt_ref.dtype)
        back_hidden = conv_row(c_ref, r, k2b_ref)
        back_mixed = back_hidden * (sig * (1.0 + mixed * (1.0 - sig)))
        bf_ref[r] = jnp.where(valid, back_mixed * scale, 0.0).astype(bf_ref.dtype)
        own = jnp.logical_and(r >= 1, r <= count)
        lv0 = lv0 + jnp.where(own, jnp.sum(back_mixed * first, axis=0, keepdims=True), 0.0)
        lv1 = lv1 + jnp.where(own, jnp.sum(back_mixed, axis=0, keepdims=True), 0.0)
        return lv0, lv1

    def out_row(i, x_ref, c_ref, hid_ref, bf_ref, k2f_ref, k1b_ref, out_ref, ig_ref):
        out_ref[i] = (x_ref[i + 2].astype(jnp.float32) + conv_row(hid_ref, i, k2f_ref)).astype(out_ref.dtype)
        ig_ref[i] = (c_ref[i + 2].astype(jnp.float32) + conv_row(bf_ref, i, k1b_ref)).astype(ig_ref.dtype)

    def g1_row(i, xt_ref, bf_ref, acc1):
        xs = jnp.concatenate([xt_ref[i + 1], xt_ref[i + 2], xt_ref[i + 3]], axis=0)
        acc1[...] += jnp.dot(xs, shifted(bf_ref[i + 1]), preferred_element_type=jnp.float32)

    def g2_row(i, hidt_ref, c_ref, acc2):
        hs = jnp.concatenate([hidt_ref[i], hidt_ref[i + 1], hidt_ref[i + 2]], axis=0)
        acc2[...] += jnp.dot(hs, shifted(c_ref[i + 2]), preferred_element_type=jnp.float32)

    return phase_one, out_row, g1_row, g2_row, conv_row


def level_and_edges(idx_ref, lt_ref):
    me = lax.axis_index("rows")
    size = lax.axis_size("rows")
    level = lt_ref[idx_ref[0]]
    return level[0:1, :] + 1.0, level[1:2, :], me > 0, me < size - 1


def interior_kernel(idx_ref, lt_ref, x_hbm, c_hbm, k1_ref, k2_ref,
                    hid_ref, bf_ref, hidt_ref, acc1, acc2, lv_ref, k1f, k2f, k2b, k1b,
                    x_ref, c_ref, xt_ref, sems):
    count = hid_ref.shape[0] - 2
    width, ch = hid_ref.shape[1], hid_ref.shape[2]
    copies = [
        pltpu.make_async_copy(x_hbm, x_ref.at[2 : count + 2], sems.at[0]),
        pltpu.make_async_copy(c_hbm, c_ref.at[2 : count + 2], sems.at[1]),
    ]
    for cp in copies:
        cp.start()
    for a in range(3):
        for b in range(3):
            rows = slice(a * ch, (a + 1) * ch)
            cols = slice(b * ch, (b + 1) * ch)
            flip = 3 * (2 - a) + (2 - b)
            k1f[rows, cols] = k1_ref[3 * a + b]
            k2f[rows, cols] = k2_ref[3 * a + b]
            k2b[rows, cols] = k2_ref[flip].astype(jnp.float32).T.astype(k2b.dtype)
            k1b[rows, cols] = k1_ref[flip].astype(jnp.float32).T.astype(k1b.dtype)
    scale, shift, top, bottom = level_and_edges(idx_ref, lt_ref)
    phase_one, out_row, g1_row, g2_row, _ = row_ops(width, ch, scale, shift, top, bottom, count)
    for cp in copies:
        cp.wait()

    zero = jnp.zeros((1, ch), jnp.float32)
    lv0, lv1 = lax.fori_loop(
        2, count, lambda r, cr: phase_one(r, x_ref, c_ref, hid_ref, hidt_ref, bf_ref, k1f, k2b, cr), (zero, zero),
        unroll=True,
    )
    lv_ref[0:1, :] = lv0
    lv_ref[1:2, :] = lv1

    def transpose_rows(r, carry):
        xt_ref[r] = x_ref[r].astype(jnp.float32).T.astype(xt_ref.dtype)
        return carry

    lax.fori_loop(2, count + 2, transpose_rows, 0, unroll=True)
    acc1[...] = jnp.zeros_like(acc1)
    acc2[...] = jnp.zeros_like(acc2)

    def middle(i, carry):
        g2_row(i, hidt_ref, c_ref, acc2)
        return carry

    lax.fori_loop(2, count - 2, middle, 0, unroll=True)

    def g1_middle(i, carry):
        g1_row(i, xt_ref, bf_ref, acc1)
        return carry

    lax.fori_loop(1, count - 1, g1_middle, 0, unroll=True)


def edge_kernel(norm, idx_ref, lt_ref, x_hbm, c_hbm, before_hbm, after_hbm, hida_hbm, bfa_hbm, hidta_hbm,
                acc1a_ref, acc2a_ref, lva_ref, k1f, k2b,
                grad_ref, hid_ref, bf_ref,
                x_ref, c_ref, hidt_ref, xt_ref, acc1, acc2, sems):
    count = hid_ref.shape[0] - 2
    width, ch = hid_ref.shape[1], hid_ref.shape[2]
    copies = [
        pltpu.make_async_copy(before_hbm.at[0:2], x_ref.at[0:2], sems.at[0]),
        pltpu.make_async_copy(x_hbm, x_ref.at[2 : count + 2], sems.at[1]),
        pltpu.make_async_copy(after_hbm.at[0:2], x_ref.at[count + 2 : count + 4], sems.at[2]),
        pltpu.make_async_copy(before_hbm.at[2:4], c_ref.at[0:2], sems.at[3]),
        pltpu.make_async_copy(c_hbm, c_ref.at[2 : count + 2], sems.at[4]),
        pltpu.make_async_copy(after_hbm.at[2:4], c_ref.at[count + 2 : count + 4], sems.at[5]),
    ]
    inner = [
        pltpu.make_async_copy(hida_hbm.at[2:count], hid_ref.at[2:count], sems.at[6]),
        pltpu.make_async_copy(bfa_hbm.at[2:count], bf_ref.at[2:count], sems.at[7]),
        pltpu.make_async_copy(hidta_hbm.at[2:count], hidt_ref.at[2:count], sems.at[8]),
    ]
    for cp in copies + inner:
        cp.start()
    scale, shift, top, bottom = level_and_edges(idx_ref, lt_ref)
    phase_one, out_row, g1_row, g2_row, _ = row_ops(width, ch, scale, shift, top, bottom, count)
    acc1[...] = acc1a_ref[...]
    acc2[...] = acc2a_ref[...]
    for cp in copies:
        cp.wait()

    carry = (lva_ref[0:1, :], lva_ref[1:2, :])
    for r in (0, 1, count, count + 1):
        carry = phase_one(r, x_ref, c_ref, hid_ref, hidt_ref, bf_ref, k1f, k2b, carry)
    lv0, lv1 = carry
    for cp in inner:
        cp.wait()
    for r in (1, 2, 3, count, count + 1, count + 2):
        xt_ref[r] = x_ref[r].astype(jnp.float32).T.astype(xt_ref.dtype)
    for i in (0, 1, count - 2, count - 1):
        g2_row(i, hidt_ref, c_ref, acc2)
    for i in (0, count - 1):
        g1_row(i, xt_ref, bf_ref, acc1)

    for a in range(3):
        for b in range(3):
            t = 3 * a + b
            blk = (slice(a * ch, (a + 1) * ch), slice(b * ch, (b + 1) * ch))
            grad_ref[t * ch : (t + 1) * ch, :] = acc1[blk] * norm
            grad_ref[(9 + t) * ch : (10 + t) * ch, :] = acc2[blk] * norm
    base = 18 * ch
    tail = grad_ref.shape[0] - base
    grad_ref[base:, :] = jnp.zeros((tail, ch), jnp.float32)
    grad_ref[base : base + 1, :] = lv0 * norm
    grad_ref[base + 1 : base + 2, :] = lv1 * norm


def out_kernel(first_row, aliased, x_hbm, c_hbm, hid_hbm, bf_hbm, k2f, k1b, *refs):
    if aliased:
        refs = refs[2:]
    out_hbm, ig_hbm, x_ref, c_ref, hid_ref, bf_ref, o_ref, g_ref, sems = refs
    n, width, ch = o_ref.shape
    copies = [
        pltpu.make_async_copy(x_hbm.at[first_row : first_row + n], x_ref.at[2 : n + 2], sems.at[0]),
        pltpu.make_async_copy(c_hbm.at[first_row : first_row + n], c_ref.at[2 : n + 2], sems.at[1]),
        pltpu.make_async_copy(hid_hbm.at[first_row : first_row + n + 2], hid_ref, sems.at[2]),
        pltpu.make_async_copy(bf_hbm.at[first_row : first_row + n + 2], bf_ref, sems.at[3]),
    ]
    for cp in copies:
        cp.start()
    one = jnp.ones((1, ch), jnp.float32)
    conv_row = row_ops(width, ch, one, one, True, True, n)[4]
    copies[0].wait()
    copies[2].wait()
    for i in range(n):
        o_ref[i] = (x_ref[i + 2].astype(jnp.float32) + conv_row(hid_ref, i, k2f)).astype(o_ref.dtype)
    store_out = pltpu.make_async_copy(o_ref, out_hbm.at[first_row : first_row + n], sems.at[4])
    store_out.start()
    copies[1].wait()
    copies[3].wait()
    for i in range(n):
        g_ref[i] = (c_ref[i + 2].astype(jnp.float32) + conv_row(bf_ref, i, k1b)).astype(g_ref.dtype)
    store_ig = pltpu.make_async_copy(g_ref, ig_hbm.at[first_row : first_row + n], sems.at[5])
    store_ig.start()
    store_out.wait()
    store_ig.wait()


def section(norm, packed_rows, level_index, level_table, inputs, cotangent, before_fn, k1, k2):
    count, width, ch = inputs.shape
    vmem = pltpu.MemorySpace.VMEM if hasattr(pltpu, "MemorySpace") else pltpu.VMEM
    spec = pl.BlockSpec(memory_space=vmem)
    anywhere = pl.BlockSpec(memory_space=pl.ANY)
    smem = pl.BlockSpec(memory_space=pltpu.SMEM)
    big = 3 * ch
    unit = width * big * big * 2
    field = jax.ShapeDtypeStruct((count, width, ch), jnp.bfloat16)
    frame = jax.ShapeDtypeStruct((count + 2, width, ch), jnp.bfloat16)
    frame_t = jax.ShapeDtypeStruct((count + 2, ch, width), jnp.bfloat16)
    square = jax.ShapeDtypeStruct((big, big), jnp.float32)
    params = pltpu.CompilerParams(vmem_limit_bytes=60 * 1024 * 1024)
    matrix = jax.ShapeDtypeStruct((big, big), jnp.bfloat16)
    hid, bf, hidt, acc1, acc2, lv, k1f, k2f, k2b, k1b = pl.pallas_call(
        interior_kernel,
        out_shape=(frame, frame, frame_t, square, square,
                   jax.ShapeDtypeStruct((2, ch), jnp.float32), matrix, matrix, matrix, matrix),
        in_specs=[smem, spec, anywhere, anywhere, spec, spec],
        out_specs=(spec,) * 10,
        scratch_shapes=[
            pltpu.VMEM((count + 4, width, ch), jnp.bfloat16),
            pltpu.VMEM((count + 4, width, ch), jnp.bfloat16),
            pltpu.VMEM((count + 4, ch, width), jnp.bfloat16),
            pltpu.SemaphoreType.DMA((2,)),
        ],
        compiler_params=params,
        cost_estimate=pl.CostEstimate(
            flops=(4 * count - 6) * unit, transcendentals=count * width * ch, bytes_accessed=8 * count * width * ch
        ),
    )(level_index, level_table, inputs, cotangent, k1, k2)
    before, after = before_fn()
    packed, hid, bf = pl.pallas_call(
        functools.partial(edge_kernel, norm),
        out_shape=(jax.ShapeDtypeStruct((packed_rows, ch), jnp.float32), frame, frame),
        in_specs=[smem, spec] + [anywhere] * 7 + [spec] * 5,
        out_specs=(spec, spec, spec),
        scratch_shapes=[
            pltpu.VMEM((count + 4, width, ch), jnp.bfloat16),
            pltpu.VMEM((count + 4, width, ch), jnp.bfloat16),
            pltpu.VMEM((count + 2, ch, width), jnp.bfloat16),
            pltpu.VMEM((count + 4, ch, width), jnp.bfloat16),
            pltpu.VMEM((big, big), jnp.float32),
            pltpu.VMEM((big, big), jnp.float32),
            pltpu.SemaphoreType.DMA((9,)),
        ],
        compiler_params=params,
        cost_estimate=pl.CostEstimate(
            flops=14 * unit, transcendentals=4 * width * ch, bytes_accessed=10 * count * width * ch
        ),
    )(level_index, level_table, inputs, cotangent, before, after, hid, bf, hidt, acc1, acc2, lv, k1f, k2b)
    step = count // 2 if count % 2 == 0 else count
    whole = jax.ShapeDtypeStruct((count, width, ch), jnp.bfloat16)
    chunks = []
    for first_row in range(0, count, step):
        aliased = first_row > 0
        chunks.append(functools.partial(
            pl.pallas_call(
                functools.partial(out_kernel, first_row, aliased),
                out_shape=(whole, whole),
                in_specs=[anywhere] * 4 + [spec] * 2 + [anywhere] * (2 if aliased else 0),
                out_specs=(anywhere, anywhere),
                scratch_shapes=[
                    pltpu.VMEM((step + 2, width, ch), jnp.bfloat16),
                    pltpu.VMEM((step + 2, width, ch), jnp.bfloat16),
                    pltpu.VMEM((step + 2, width, ch), jnp.bfloat16),
                    pltpu.VMEM((step + 2, width, ch), jnp.bfloat16),
                    pltpu.VMEM((step, width, ch), jnp.bfloat16),
                    pltpu.VMEM((step, width, ch), jnp.bfloat16),
                    pltpu.SemaphoreType.DMA((6,)),
                ],
                input_output_aliases={6: 0, 7: 1} if aliased else {},
                compiler_params=params,
                cost_estimate=pl.CostEstimate(
                    flops=2 * step * unit, transcendentals=0, bytes_accessed=8 * step * width * ch
                ),
            ),
            inputs, cotangent, hid, bf, k2f, k1b,
        ))
    return chunks, packed


def butterfly_sum(block, riders):
    n = lax.axis_size("rows")
    me = lax.axis_index("rows")
    bits = []
    k = 1
    while k < n:
        bits.append(k)
        k *= 2
    other = list(bits)
    if len(bits) > 2:
        other[1], other[2] = bits[2], bits[1]
    orders = list(zip(bits, other))
    even = me % 2 == 0

    def step_of(k0, k1):
        perm = [(i, i ^ (k0 if i % 2 == 0 else k1)) for i in range(n)]
        low = jnp.where(even, (me // k0) % 2, (me // k1) % 2) == 0
        return perm, low

    state = ()
    count = 0
    piece = block
    for k0, k1 in orders:
        perm, low = step_of(k0, k1)
        half = piece.shape[0] // 2
        lo, hi = piece[:half], piece[half:]
        keep = jnp.where(low, lo, hi)
        send = jnp.where(low, hi, lo)
        got = lax.ppermute(send, "rows", perm)
        if count in riders:
            got, state = lax.optimization_barrier((got, riders[count](*state)))
        count += 1
        piece = keep + got
    for k0, k1 in reversed(orders):
        perm, low = step_of(k0, k1)
        got = lax.ppermute(piece, "rows", perm)
        if count in riders:
            got, state = lax.optimization_barrier((got, riders[count](*state)))
        count += 1
        piece = jnp.where(low, jnp.concatenate([piece, got]), jnp.concatenate([got, piece]))
    return piece, state


def local(inputs, cotangent, first_kernel, second_kernel, level_table, level_index):
    count = inputs.shape[0]
    width = inputs.shape[1]
    ch = inputs.shape[2]
    size = lax.axis_size("rows")
    total_rows = count * size
    norm = 1.0 / math.sqrt(total_rows * width)

    up = [(i, i + 1) for i in range(size - 1)]
    down = [(i + 1, i) for i in range(size - 1)]
    before = lax.ppermute(jnp.concatenate([inputs[-2:], cotangent[-2:]]), "rows", up)
    after = lax.ppermute(jnp.concatenate([inputs[:2], cotangent[:2]]), "rows", down)
    halo = lambda: (before, after)

    used = 18 * ch + 2
    packed_rows = used + (-used % size)
    chunks, packed = section(
        norm, packed_rows, level_index, level_table, inputs, cotangent, halo,
        first_kernel, second_kernel,
    )
    steps = 2 * (size.bit_length() - 1)
    places = [1, steps - 2] if len(chunks) == 2 and steps >= 4 else list(range(len(chunks)))
    total, (outputs, input_grad) = butterfly_sum(packed, dict(zip(places, chunks)))
    first_sum = total[: 9 * ch].reshape(9, ch, ch)
    second_sum = total[9 * ch : 18 * ch].reshape(9, ch, ch)
    level_sum = total[18 * ch : 18 * ch + 2]
    return (outputs, input_grad, first_sum, second_sum, level_sum)


def solution(mesh):
    return jax.shard_map(
        local,
        mesh=mesh,
        in_specs=(
            P(("groups", "rows"), None, None),
            P(("groups", "rows"), None, None),
            P(),
            P(),
            P(),
            P("groups"),
        ),
        out_specs=(
            P(("groups", "rows"), None, None),
            P(("groups", "rows"), None, None),
            P("groups", None, None),
            P("groups", None, None),
            P("groups", None),
        ),
        check_vma=False,
    )
```

```python
import functools
import math

import jax
import jax.numpy as jnp
from jax import lax
from jax.experimental import pallas as pl
from jax.experimental.pallas import tpu as pltpu
from jax.sharding import PartitionSpec as P


def row_ops(width, ch, scale, shift, top, bottom, count):
    col = lax.broadcasted_iota(jnp.int32, (width, ch), 0)
    not_first = col > 0
    not_last = col < width - 1

    def combine(y):
        left = pltpu.roll(y[:, 0:ch], 1, 0)
        right = pltpu.roll(y[:, 2 * ch:3 * ch], width - 1, 0)
        return y[:, ch:2 * ch] + jnp.where(not_first, left, 0.0) + jnp.where(not_last, right, 0.0)

    def conv_row(ref, r, matrix_ref):
        rows = jnp.concatenate([ref[r], ref[r + 1], ref[r + 2]], axis=1)
        y = jnp.dot(rows, matrix_ref[...], preferred_element_type=jnp.float32)
        return combine(y)

    def shifted(g):
        g32 = g.astype(jnp.float32)
        g0 = jnp.where(not_last, pltpu.roll(g32, width - 1, 0), 0.0)
        g2 = jnp.where(not_first, pltpu.roll(g32, 1, 0), 0.0)
        return jnp.concatenate([g0.astype(g.dtype), g, g2.astype(g.dtype)], axis=1)

    def phase_one(r, x_ref, c_ref, hid_ref, hidt_ref, bf_ref, k1f_ref, k2b_ref, carry):
        lv0, lv1 = carry
        valid = jnp.logical_and(jnp.logical_or(r > 0, top), jnp.logical_or(r < count + 1, bottom))
        first = conv_row(x_ref, r, k1f_ref)
        mixed = first * scale + shift
        sig = 0.5 + 0.5 * jnp.tanh(0.5 * mixed)
        hidden = jnp.where(valid, mixed * sig, 0.0)
        hid_ref[r] = hidden.astype(hid_ref.dtype)
        hidt_ref[r] = hidden.T.astype(hidt_ref.dtype)
        back_hidden = conv_row(c_ref, r, k2b_ref)
        back_mixed = back_hidden * (sig * (1.0 + mixed * (1.0 - sig)))
        bf_ref[r] = jnp.where(valid, back_mixed * scale, 0.0).astype(bf_ref.dtype)
        own = jnp.logical_and(r >= 1, r <= count)
        lv0 = lv0 + jnp.where(own, jnp.sum(back_mixed * first, axis=0, keepdims=True), 0.0)
        lv1 = lv1 + jnp.where(own, jnp.sum(back_mixed, axis=0, keepdims=True), 0.0)
        return lv0, lv1

    def out_row(i, x_ref, c_ref, hid_ref, bf_ref, k2f_ref, k1b_ref, out_ref, ig_ref):
        out_ref[i] = (x_ref[i + 2].astype(jnp.float32) + conv_row(hid_ref, i, k2f_ref)).astype(out_ref.dtype)
        ig_ref[i] = (c_ref[i + 2].astype(jnp.float32) + conv_row(bf_ref, i, k1b_ref)).astype(ig_ref.dtype)

    def g1_row(i, xt_ref, bf_ref, acc1):
        xs = jnp.concatenate([xt_ref[i + 1], xt_ref[i + 2], xt_ref[i + 3]], axis=0)
        acc1[...] += jnp.dot(xs, shifted(bf_ref[i + 1]), preferred_element_type=jnp.float32)

    def g2_row(i, hidt_ref, c_ref, acc2):
        hs = jnp.concatenate([hidt_ref[i], hidt_ref[i + 1], hidt_ref[i + 2]], axis=0)
        acc2[...] += jnp.dot(hs, shifted(c_ref[i + 2]), preferred_element_type=jnp.float32)

    return phase_one, out_row, g1_row, g2_row, conv_row


def level_and_edges(idx_ref, lt_ref):
    me = lax.axis_index("rows")
    size = lax.axis_size("rows")
    level = lt_ref[idx_ref[0]]
    return level[0:1, :] + 1.0, level[1:2, :], me > 0, me < size - 1


def interior_kernel(idx_ref, lt_ref, x_hbm, c_hbm, k1_ref, k2_ref,
                    hid_ref, bf_ref, hidt_ref, acc1, acc2, lv_ref, k1f, k2f, k2b, k1b,
                    x_ref, c_ref, xt_ref, sems):
    count = hid_ref.shape[0] - 2
    width, ch = hid_ref.shape[1], hid_ref.shape[2]
    copies = [
        pltpu.make_async_copy(x_hbm, x_ref.at[2 : count + 2], sems.at[0]),
        pltpu.make_async_copy(c_hbm, c_ref.at[2 : count + 2], sems.at[1]),
    ]
    for cp in copies:
        cp.start()
    for a in range(3):
        for b in range(3):
            rows = slice(a * ch, (a + 1) * ch)
            cols = slice(b * ch, (b + 1) * ch)
            flip = 3 * (2 - a) + (2 - b)
            k1f[rows, cols] = k1_ref[3 * a + b]
            k2f[rows, cols] = k2_ref[3 * a + b]
            k2b[rows, cols] = k2_ref[flip].astype(jnp.float32).T.astype(k2b.dtype)
            k1b[rows, cols] = k1_ref[flip].astype(jnp.float32).T.astype(k1b.dtype)
    scale, shift, top, bottom = level_and_edges(idx_ref, lt_ref)
    phase_one, out_row, g1_row, g2_row, _ = row_ops(width, ch, scale, shift, top, bottom, count)
    for cp in copies:
        cp.wait()

    zero = jnp.zeros((1, ch), jnp.float32)
    lv0, lv1 = lax.fori_loop(
        2, count, lambda r, cr: phase_one(r, x_ref, c_ref, hid_ref, hidt_ref, bf_ref, k1f, k2b, cr), (zero, zero),
        unroll=True,
    )
    lv_ref[0:1, :] = lv0
    lv_ref[1:2, :] = lv1

    def transpose_rows(r, carry):
        xt_ref[r] = x_ref[r].astype(jnp.float32).T.astype(xt_ref.dtype)
        return carry

    lax.fori_loop(2, count + 2, transpose_rows, 0, unroll=True)
    acc1[...] = jnp.zeros_like(acc1)
    acc2[...] = jnp.zeros_like(acc2)

    def middle(i, carry):
        g2_row(i, hidt_ref, c_ref, acc2)
        return carry

    lax.fori_loop(2, count - 2, middle, 0, unroll=True)

    def g1_middle(i, carry):
        g1_row(i, xt_ref, bf_ref, acc1)
        return carry

    lax.fori_loop(1, count - 1, g1_middle, 0, unroll=True)


def edge_kernel(norm, idx_ref, lt_ref, x_hbm, c_hbm, before_hbm, after_hbm, hida_hbm, bfa_hbm, hidta_hbm,
                acc1a_ref, acc2a_ref, lva_ref, k1f, k2b,
                grad_ref, hid_ref, bf_ref,
                x_ref, c_ref, hidt_ref, xt_ref, acc1, acc2, sems):
    count = hid_ref.shape[0] - 2
    width, ch = hid_ref.shape[1], hid_ref.shape[2]
    copies = [
        pltpu.make_async_copy(before_hbm.at[0:2], x_ref.at[0:2], sems.at[0]),
        pltpu.make_async_copy(x_hbm, x_ref.at[2 : count + 2], sems.at[1]),
        pltpu.make_async_copy(after_hbm.at[0:2], x_ref.at[count + 2 : count + 4], sems.at[2]),
        pltpu.make_async_copy(before_hbm.at[2:4], c_ref.at[0:2], sems.at[3]),
        pltpu.make_async_copy(c_hbm, c_ref.at[2 : count + 2], sems.at[4]),
        pltpu.make_async_copy(after_hbm.at[2:4], c_ref.at[count + 2 : count + 4], sems.at[5]),
    ]
    inner = [
        pltpu.make_async_copy(hida_hbm.at[2:count], hid_ref.at[2:count], sems.at[6]),
        pltpu.make_async_copy(bfa_hbm.at[2:count], bf_ref.at[2:count], sems.at[7]),
        pltpu.make_async_copy(hidta_hbm.at[2:count], hidt_ref.at[2:count], sems.at[8]),
    ]
    for cp in copies + inner:
        cp.start()
    scale, shift, top, bottom = level_and_edges(idx_ref, lt_ref)
    phase_one, out_row, g1_row, g2_row, _ = row_ops(width, ch, scale, shift, top, bottom, count)
    acc1[...] = acc1a_ref[...]
    acc2[...] = acc2a_ref[...]
    for cp in copies:
        cp.wait()

    carry = (lva_ref[0:1, :], lva_ref[1:2, :])
    for r in (0, 1, count, count + 1):
        carry = phase_one(r, x_ref, c_ref, hid_ref, hidt_ref, bf_ref, k1f, k2b, carry)
    lv0, lv1 = carry
    for cp in inner:
        cp.wait()
    for r in (1, 2, 3, count, count + 1, count + 2):
        xt_ref[r] = x_ref[r].astype(jnp.float32).T.astype(xt_ref.dtype)
    for i in (0, 1, count - 2, count - 1):
        g2_row(i, hidt_ref, c_ref, acc2)
    for i in (0, count - 1):
        g1_row(i, xt_ref, bf_ref, acc1)

    for a in range(3):
        for b in range(3):
            t = 3 * a + b
            blk = (slice(a * ch, (a + 1) * ch), slice(b * ch, (b + 1) * ch))
            grad_ref[t * ch : (t + 1) * ch, :] = acc1[blk] * norm
            grad_ref[(9 + t) * ch : (10 + t) * ch, :] = acc2[blk] * norm
    base = 18 * ch
    tail = grad_ref.shape[0] - base
    grad_ref[base:, :] = jnp.zeros((tail, ch), jnp.float32)
    grad_ref[base : base + 1, :] = lv0 * norm
    grad_ref[base + 1 : base + 2, :] = lv1 * norm


def out_kernel(first_row, aliased, x_hbm, c_hbm, hid_hbm, bf_hbm, k2f, k1b, *refs):
    if aliased:
        refs = refs[2:]
    out_hbm, ig_hbm, x_ref, c_ref, hid_ref, bf_ref, o_ref, g_ref, sems = refs
    n, width, ch = o_ref.shape
    copies = [
        pltpu.make_async_copy(x_hbm.at[first_row : first_row + n], x_ref.at[2 : n + 2], sems.at[0]),
        pltpu.make_async_copy(c_hbm.at[first_row : first_row + n], c_ref.at[2 : n + 2], sems.at[1]),
        pltpu.make_async_copy(hid_hbm.at[first_row : first_row + n + 2], hid_ref, sems.at[2]),
        pltpu.make_async_copy(bf_hbm.at[first_row : first_row + n + 2], bf_ref, sems.at[3]),
    ]
    for cp in copies:
        cp.start()
    one = jnp.ones((1, ch), jnp.float32)
    conv_row = row_ops(width, ch, one, one, True, True, n)[4]
    copies[0].wait()
    copies[2].wait()
    for i in range(n):
        o_ref[i] = (x_ref[i + 2].astype(jnp.float32) + conv_row(hid_ref, i, k2f)).astype(o_ref.dtype)
    store_out = pltpu.make_async_copy(o_ref, out_hbm.at[first_row : first_row + n], sems.at[4])
    store_out.start()
    copies[1].wait()
    copies[3].wait()
    for i in range(n):
        g_ref[i] = (c_ref[i + 2].astype(jnp.float32) + conv_row(bf_ref, i, k1b)).astype(g_ref.dtype)
    store_ig = pltpu.make_async_copy(g_ref, ig_hbm.at[first_row : first_row + n], sems.at[5])
    store_ig.start()
    store_out.wait()
    store_ig.wait()


def section(norm, packed_rows, level_index, level_table, inputs, cotangent, before_fn, k1, k2):
    count, width, ch = inputs.shape
    vmem = pltpu.MemorySpace.VMEM if hasattr(pltpu, "MemorySpace") else pltpu.VMEM
    spec = pl.BlockSpec(memory_space=vmem)
    anywhere = pl.BlockSpec(memory_space=pl.ANY)
    smem = pl.BlockSpec(memory_space=pltpu.SMEM)
    big = 3 * ch
    unit = width * big * big * 2
    field = jax.ShapeDtypeStruct((count, width, ch), jnp.bfloat16)
    frame = jax.ShapeDtypeStruct((count + 2, width, ch), jnp.bfloat16)
    frame_t = jax.ShapeDtypeStruct((count + 2, ch, width), jnp.bfloat16)
    square = jax.ShapeDtypeStruct((big, big), jnp.float32)
    params = pltpu.CompilerParams(vmem_limit_bytes=60 * 1024 * 1024)
    matrix = jax.ShapeDtypeStruct((big, big), jnp.bfloat16)
    hid, bf, hidt, acc1, acc2, lv, k1f, k2f, k2b, k1b = pl.pallas_call(
        interior_kernel,
        out_shape=(frame, frame, frame_t, square, square,
                   jax.ShapeDtypeStruct((2, ch), jnp.float32), matrix, matrix, matrix, matrix),
        in_specs=[smem, spec, anywhere, anywhere, spec, spec],
        out_specs=(spec,) * 10,
        scratch_shapes=[
            pltpu.VMEM((count + 4, width, ch), jnp.bfloat16),
            pltpu.VMEM((count + 4, width, ch), jnp.bfloat16),
            pltpu.VMEM((count + 4, ch, width), jnp.bfloat16),
            pltpu.SemaphoreType.DMA((2,)),
        ],
        compiler_params=params,
        cost_estimate=pl.CostEstimate(
            flops=(4 * count - 6) * unit, transcendentals=count * width * ch, bytes_accessed=8 * count * width * ch
        ),
    )(level_index, level_table, inputs, cotangent, k1, k2)
    before, after = before_fn()
    packed, hid, bf = pl.pallas_call(
        functools.partial(edge_kernel, norm),
        out_shape=(jax.ShapeDtypeStruct((packed_rows, ch), jnp.float32), frame, frame),
        in_specs=[smem, spec] + [anywhere] * 7 + [spec] * 5,
        out_specs=(spec, spec, spec),
        scratch_shapes=[
            pltpu.VMEM((count + 4, width, ch), jnp.bfloat16),
            pltpu.VMEM((count + 4, width, ch), jnp.bfloat16),
            pltpu.VMEM((count + 2, ch, width), jnp.bfloat16),
            pltpu.VMEM((count + 4, ch, width), jnp.bfloat16),
            pltpu.VMEM((big, big), jnp.float32),
            pltpu.VMEM((big, big), jnp.float32),
            pltpu.SemaphoreType.DMA((9,)),
        ],
        compiler_params=params,
        cost_estimate=pl.CostEstimate(
            flops=14 * unit, transcendentals=4 * width * ch, bytes_accessed=10 * count * width * ch
        ),
    )(level_index, level_table, inputs, cotangent, before, after, hid, bf, hidt, acc1, acc2, lv, k1f, k2b)
    step = count // 2 if count % 2 == 0 else count
    whole = jax.ShapeDtypeStruct((count, width, ch), jnp.bfloat16)
    chunks = []
    for first_row in range(0, count, step):
        aliased = first_row > 0
        chunks.append(functools.partial(
            pl.pallas_call(
                functools.partial(out_kernel, first_row, aliased),
                out_shape=(whole, whole),
                in_specs=[anywhere] * 4 + [spec] * 2 + [anywhere] * (2 if aliased else 0),
                out_specs=(anywhere, anywhere),
                scratch_shapes=[
                    pltpu.VMEM((step + 2, width, ch), jnp.bfloat16),
                    pltpu.VMEM((step + 2, width, ch), jnp.bfloat16),
                    pltpu.VMEM((step + 2, width, ch), jnp.bfloat16),
                    pltpu.VMEM((step + 2, width, ch), jnp.bfloat16),
                    pltpu.VMEM((step, width, ch), jnp.bfloat16),
                    pltpu.VMEM((step, width, ch), jnp.bfloat16),
                    pltpu.SemaphoreType.DMA((6,)),
                ],
                input_output_aliases={6: 0, 7: 1} if aliased else {},
                compiler_params=params,
                cost_estimate=pl.CostEstimate(
                    flops=2 * step * unit, transcendentals=0, bytes_accessed=8 * step * width * ch
                ),
            ),
            inputs, cotangent, hid, bf, k2f, k1b,
        ))
    return chunks, packed


def butterfly_sum(block, riders):
    n = lax.axis_size("rows")
    me = lax.axis_index("rows")
    bits = []
    k = 1
    while k < n:
        bits.append(k)
        k *= 2
    other = list(bits)
    if len(bits) > 2:
        other[1], other[2] = bits[2], bits[1]
    orders = list(zip(bits, other))
    even = me % 2 == 0

    def step_of(k0, k1):
        perm = [(i, i ^ (k0 if i % 2 == 0 else k1)) for i in range(n)]
        low = jnp.where(even, (me // k0) % 2, (me // k1) % 2) == 0
        return perm, low

    state = ()
    count = 0
    piece = block
    for k0, k1 in orders:
        perm, low = step_of(k0, k1)
        half = piece.shape[0] // 2
        lo, hi = piece[:half], piece[half:]
        keep = jnp.where(low, lo, hi)
        send = jnp.where(low, hi, lo)
        got = lax.ppermute(send, "rows", perm)
        if count in riders:
            got, state = lax.optimization_barrier((got, riders[count](*state)))
        count += 1
        piece = keep + got
    for k0, k1 in reversed(orders):
        perm, low = step_of(k0, k1)
        got = lax.ppermute(piece, "rows", perm)
        if count in riders:
            got, state = lax.optimization_barrier((got, riders[count](*state)))
        count += 1
        piece = jnp.where(low, jnp.concatenate([piece, got]), jnp.concatenate([got, piece]))
    return piece, state


def local(inputs, cotangent, first_kernel, second_kernel, level_table, level_index):
    count = inputs.shape[0]
    width = inputs.shape[1]
    ch = inputs.shape[2]
    size = lax.axis_size("rows")
    total_rows = count * size
    norm = 1.0 / math.sqrt(total_rows * width)

    up = [(i, i + 1) for i in range(size - 1)]
    down = [(i + 1, i) for i in range(size - 1)]
    before = lax.ppermute(jnp.concatenate([inputs[-2:], cotangent[-2:]]), "rows", up)
    after = lax.ppermute(jnp.concatenate([inputs[:2], cotangent[:2]]), "rows", down)
    halo = lambda: (before, after)

    used = 18 * ch + 2
    packed_rows = used + (-used % size)
    chunks, packed = section(
        norm, packed_rows, level_index, level_table, inputs, cotangent, halo,
        first_kernel, second_kernel,
    )
    steps = 2 * (size.bit_length() - 1)
    places = [1, steps - 3] if len(chunks) == 2 and steps >= 4 else list(range(len(chunks)))
    total, (outputs, input_grad) = butterfly_sum(packed, dict(zip(places, chunks)))
    first_sum = total[: 9 * ch].reshape(9, ch, ch)
    second_sum = total[9 * ch : 18 * ch].reshape(9, ch, ch)
    level_sum = total[18 * ch : 18 * ch + 2]
    return (outputs, input_grad, first_sum, second_sum, level_sum)


def solution(mesh):
    return jax.shard_map(
        local,
        mesh=mesh,
        in_specs=(
            P(("groups", "rows"), None, None),
            P(("groups", "rows"), None, None),
            P(),
            P(),
            P(),
            P("groups"),
        ),
        out_specs=(
            P(("groups", "rows"), None, None),
            P(("groups", "rows"), None, None),
            P("groups", None, None),
            P("groups", None, None),
            P("groups", None),
        ),
        check_vma=False,
    )
```

```python
import functools
import math

import jax
import jax.numpy as jnp
from jax import lax
from jax.experimental import pallas as pl
from jax.experimental.pallas import tpu as pltpu
from jax.sharding import PartitionSpec as P


def row_ops(width, ch, scale, shift, top, bottom, count):
    col = lax.broadcasted_iota(jnp.int32, (width, ch), 0)
    not_first = col > 0
    not_last = col < width - 1

    def combine(y):
        left = pltpu.roll(y[:, 0:ch], 1, 0)
        right = pltpu.roll(y[:, 2 * ch:3 * ch], width - 1, 0)
        return y[:, ch:2 * ch] + jnp.where(not_first, left, 0.0) + jnp.where(not_last, right, 0.0)

    def conv_row(ref, r, matrix_ref):
        rows = jnp.concatenate([ref[r], ref[r + 1], ref[r + 2]], axis=1)
        y = jnp.dot(rows, matrix_ref[...], preferred_element_type=jnp.float32)
        return combine(y)

    def shifted(g):
        g32 = g.astype(jnp.float32)
        g0 = jnp.where(not_last, pltpu.roll(g32, width - 1, 0), 0.0)
        g2 = jnp.where(not_first, pltpu.roll(g32, 1, 0), 0.0)
        return jnp.concatenate([g0.astype(g.dtype), g, g2.astype(g.dtype)], axis=1)

    def phase_one(r, x_ref, c_ref, hid_ref, hidt_ref, bf_ref, k1f_ref, k2b_ref, carry):
        lv0, lv1 = carry
        valid = jnp.logical_and(jnp.logical_or(r > 0, top), jnp.logical_or(r < count + 1, bottom))
        first = conv_row(x_ref, r, k1f_ref)
        mixed = first * scale + shift
        sig = 0.5 + 0.5 * jnp.tanh(0.5 * mixed)
        hidden = jnp.where(valid, mixed * sig, 0.0)
        hid_ref[r] = hidden.astype(hid_ref.dtype)
        hidt_ref[r] = hidden.T.astype(hidt_ref.dtype)
        back_hidden = conv_row(c_ref, r, k2b_ref)
        back_mixed = back_hidden * (sig * (1.0 + mixed * (1.0 - sig)))
        bf_ref[r] = jnp.where(valid, back_mixed * scale, 0.0).astype(bf_ref.dtype)
        own = jnp.logical_and(r >= 1, r <= count)
        lv0 = lv0 + jnp.where(own, jnp.sum(back_mixed * first, axis=0, keepdims=True), 0.0)
        lv1 = lv1 + jnp.where(own, jnp.sum(back_mixed, axis=0, keepdims=True), 0.0)
        return lv0, lv1

    def out_row(i, x_ref, c_ref, hid_ref, bf_ref, k2f_ref, k1b_ref, out_ref, ig_ref):
        out_ref[i] = (x_ref[i + 2].astype(jnp.float32) + conv_row(hid_ref, i, k2f_ref)).astype(out_ref.dtype)
        ig_ref[i] = (c_ref[i + 2].astype(jnp.float32) + conv_row(bf_ref, i, k1b_ref)).astype(ig_ref.dtype)

    def g1_row(i, xt_ref, bf_ref, acc1):
        xs = jnp.concatenate([xt_ref[i + 1], xt_ref[i + 2], xt_ref[i + 3]], axis=0)
        acc1[...] += jnp.dot(xs, shifted(bf_ref[i + 1]), preferred_element_type=jnp.float32)

    def g2_row(i, hidt_ref, c_ref, acc2):
        hs = jnp.concatenate([hidt_ref[i], hidt_ref[i + 1], hidt_ref[i + 2]], axis=0)
        acc2[...] += jnp.dot(hs, shifted(c_ref[i + 2]), preferred_element_type=jnp.float32)

    return phase_one, out_row, g1_row, g2_row, conv_row


def level_and_edges(idx_ref, lt_ref):
    me = lax.axis_index("rows")
    size = lax.axis_size("rows")
    level = lt_ref[idx_ref[0]]
    return level[0:1, :] + 1.0, level[1:2, :], me > 0, me < size - 1


def interior_kernel(idx_ref, lt_ref, x_hbm, c_hbm, k1_ref, k2_ref,
                    hid_ref, bf_ref, hidt_ref, acc1, acc2, lv_ref, k1f, k2f, k2b, k1b,
                    x_ref, c_ref, xt_ref, sems):
    count = hid_ref.shape[0] - 2
    width, ch = hid_ref.shape[1], hid_ref.shape[2]
    copies = [
        pltpu.make_async_copy(x_hbm, x_ref.at[2 : count + 2], sems.at[0]),
        pltpu.make_async_copy(c_hbm, c_ref.at[2 : count + 2], sems.at[1]),
    ]
    for cp in copies:
        cp.start()
    for a in range(3):
        for b in range(3):
            rows = slice(a * ch, (a + 1) * ch)
            cols = slice(b * ch, (b + 1) * ch)
            flip = 3 * (2 - a) + (2 - b)
            k1f[rows, cols] = k1_ref[3 * a + b]
            k2f[rows, cols] = k2_ref[3 * a + b]
            k2b[rows, cols] = k2_ref[flip].astype(jnp.float32).T.astype(k2b.dtype)
            k1b[rows, cols] = k1_ref[flip].astype(jnp.float32).T.astype(k1b.dtype)
    scale, shift, top, bottom = level_and_edges(idx_ref, lt_ref)
    phase_one, out_row, g1_row, g2_row, _ = row_ops(width, ch, scale, shift, top, bottom, count)
    for cp in copies:
        cp.wait()

    zero = jnp.zeros((1, ch), jnp.float32)
    lv0, lv1 = lax.fori_loop(
        2, count, lambda r, cr: phase_one(r, x_ref, c_ref, hid_ref, hidt_ref, bf_ref, k1f, k2b, cr), (zero, zero),
        unroll=True,
    )
    lv_ref[0:1, :] = lv0
    lv_ref[1:2, :] = lv1

    def transpose_rows(r, carry):
        xt_ref[r] = x_ref[r].astype(jnp.float32).T.astype(xt_ref.dtype)
        return carry

    lax.fori_loop(2, count + 2, transpose_rows, 0, unroll=True)
    acc1[...] = jnp.zeros_like(acc1)
    acc2[...] = jnp.zeros_like(acc2)

    def middle(i, carry):
        g2_row(i, hidt_ref, c_ref, acc2)
        return carry

    lax.fori_loop(2, count - 2, middle, 0, unroll=True)

    def g1_middle(i, carry):
        g1_row(i, xt_ref, bf_ref, acc1)
        return carry

    lax.fori_loop(1, count - 1, g1_middle, 0, unroll=True)


def edge_kernel(norm, idx_ref, lt_ref, x_hbm, c_hbm, before_hbm, after_hbm, hida_hbm, bfa_hbm, hidta_hbm,
                acc1a_ref, acc2a_ref, lva_ref, k1f, k2b,
                grad_ref, hid_ref, bf_ref,
                x_ref, c_ref, hidt_ref, xt_ref, acc1, acc2, sems):
    count = hid_ref.shape[0] - 2
    width, ch = hid_ref.shape[1], hid_ref.shape[2]
    copies = [
        pltpu.make_async_copy(before_hbm.at[0:2], x_ref.at[0:2], sems.at[0]),
        pltpu.make_async_copy(x_hbm, x_ref.at[2 : count + 2], sems.at[1]),
        pltpu.make_async_copy(after_hbm.at[0:2], x_ref.at[count + 2 : count + 4], sems.at[2]),
        pltpu.make_async_copy(before_hbm.at[2:4], c_ref.at[0:2], sems.at[3]),
        pltpu.make_async_copy(c_hbm, c_ref.at[2 : count + 2], sems.at[4]),
        pltpu.make_async_copy(after_hbm.at[2:4], c_ref.at[count + 2 : count + 4], sems.at[5]),
    ]
    inner = [
        pltpu.make_async_copy(hida_hbm.at[2:count], hid_ref.at[2:count], sems.at[6]),
        pltpu.make_async_copy(bfa_hbm.at[2:count], bf_ref.at[2:count], sems.at[7]),
        pltpu.make_async_copy(hidta_hbm.at[2:count], hidt_ref.at[2:count], sems.at[8]),
    ]
    for cp in copies + inner:
        cp.start()
    scale, shift, top, bottom = level_and_edges(idx_ref, lt_ref)
    phase_one, out_row, g1_row, g2_row, _ = row_ops(width, ch, scale, shift, top, bottom, count)
    acc1[...] = acc1a_ref[...]
    acc2[...] = acc2a_ref[...]
    for cp in copies:
        cp.wait()

    carry = (lva_ref[0:1, :], lva_ref[1:2, :])
    for r in (0, 1, count, count + 1):
        carry = phase_one(r, x_ref, c_ref, hid_ref, hidt_ref, bf_ref, k1f, k2b, carry)
    lv0, lv1 = carry
    for cp in inner:
        cp.wait()
    for r in (1, 2, 3, count, count + 1, count + 2):
        xt_ref[r] = x_ref[r].astype(jnp.float32).T.astype(xt_ref.dtype)
    for i in (0, 1, count - 2, count - 1):
        g2_row(i, hidt_ref, c_ref, acc2)
    for i in (0, count - 1):
        g1_row(i, xt_ref, bf_ref, acc1)

    half = grad_ref.shape[0] // 2
    base = 9 * ch
    grad_ref[base:half, :] = jnp.zeros((half - base, ch), jnp.float32)
    grad_ref[half + base :, :] = jnp.zeros((grad_ref.shape[0] - half - base, ch), jnp.float32)
    for a in range(3):
        for b in range(3):
            t = 3 * a + b
            blk = (slice(a * ch, (a + 1) * ch), slice(b * ch, (b + 1) * ch))
            grad_ref[t * ch : (t + 1) * ch, :] = acc1[blk] * norm
            grad_ref[half + t * ch : half + (t + 1) * ch, :] = acc2[blk] * norm
    grad_ref[base : base + 1, :] = lv0 * norm
    grad_ref[base + 1 : base + 2, :] = lv1 * norm


def out_kernel(first_row, aliased, x_hbm, c_hbm, hid_hbm, bf_hbm, k2f, k1b, *refs):
    if aliased:
        refs = refs[2:]
    out_hbm, ig_hbm, x_ref, c_ref, hid_ref, bf_ref, o_ref, g_ref, sems = refs
    n, width, ch = o_ref.shape
    copies = [
        pltpu.make_async_copy(x_hbm.at[first_row : first_row + n], x_ref.at[2 : n + 2], sems.at[0]),
        pltpu.make_async_copy(c_hbm.at[first_row : first_row + n], c_ref.at[2 : n + 2], sems.at[1]),
        pltpu.make_async_copy(hid_hbm.at[first_row : first_row + n + 2], hid_ref, sems.at[2]),
        pltpu.make_async_copy(bf_hbm.at[first_row : first_row + n + 2], bf_ref, sems.at[3]),
    ]
    for cp in copies:
        cp.start()
    one = jnp.ones((1, ch), jnp.float32)
    conv_row = row_ops(width, ch, one, one, True, True, n)[4]
    copies[0].wait()
    copies[2].wait()
    for i in range(n):
        o_ref[i] = (x_ref[i + 2].astype(jnp.float32) + conv_row(hid_ref, i, k2f)).astype(o_ref.dtype)
    store_out = pltpu.make_async_copy(o_ref, out_hbm.at[first_row : first_row + n], sems.at[4])
    store_out.start()
    copies[1].wait()
    copies[3].wait()
    for i in range(n):
        g_ref[i] = (c_ref[i + 2].astype(jnp.float32) + conv_row(bf_ref, i, k1b)).astype(g_ref.dtype)
    store_ig = pltpu.make_async_copy(g_ref, ig_hbm.at[first_row : first_row + n], sems.at[5])
    store_ig.start()
    store_out.wait()
    store_ig.wait()


def section(norm, packed_rows, level_index, level_table, inputs, cotangent, before_fn, k1, k2):
    count, width, ch = inputs.shape
    vmem = pltpu.MemorySpace.VMEM if hasattr(pltpu, "MemorySpace") else pltpu.VMEM
    spec = pl.BlockSpec(memory_space=vmem)
    anywhere = pl.BlockSpec(memory_space=pl.ANY)
    smem = pl.BlockSpec(memory_space=pltpu.SMEM)
    big = 3 * ch
    unit = width * big * big * 2
    field = jax.ShapeDtypeStruct((count, width, ch), jnp.bfloat16)
    frame = jax.ShapeDtypeStruct((count + 2, width, ch), jnp.bfloat16)
    frame_t = jax.ShapeDtypeStruct((count + 2, ch, width), jnp.bfloat16)
    square = jax.ShapeDtypeStruct((big, big), jnp.float32)
    params = pltpu.CompilerParams(vmem_limit_bytes=60 * 1024 * 1024)
    matrix = jax.ShapeDtypeStruct((big, big), jnp.bfloat16)
    hid, bf, hidt, acc1, acc2, lv, k1f, k2f, k2b, k1b = pl.pallas_call(
        interior_kernel,
        out_shape=(frame, frame, frame_t, square, square,
                   jax.ShapeDtypeStruct((2, ch), jnp.float32), matrix, matrix, matrix, matrix),
        in_specs=[smem, spec, anywhere, anywhere, spec, spec],
        out_specs=(spec,) * 10,
        scratch_shapes=[
            pltpu.VMEM((count + 4, width, ch), jnp.bfloat16),
            pltpu.VMEM((count + 4, width, ch), jnp.bfloat16),
            pltpu.VMEM((count + 4, ch, width), jnp.bfloat16),
            pltpu.SemaphoreType.DMA((2,)),
        ],
        compiler_params=params,
        cost_estimate=pl.CostEstimate(
            flops=(4 * count - 6) * unit, transcendentals=count * width * ch, bytes_accessed=8 * count * width * ch
        ),
    )(level_index, level_table, inputs, cotangent, k1, k2)
    before, after = before_fn()
    packed, hid, bf = pl.pallas_call(
        functools.partial(edge_kernel, norm),
        out_shape=(jax.ShapeDtypeStruct((packed_rows, ch), jnp.float32), frame, frame),
        in_specs=[smem, spec] + [anywhere] * 7 + [spec] * 5,
        out_specs=(spec, spec, spec),
        scratch_shapes=[
            pltpu.VMEM((count + 4, width, ch), jnp.bfloat16),
            pltpu.VMEM((count + 4, width, ch), jnp.bfloat16),
            pltpu.VMEM((count + 2, ch, width), jnp.bfloat16),
            pltpu.VMEM((count + 4, ch, width), jnp.bfloat16),
            pltpu.VMEM((big, big), jnp.float32),
            pltpu.VMEM((big, big), jnp.float32),
            pltpu.SemaphoreType.DMA((9,)),
        ],
        compiler_params=params,
        cost_estimate=pl.CostEstimate(
            flops=14 * unit, transcendentals=4 * width * ch, bytes_accessed=10 * count * width * ch
        ),
    )(level_index, level_table, inputs, cotangent, before, after, hid, bf, hidt, acc1, acc2, lv, k1f, k2b)
    step = count // 2 if count % 2 == 0 else count
    whole = jax.ShapeDtypeStruct((count, width, ch), jnp.bfloat16)
    chunks = []
    for first_row in range(0, count, step):
        aliased = first_row > 0
        chunks.append(functools.partial(
            pl.pallas_call(
                functools.partial(out_kernel, first_row, aliased),
                out_shape=(whole, whole),
                in_specs=[anywhere] * 4 + [spec] * 2 + [anywhere] * (2 if aliased else 0),
                out_specs=(anywhere, anywhere),
                scratch_shapes=[
                    pltpu.VMEM((step + 2, width, ch), jnp.bfloat16),
                    pltpu.VMEM((step + 2, width, ch), jnp.bfloat16),
                    pltpu.VMEM((step + 2, width, ch), jnp.bfloat16),
                    pltpu.VMEM((step + 2, width, ch), jnp.bfloat16),
                    pltpu.VMEM((step, width, ch), jnp.bfloat16),
                    pltpu.VMEM((step, width, ch), jnp.bfloat16),
                    pltpu.SemaphoreType.DMA((6,)),
                ],
                input_output_aliases={6: 0, 7: 1} if aliased else {},
                compiler_params=params,
                cost_estimate=pl.CostEstimate(
                    flops=2 * step * unit, transcendentals=0, bytes_accessed=8 * step * width * ch
                ),
            ),
            inputs, cotangent, hid, bf, k2f, k1b,
        ))
    return chunks, packed


def butterfly_sum(block, riders):
    n = lax.axis_size("rows")
    me = lax.axis_index("rows")
    bits = []
    k = 1
    while k < n:
        bits.append(k)
        k *= 2
    other = list(bits)
    if len(bits) > 2:
        other[1], other[2] = bits[2], bits[1]
    orders = list(zip(bits, other))
    even = me % 2 == 0

    def step_of(k0, k1):
        perm = [(i, i ^ (k0 if i % 2 == 0 else k1)) for i in range(n)]
        low = jnp.where(even, (me // k0) % 2, (me // k1) % 2) == 0
        return perm, low

    state = ()
    count = 0
    piece = block
    for k0, k1 in orders:
        perm, low = step_of(k0, k1)
        half = piece.shape[0] // 2
        lo, hi = piece[:half], piece[half:]
        keep = jnp.where(low, lo, hi)
        send = jnp.where(low, hi, lo)
        got = lax.ppermute(send, "rows", perm)
        if count in riders:
            got, state = lax.optimization_barrier((got, riders[count](*state)))
        count += 1
        piece = keep + got
    for k0, k1 in reversed(orders):
        perm, low = step_of(k0, k1)
        got = lax.ppermute(piece, "rows", perm)
        if count in riders:
            got, state = lax.optimization_barrier((got, riders[count](*state)))
        count += 1
        if count < 2 * len(orders):
            piece = jnp.where(low, jnp.concatenate([piece, got]), jnp.concatenate([got, piece]))
    return (jnp.where(low, piece, got), jnp.where(low, got, piece)), state


def local(inputs, cotangent, first_kernel, second_kernel, level_table, level_index):
    count = inputs.shape[0]
    width = inputs.shape[1]
    ch = inputs.shape[2]
    size = lax.axis_size("rows")
    total_rows = count * size
    norm = 1.0 / math.sqrt(total_rows * width)

    up = [(i, i + 1) for i in range(size - 1)]
    down = [(i + 1, i) for i in range(size - 1)]
    before = lax.ppermute(jnp.concatenate([inputs[-2:], cotangent[-2:]]), "rows", up)
    after = lax.ppermute(jnp.concatenate([inputs[:2], cotangent[:2]]), "rows", down)
    halo = lambda: (before, after)

    used = 9 * ch + 2
    half_rows = used + (-used % max(size // 2, 1))
    packed_rows = 2 * half_rows
    chunks, packed = section(
        norm, packed_rows, level_index, level_table, inputs, cotangent, halo,
        first_kernel, second_kernel,
    )
    steps = 2 * (size.bit_length() - 1)
    places = [1, steps - 2] if len(chunks) == 2 and steps >= 4 else list(range(len(chunks)))
    (lower, upper), (outputs, input_grad) = butterfly_sum(packed, dict(zip(places, chunks)))
    first_sum = lower[: 9 * ch].reshape(9, ch, ch)
    level_sum = lower[9 * ch : 9 * ch + 2]
    second_sum = upper[: 9 * ch].reshape(9, ch, ch)
    return (outputs, input_grad, first_sum, second_sum, level_sum)


def solution(mesh):
    return jax.shard_map(
        local,
        mesh=mesh,
        in_specs=(
            P(("groups", "rows"), None, None),
            P(("groups", "rows"), None, None),
            P(),
            P(),
            P(),
            P("groups"),
        ),
        out_specs=(
            P(("groups", "rows"), None, None),
            P(("groups", "rows"), None, None),
            P("groups", None, None),
            P("groups", None, None),
            P("groups", None),
        ),
        check_vma=False,
    )
```

```python
import functools
import math

import jax
import jax.numpy as jnp
from jax import lax
from jax.experimental import pallas as pl
from jax.experimental.pallas import tpu as pltpu
from jax.sharding import PartitionSpec as P


def row_ops(width, ch, scale, shift, top, bottom, count):
    col = lax.broadcasted_iota(jnp.int32, (width, ch), 0)
    not_first = col > 0
    not_last = col < width - 1

    def combine(y):
        left = pltpu.roll(y[:, 0:ch], 1, 0)
        right = pltpu.roll(y[:, 2 * ch:3 * ch], width - 1, 0)
        return y[:, ch:2 * ch] + jnp.where(not_first, left, 0.0) + jnp.where(not_last, right, 0.0)

    def conv_row(ref, r, matrix_ref):
        rows = jnp.concatenate([ref[r], ref[r + 1], ref[r + 2]], axis=1)
        y = jnp.dot(rows, matrix_ref[...], preferred_element_type=jnp.float32)
        return combine(y)

    def shifted(g):
        g32 = g.astype(jnp.float32)
        g0 = jnp.where(not_last, pltpu.roll(g32, width - 1, 0), 0.0)
        g2 = jnp.where(not_first, pltpu.roll(g32, 1, 0), 0.0)
        return jnp.concatenate([g0.astype(g.dtype), g, g2.astype(g.dtype)], axis=1)

    def phase_one(r, x_ref, c_ref, hid_ref, hidt_ref, bf_ref, k1f_ref, k2b_ref, carry):
        lv0, lv1 = carry
        valid = jnp.logical_and(jnp.logical_or(r > 0, top), jnp.logical_or(r < count + 1, bottom))
        first = conv_row(x_ref, r, k1f_ref)
        mixed = first * scale + shift
        sig = 0.5 + 0.5 * jnp.tanh(0.5 * mixed)
        hidden = jnp.where(valid, mixed * sig, 0.0)
        hid_ref[r] = hidden.astype(hid_ref.dtype)
        hidt_ref[r] = hidden.T.astype(hidt_ref.dtype)
        back_hidden = conv_row(c_ref, r, k2b_ref)
        back_mixed = back_hidden * (sig * (1.0 + mixed * (1.0 - sig)))
        bf_ref[r] = jnp.where(valid, back_mixed * scale, 0.0).astype(bf_ref.dtype)
        own = jnp.logical_and(r >= 1, r <= count)
        lv0 = lv0 + jnp.where(own, jnp.sum(back_mixed * first, axis=0, keepdims=True), 0.0)
        lv1 = lv1 + jnp.where(own, jnp.sum(back_mixed, axis=0, keepdims=True), 0.0)
        return lv0, lv1

    def out_row(i, x_ref, c_ref, hid_ref, bf_ref, k2f_ref, k1b_ref, out_ref, ig_ref):
        out_ref[i] = (x_ref[i + 2].astype(jnp.float32) + conv_row(hid_ref, i, k2f_ref)).astype(out_ref.dtype)
        ig_ref[i] = (c_ref[i + 2].astype(jnp.float32) + conv_row(bf_ref, i, k1b_ref)).astype(ig_ref.dtype)

    def g1_row(i, xt_ref, bf_ref, acc1, fresh=False):
        xs = jnp.concatenate([xt_ref[i + 1], xt_ref[i + 2], xt_ref[i + 3]], axis=0)
        term = jnp.dot(xs, shifted(bf_ref[i + 1]), preferred_element_type=jnp.float32)
        acc1[...] = term if fresh else acc1[...] + term

    def g2_row(i, hidt_ref, c_ref, acc2, fresh=False):
        hs = jnp.concatenate([hidt_ref[i], hidt_ref[i + 1], hidt_ref[i + 2]], axis=0)
        term = jnp.dot(hs, shifted(c_ref[i + 2]), preferred_element_type=jnp.float32)
        acc2[...] = term if fresh else acc2[...] + term

    return phase_one, out_row, g1_row, g2_row, conv_row


def level_and_edges(idx_ref, lt_ref):
    me = lax.axis_index("rows")
    size = lax.axis_size("rows")
    level = lt_ref[idx_ref[0]]
    return level[0:1, :] + 1.0, level[1:2, :], me > 0, me < size - 1


def interior_kernel(idx_ref, lt_ref, x_hbm, c_hbm, k1_ref, k2_ref,
                    hid_ref, bf_ref, hidt_ref, acc1, acc2, lv_ref, k1f, k2f, k2b, k1b,
                    x_ref, c_ref, xt_ref, sems):
    count = hid_ref.shape[0] - 2
    width, ch = hid_ref.shape[1], hid_ref.shape[2]
    copies = [
        pltpu.make_async_copy(x_hbm, x_ref.at[2 : count + 2], sems.at[0]),
        pltpu.make_async_copy(c_hbm, c_ref.at[2 : count + 2], sems.at[1]),
    ]
    for cp in copies:
        cp.start()
    for a in range(3):
        for b in range(3):
            rows = slice(a * ch, (a + 1) * ch)
            cols = slice(b * ch, (b + 1) * ch)
            flip = 3 * (2 - a) + (2 - b)
            k1f[rows, cols] = k1_ref[3 * a + b]
            k2f[rows, cols] = k2_ref[3 * a + b]
            k2b[rows, cols] = k2_ref[flip].astype(jnp.float32).T.astype(k2b.dtype)
            k1b[rows, cols] = k1_ref[flip].astype(jnp.float32).T.astype(k1b.dtype)
    scale, shift, top, bottom = level_and_edges(idx_ref, lt_ref)
    phase_one, out_row, g1_row, g2_row, _ = row_ops(width, ch, scale, shift, top, bottom, count)
    for cp in copies:
        cp.wait()

    zero = jnp.zeros((1, ch), jnp.float32)
    lv0, lv1 = lax.fori_loop(
        2, count, lambda r, cr: phase_one(r, x_ref, c_ref, hid_ref, hidt_ref, bf_ref, k1f, k2b, cr), (zero, zero),
        unroll=True,
    )
    lv_ref[0:1, :] = lv0
    lv_ref[1:2, :] = lv1

    def transpose_rows(r, carry):
        xt_ref[r] = x_ref[r].astype(jnp.float32).T.astype(xt_ref.dtype)
        return carry

    lax.fori_loop(2, count + 2, transpose_rows, 0, unroll=True)
    acc1[...] = jnp.zeros_like(acc1)
    acc2[...] = jnp.zeros_like(acc2)

    def middle(i, carry):
        g2_row(i, hidt_ref, c_ref, acc2)
        return carry

    lax.fori_loop(2, count - 2, middle, 0, unroll=True)

    def g1_middle(i, carry):
        g1_row(i, xt_ref, bf_ref, acc1)
        return carry

    lax.fori_loop(1, count - 1, g1_middle, 0, unroll=True)


def edge_kernel(norm, idx_ref, lt_ref, x_hbm, c_hbm, before_hbm, after_hbm, hida_hbm, bfa_hbm, hidta_hbm,
                acc1a_ref, acc2a_ref, lva_ref, k1f, k2b,
                grad_ref, hid_ref, bf_ref,
                x_ref, c_ref, hidt_ref, xt_ref, acc1, acc2, sems):
    count = hid_ref.shape[0] - 2
    width, ch = hid_ref.shape[1], hid_ref.shape[2]
    copies = [
        pltpu.make_async_copy(before_hbm.at[0:2], x_ref.at[0:2], sems.at[0]),
        pltpu.make_async_copy(x_hbm, x_ref.at[2 : count + 2], sems.at[1]),
        pltpu.make_async_copy(after_hbm.at[0:2], x_ref.at[count + 2 : count + 4], sems.at[2]),
        pltpu.make_async_copy(before_hbm.at[2:4], c_ref.at[0:2], sems.at[3]),
        pltpu.make_async_copy(c_hbm, c_ref.at[2 : count + 2], sems.at[4]),
        pltpu.make_async_copy(after_hbm.at[2:4], c_ref.at[count + 2 : count + 4], sems.at[5]),
    ]
    inner = [
        pltpu.make_async_copy(hida_hbm.at[2:count], hid_ref.at[2:count], sems.at[6]),
        pltpu.make_async_copy(bfa_hbm.at[2:count], bf_ref.at[2:count], sems.at[7]),
        pltpu.make_async_copy(hidta_hbm.at[2:count], hidt_ref.at[2:count], sems.at[8]),
    ]
    for cp in copies + inner:
        cp.start()
    scale, shift, top, bottom = level_and_edges(idx_ref, lt_ref)
    phase_one, out_row, g1_row, g2_row, _ = row_ops(width, ch, scale, shift, top, bottom, count)
    for cp in copies:
        cp.wait()

    carry = (lva_ref[0:1, :], lva_ref[1:2, :])
    for r in (0, 1, count, count + 1):
        carry = phase_one(r, x_ref, c_ref, hid_ref, hidt_ref, bf_ref, k1f, k2b, carry)
    lv0, lv1 = carry
    for cp in inner:
        cp.wait()
    for r in (1, 2, 3, count, count + 1, count + 2):
        xt_ref[r] = x_ref[r].astype(jnp.float32).T.astype(xt_ref.dtype)
    for n, i in enumerate((0, 1, count - 2, count - 1)):
        g2_row(i, hidt_ref, c_ref, acc2, n == 0)
    for n, i in enumerate((0, count - 1)):
        g1_row(i, xt_ref, bf_ref, acc1, n == 0)

    for a in range(3):
        for b in range(3):
            t = 3 * a + b
            blk = (slice(a * ch, (a + 1) * ch), slice(b * ch, (b + 1) * ch))
            grad_ref[t * ch : (t + 1) * ch, :] = (acc1a_ref[blk] + acc1[blk]) * norm
            grad_ref[(9 + t) * ch : (10 + t) * ch, :] = (acc2a_ref[blk] + acc2[blk]) * norm
    base = 18 * ch
    tail = grad_ref.shape[0] - base
    grad_ref[base:, :] = jnp.zeros((tail, ch), jnp.float32)
    grad_ref[base : base + 1, :] = lv0 * norm
    grad_ref[base + 1 : base + 2, :] = lv1 * norm


def out_kernel(first_row, aliased, x_hbm, c_hbm, hid_hbm, bf_hbm, k2f, k1b, *refs):
    if aliased:
        refs = refs[2:]
    out_hbm, ig_hbm, x_ref, c_ref, hid_ref, bf_ref, o_ref, g_ref, sems = refs
    n, width, ch = o_ref.shape
    copies = [
        pltpu.make_async_copy(x_hbm.at[first_row : first_row + n], x_ref.at[2 : n + 2], sems.at[0]),
        pltpu.make_async_copy(c_hbm.at[first_row : first_row + n], c_ref.at[2 : n + 2], sems.at[1]),
        pltpu.make_async_copy(hid_hbm.at[first_row : first_row + n + 2], hid_ref, sems.at[2]),
        pltpu.make_async_copy(bf_hbm.at[first_row : first_row + n + 2], bf_ref, sems.at[3]),
    ]
    for cp in copies:
        cp.start()
    one = jnp.ones((1, ch), jnp.float32)
    conv_row = row_ops(width, ch, one, one, True, True, n)[4]
    copies[0].wait()
    copies[2].wait()
    for i in range(n):
        o_ref[i] = (x_ref[i + 2].astype(jnp.float32) + conv_row(hid_ref, i, k2f)).astype(o_ref.dtype)
    store_out = pltpu.make_async_copy(o_ref, out_hbm.at[first_row : first_row + n], sems.at[4])
    store_out.start()
    copies[1].wait()
    copies[3].wait()
    for i in range(n):
        g_ref[i] = (c_ref[i + 2].astype(jnp.float32) + conv_row(bf_ref, i, k1b)).astype(g_ref.dtype)
    store_ig = pltpu.make_async_copy(g_ref, ig_hbm.at[first_row : first_row + n], sems.at[5])
    store_ig.start()
    store_out.wait()
    store_ig.wait()


def section(norm, packed_rows, level_index, level_table, inputs, cotangent, before_fn, k1, k2):
    count, width, ch = inputs.shape
    vmem = pltpu.MemorySpace.VMEM if hasattr(pltpu, "MemorySpace") else pltpu.VMEM
    spec = pl.BlockSpec(memory_space=vmem)
    anywhere = pl.BlockSpec(memory_space=pl.ANY)
    smem = pl.BlockSpec(memory_space=pltpu.SMEM)
    big = 3 * ch
    unit = width * big * big * 2
    field = jax.ShapeDtypeStruct((count, width, ch), jnp.bfloat16)
    frame = jax.ShapeDtypeStruct((count + 2, width, ch), jnp.bfloat16)
    frame_t = jax.ShapeDtypeStruct((count + 2, ch, width), jnp.bfloat16)
    square = jax.ShapeDtypeStruct((big, big), jnp.float32)
    params = pltpu.CompilerParams(vmem_limit_bytes=60 * 1024 * 1024)
    matrix = jax.ShapeDtypeStruct((big, big), jnp.bfloat16)
    hid, bf, hidt, acc1, acc2, lv, k1f, k2f, k2b, k1b = pl.pallas_call(
        interior_kernel,
        out_shape=(frame, frame, frame_t, square, square,
                   jax.ShapeDtypeStruct((2, ch), jnp.float32), matrix, matrix, matrix, matrix),
        in_specs=[smem, spec, anywhere, anywhere, spec, spec],
        out_specs=(spec,) * 10,
        scratch_shapes=[
            pltpu.VMEM((count + 4, width, ch), jnp.bfloat16),
            pltpu.VMEM((count + 4, width, ch), jnp.bfloat16),
            pltpu.VMEM((count + 4, ch, width), jnp.bfloat16),
            pltpu.SemaphoreType.DMA((2,)),
        ],
        compiler_params=params,
        cost_estimate=pl.CostEstimate(
            flops=(4 * count - 6) * unit, transcendentals=count * width * ch, bytes_accessed=8 * count * width * ch
        ),
    )(level_index, level_table, inputs, cotangent, k1, k2)
    before, after = before_fn()
    packed, hid, bf = pl.pallas_call(
        functools.partial(edge_kernel, norm),
        out_shape=(jax.ShapeDtypeStruct((packed_rows, ch), jnp.float32), frame, frame),
        in_specs=[smem, spec] + [anywhere] * 7 + [spec] * 5,
        out_specs=(spec, spec, spec),
        scratch_shapes=[
            pltpu.VMEM((count + 4, width, ch), jnp.bfloat16),
            pltpu.VMEM((count + 4, width, ch), jnp.bfloat16),
            pltpu.VMEM((count + 2, ch, width), jnp.bfloat16),
            pltpu.VMEM((count + 4, ch, width), jnp.bfloat16),
            pltpu.VMEM((big, big), jnp.float32),
            pltpu.VMEM((big, big), jnp.float32),
            pltpu.SemaphoreType.DMA((9,)),
        ],
        compiler_params=params,
        cost_estimate=pl.CostEstimate(
            flops=14 * unit, transcendentals=4 * width * ch, bytes_accessed=10 * count * width * ch
        ),
    )(level_index, level_table, inputs, cotangent, before, after, hid, bf, hidt, acc1, acc2, lv, k1f, k2b)
    step = count // 2 if count % 2 == 0 else count
    whole = jax.ShapeDtypeStruct((count, width, ch), jnp.bfloat16)
    chunks = []
    for first_row in range(0, count, step):
        aliased = first_row > 0
        chunks.append(functools.partial(
            pl.pallas_call(
                functools.partial(out_kernel, first_row, aliased),
                out_shape=(whole, whole),
                in_specs=[anywhere] * 4 + [spec] * 2 + [anywhere] * (2 if aliased else 0),
                out_specs=(anywhere, anywhere),
                scratch_shapes=[
                    pltpu.VMEM((step + 2, width, ch), jnp.bfloat16),
                    pltpu.VMEM((step + 2, width, ch), jnp.bfloat16),
                    pltpu.VMEM((step + 2, width, ch), jnp.bfloat16),
                    pltpu.VMEM((step + 2, width, ch), jnp.bfloat16),
                    pltpu.VMEM((step, width, ch), jnp.bfloat16),
                    pltpu.VMEM((step, width, ch), jnp.bfloat16),
                    pltpu.SemaphoreType.DMA((6,)),
                ],
                input_output_aliases={6: 0, 7: 1} if aliased else {},
                compiler_params=params,
                cost_estimate=pl.CostEstimate(
                    flops=2 * step * unit, transcendentals=0, bytes_accessed=8 * step * width * ch
                ),
            ),
            inputs, cotangent, hid, bf, k2f, k1b,
        ))
    return chunks, packed


def butterfly_sum(block, riders):
    n = lax.axis_size("rows")
    me = lax.axis_index("rows")
    bits = []
    k = 1
    while k < n:
        bits.append(k)
        k *= 2
    other = list(bits)
    if len(bits) > 2:
        other[1], other[2] = bits[2], bits[1]
    orders = list(zip(bits, other))
    even = me % 2 == 0

    def step_of(k0, k1):
        perm = [(i, i ^ (k0 if i % 2 == 0 else k1)) for i in range(n)]
        low = jnp.where(even, (me // k0) % 2, (me // k1) % 2) == 0
        return perm, low

    state = ()
    count = 0
    piece = block
    for k0, k1 in orders:
        perm, low = step_of(k0, k1)
        half = piece.shape[0] // 2
        lo, hi = piece[:half], piece[half:]
        keep = jnp.where(low, lo, hi)
        send = jnp.where(low, hi, lo)
        got = lax.ppermute(send, "rows", perm)
        if count in riders:
            got, state = lax.optimization_barrier((got, riders[count](*state)))
        count += 1
        piece = keep + got
    for k0, k1 in reversed(orders):
        perm, low = step_of(k0, k1)
        got = lax.ppermute(piece, "rows", perm)
        if count in riders:
            got, state = lax.optimization_barrier((got, riders[count](*state)))
        count += 1
        piece = jnp.where(low, jnp.concatenate([piece, got]), jnp.concatenate([got, piece]))
    return piece, state


def local(inputs, cotangent, first_kernel, second_kernel, level_table, level_index):
    count = inputs.shape[0]
    width = inputs.shape[1]
    ch = inputs.shape[2]
    size = lax.axis_size("rows")
    total_rows = count * size
    norm = 1.0 / math.sqrt(total_rows * width)

    up = [(i, i + 1) for i in range(size - 1)]
    down = [(i + 1, i) for i in range(size - 1)]
    before = lax.ppermute(jnp.concatenate([inputs[-2:], cotangent[-2:]]), "rows", up)
    after = lax.ppermute(jnp.concatenate([inputs[:2], cotangent[:2]]), "rows", down)
    halo = lambda: (before, after)

    used = 18 * ch + 2
    packed_rows = used + (-used % size)
    chunks, packed = section(
        norm, packed_rows, level_index, level_table, inputs, cotangent, halo,
        first_kernel, second_kernel,
    )
    steps = 2 * (size.bit_length() - 1)
    places = [1, steps - 2] if len(chunks) == 2 and steps >= 4 else list(range(len(chunks)))
    total, (outputs, input_grad) = butterfly_sum(packed, dict(zip(places, chunks)))
    first_sum = total[: 9 * ch].reshape(9, ch, ch)
    second_sum = total[9 * ch : 18 * ch].reshape(9, ch, ch)
    level_sum = total[18 * ch : 18 * ch + 2]
    return (outputs, input_grad, first_sum, second_sum, level_sum)


def solution(mesh):
    return jax.shard_map(
        local,
        mesh=mesh,
        in_specs=(
            P(("groups", "rows"), None, None),
            P(("groups", "rows"), None, None),
            P(),
            P(),
            P(),
            P("groups"),
        ),
        out_specs=(
            P(("groups", "rows"), None, None),
            P(("groups", "rows"), None, None),
            P("groups", None, None),
            P("groups", None, None),
            P("groups", None),
        ),
        check_vma=False,
    )
```

```python
import functools
import math

import jax
import jax.numpy as jnp
from jax import lax
from jax.experimental import pallas as pl
from jax.experimental.pallas import tpu as pltpu
from jax.sharding import PartitionSpec as P


def row_ops(width, ch, scale, shift, top, bottom, count):
    col = lax.broadcasted_iota(jnp.int32, (width, ch), 0)
    not_first = col > 0
    not_last = col < width - 1

    def combine(y):
        left = pltpu.roll(y[:, 0:ch], 1, 0)
        right = pltpu.roll(y[:, 2 * ch:3 * ch], width - 1, 0)
        return y[:, ch:2 * ch] + jnp.where(not_first, left, 0.0) + jnp.where(not_last, right, 0.0)

    def conv_row(ref, r, matrix_ref):
        rows = jnp.concatenate([ref[r], ref[r + 1], ref[r + 2]], axis=1)
        y = jnp.dot(rows, matrix_ref[...], preferred_element_type=jnp.float32)
        return combine(y)

    def shifted(g):
        g32 = g.astype(jnp.float32)
        g0 = jnp.where(not_last, pltpu.roll(g32, width - 1, 0), 0.0)
        g2 = jnp.where(not_first, pltpu.roll(g32, 1, 0), 0.0)
        return jnp.concatenate([g0.astype(g.dtype), g, g2.astype(g.dtype)], axis=1)

    def phase_one(r, x_ref, c_ref, hid_ref, hidt_ref, bf_ref, k1f_ref, k2b_ref, carry):
        lv0, lv1 = carry
        valid = jnp.logical_and(jnp.logical_or(r > 0, top), jnp.logical_or(r < count + 1, bottom))
        first = conv_row(x_ref, r, k1f_ref)
        mixed = first * scale + shift
        sig = 0.5 + 0.5 * jnp.tanh(0.5 * mixed)
        hidden = jnp.where(valid, mixed * sig, 0.0)
        hid_ref[r] = hidden.astype(hid_ref.dtype)
        hidt_ref[r] = hidden.T.astype(hidt_ref.dtype)
        back_hidden = conv_row(c_ref, r, k2b_ref)
        back_mixed = back_hidden * (sig * (1.0 + mixed * (1.0 - sig)))
        bf_ref[r] = jnp.where(valid, back_mixed * scale, 0.0).astype(bf_ref.dtype)
        own = jnp.logical_and(r >= 1, r <= count)
        lv0 = lv0 + jnp.where(own, jnp.sum(back_mixed * first, axis=0, keepdims=True), 0.0)
        lv1 = lv1 + jnp.where(own, jnp.sum(back_mixed, axis=0, keepdims=True), 0.0)
        return lv0, lv1

    def out_row(i, x_ref, c_ref, hid_ref, bf_ref, k2f_ref, k1b_ref, out_ref, ig_ref):
        out_ref[i] = (x_ref[i + 2].astype(jnp.float32) + conv_row(hid_ref, i, k2f_ref)).astype(out_ref.dtype)
        ig_ref[i] = (c_ref[i + 2].astype(jnp.float32) + conv_row(bf_ref, i, k1b_ref)).astype(ig_ref.dtype)

    def g1_row(i, xt_ref, bf_ref, acc1):
        xs = jnp.concatenate([xt_ref[i + 1], xt_ref[i + 2], xt_ref[i + 3]], axis=0)
        acc1[...] += jnp.dot(xs, shifted(bf_ref[i + 1]), preferred_element_type=jnp.float32)

    def g2_row(i, hidt_ref, c_ref, acc2):
        hs = jnp.concatenate([hidt_ref[i], hidt_ref[i + 1], hidt_ref[i + 2]], axis=0)
        acc2[...] += jnp.dot(hs, shifted(c_ref[i + 2]), preferred_element_type=jnp.float32)

    return phase_one, out_row, g1_row, g2_row, conv_row


def level_and_edges(idx_ref, lt_ref):
    me = lax.axis_index("rows")
    size = lax.axis_size("rows")
    level = lt_ref[idx_ref[0]]
    return level[0:1, :] + 1.0, level[1:2, :], me > 0, me < size - 1


def interior_kernel(idx_ref, lt_ref, x_hbm, c_hbm, k1_ref, k2_ref,
                    hid_ref, bf_ref, hidt_ref, acc1, acc2, lv_ref, k1f, k2f, k2b, k1b,
                    x_ref, c_ref, xt_ref, sems):
    count = hid_ref.shape[0] - 2
    width, ch = hid_ref.shape[1], hid_ref.shape[2]
    copies = [
        pltpu.make_async_copy(x_hbm, x_ref.at[2 : count + 2], sems.at[0]),
        pltpu.make_async_copy(c_hbm, c_ref.at[2 : count + 2], sems.at[1]),
    ]
    for cp in copies:
        cp.start()
    for a in range(3):
        for b in range(3):
            rows = slice(a * ch, (a + 1) * ch)
            cols = slice(b * ch, (b + 1) * ch)
            flip = 3 * (2 - a) + (2 - b)
            k1f[rows, cols] = k1_ref[3 * a + b]
            k2f[rows, cols] = k2_ref[3 * a + b]
            k2b[rows, cols] = k2_ref[flip].astype(jnp.float32).T.astype(k2b.dtype)
            k1b[rows, cols] = k1_ref[flip].astype(jnp.float32).T.astype(k1b.dtype)
    scale, shift, top, bottom = level_and_edges(idx_ref, lt_ref)
    phase_one, out_row, g1_row, g2_row, _ = row_ops(width, ch, scale, shift, top, bottom, count)
    for cp in copies:
        cp.wait()

    zero = jnp.zeros((1, ch), jnp.float32)
    lv0, lv1 = lax.fori_loop(
        2, count, lambda r, cr: phase_one(r, x_ref, c_ref, hid_ref, hidt_ref, bf_ref, k1f, k2b, cr), (zero, zero),
        unroll=True,
    )
    lv_ref[0:1, :] = lv0
    lv_ref[1:2, :] = lv1

    def transpose_rows(r, carry):
        xt_ref[r] = x_ref[r].astype(jnp.float32).T.astype(xt_ref.dtype)
        return carry

    lax.fori_loop(2, count + 2, transpose_rows, 0, unroll=True)
    acc1[...] = jnp.zeros_like(acc1)
    acc2[...] = jnp.zeros_like(acc2)

    def middle(i, carry):
        g2_row(i, hidt_ref, c_ref, acc2)
        return carry

    lax.fori_loop(2, count - 2, middle, 0, unroll=True)

    def g1_middle(i, carry):
        g1_row(i, xt_ref, bf_ref, acc1)
        return carry

    lax.fori_loop(1, count - 1, g1_middle, 0, unroll=True)


def edge_kernel(norm, idx_ref, lt_ref, x_hbm, c_hbm, before_hbm, after_hbm, hida_hbm, bfa_hbm, hidta_hbm,
                acc1a_ref, acc2a_ref, lva_ref, k1f, k2b,
                keep_ref, send_ref, hid_ref, bf_ref,
                x_ref, c_ref, hidt_ref, xt_ref, acc1, acc2, sems, grad_ref):
    count = hid_ref.shape[0] - 2
    width, ch = hid_ref.shape[1], hid_ref.shape[2]
    copies = [
        pltpu.make_async_copy(before_hbm.at[0:2], x_ref.at[0:2], sems.at[0]),
        pltpu.make_async_copy(x_hbm, x_ref.at[2 : count + 2], sems.at[1]),
        pltpu.make_async_copy(after_hbm.at[0:2], x_ref.at[count + 2 : count + 4], sems.at[2]),
        pltpu.make_async_copy(before_hbm.at[2:4], c_ref.at[0:2], sems.at[3]),
        pltpu.make_async_copy(c_hbm, c_ref.at[2 : count + 2], sems.at[4]),
        pltpu.make_async_copy(after_hbm.at[2:4], c_ref.at[count + 2 : count + 4], sems.at[5]),
    ]
    inner = [
        pltpu.make_async_copy(hida_hbm.at[2:count], hid_ref.at[2:count], sems.at[6]),
        pltpu.make_async_copy(bfa_hbm.at[2:count], bf_ref.at[2:count], sems.at[7]),
        pltpu.make_async_copy(hidta_hbm.at[2:count], hidt_ref.at[2:count], sems.at[8]),
    ]
    for cp in copies + inner:
        cp.start()
    scale, shift, top, bottom = level_and_edges(idx_ref, lt_ref)
    phase_one, out_row, g1_row, g2_row, _ = row_ops(width, ch, scale, shift, top, bottom, count)
    acc1[...] = acc1a_ref[...]
    acc2[...] = acc2a_ref[...]
    for cp in copies:
        cp.wait()

    carry = (lva_ref[0:1, :], lva_ref[1:2, :])
    for r in (0, 1, count, count + 1):
        carry = phase_one(r, x_ref, c_ref, hid_ref, hidt_ref, bf_ref, k1f, k2b, carry)
    lv0, lv1 = carry
    for cp in inner:
        cp.wait()
    for r in (1, 2, 3, count, count + 1, count + 2):
        xt_ref[r] = x_ref[r].astype(jnp.float32).T.astype(xt_ref.dtype)
    for i in (0, 1, count - 2, count - 1):
        g2_row(i, hidt_ref, c_ref, acc2)
    for i in (0, count - 1):
        g1_row(i, xt_ref, bf_ref, acc1)

    for a in range(3):
        for b in range(3):
            t = 3 * a + b
            blk = (slice(a * ch, (a + 1) * ch), slice(b * ch, (b + 1) * ch))
            grad_ref[t * ch : (t + 1) * ch, :] = acc1[blk] * norm
            grad_ref[(9 + t) * ch : (10 + t) * ch, :] = acc2[blk] * norm
    base = 18 * ch
    tail = grad_ref.shape[0] - base
    grad_ref[base:, :] = jnp.zeros((tail, ch), jnp.float32)
    grad_ref[base : base + 1, :] = lv0 * norm
    grad_ref[base + 1 : base + 2, :] = lv1 * norm
    half = keep_ref.shape[0]
    even = lax.axis_index("rows") % 2 == 0
    lo, hi = grad_ref[0:half, :], grad_ref[half:, :]
    keep_ref[...] = jnp.where(even, lo, hi)
    send_ref[...] = jnp.where(even, hi, lo)


def out_kernel(first_row, aliased, x_hbm, c_hbm, hid_hbm, bf_hbm, k2f, k1b, *refs):
    if aliased:
        refs = refs[2:]
    out_hbm, ig_hbm, x_ref, c_ref, hid_ref, bf_ref, o_ref, g_ref, sems = refs
    n, width, ch = o_ref.shape
    copies = [
        pltpu.make_async_copy(x_hbm.at[first_row : first_row + n], x_ref.at[2 : n + 2], sems.at[0]),
        pltpu.make_async_copy(c_hbm.at[first_row : first_row + n], c_ref.at[2 : n + 2], sems.at[1]),
        pltpu.make_async_copy(hid_hbm.at[first_row : first_row + n + 2], hid_ref, sems.at[2]),
        pltpu.make_async_copy(bf_hbm.at[first_row : first_row + n + 2], bf_ref, sems.at[3]),
    ]
    for cp in copies:
        cp.start()
    one = jnp.ones((1, ch), jnp.float32)
    conv_row = row_ops(width, ch, one, one, True, True, n)[4]
    copies[0].wait()
    copies[2].wait()
    for i in range(n):
        o_ref[i] = (x_ref[i + 2].astype(jnp.float32) + conv_row(hid_ref, i, k2f)).astype(o_ref.dtype)
    store_out = pltpu.make_async_copy(o_ref, out_hbm.at[first_row : first_row + n], sems.at[4])
    store_out.start()
    copies[1].wait()
    copies[3].wait()
    for i in range(n):
        g_ref[i] = (c_ref[i + 2].astype(jnp.float32) + conv_row(bf_ref, i, k1b)).astype(g_ref.dtype)
    store_ig = pltpu.make_async_copy(g_ref, ig_hbm.at[first_row : first_row + n], sems.at[5])
    store_ig.start()
    store_out.wait()
    store_ig.wait()


def section(norm, packed_rows, level_index, level_table, inputs, cotangent, before_fn, k1, k2):
    count, width, ch = inputs.shape
    vmem = pltpu.MemorySpace.VMEM if hasattr(pltpu, "MemorySpace") else pltpu.VMEM
    spec = pl.BlockSpec(memory_space=vmem)
    anywhere = pl.BlockSpec(memory_space=pl.ANY)
    smem = pl.BlockSpec(memory_space=pltpu.SMEM)
    big = 3 * ch
    unit = width * big * big * 2
    field = jax.ShapeDtypeStruct((count, width, ch), jnp.bfloat16)
    frame = jax.ShapeDtypeStruct((count + 2, width, ch), jnp.bfloat16)
    frame_t = jax.ShapeDtypeStruct((count + 2, ch, width), jnp.bfloat16)
    square = jax.ShapeDtypeStruct((big, big), jnp.float32)
    params = pltpu.CompilerParams(vmem_limit_bytes=60 * 1024 * 1024)
    matrix = jax.ShapeDtypeStruct((big, big), jnp.bfloat16)
    hid, bf, hidt, acc1, acc2, lv, k1f, k2f, k2b, k1b = pl.pallas_call(
        interior_kernel,
        out_shape=(frame, frame, frame_t, square, square,
                   jax.ShapeDtypeStruct((2, ch), jnp.float32), matrix, matrix, matrix, matrix),
        in_specs=[smem, spec, anywhere, anywhere, spec, spec],
        out_specs=(spec,) * 10,
        scratch_shapes=[
            pltpu.VMEM((count + 4, width, ch), jnp.bfloat16),
            pltpu.VMEM((count + 4, width, ch), jnp.bfloat16),
            pltpu.VMEM((count + 4, ch, width), jnp.bfloat16),
            pltpu.SemaphoreType.DMA((2,)),
        ],
        compiler_params=params,
        cost_estimate=pl.CostEstimate(
            flops=(4 * count - 6) * unit, transcendentals=count * width * ch, bytes_accessed=8 * count * width * ch
        ),
    )(level_index, level_table, inputs, cotangent, k1, k2)
    before, after = before_fn()
    halfrows = jax.ShapeDtypeStruct((packed_rows // 2, ch), jnp.float32)
    keep, send, hid, bf = pl.pallas_call(
        functools.partial(edge_kernel, norm),
        out_shape=(halfrows, halfrows, frame, frame),
        in_specs=[smem, spec] + [anywhere] * 7 + [spec] * 5,
        out_specs=(spec, spec, spec, spec),
        scratch_shapes=[
            pltpu.VMEM((count + 4, width, ch), jnp.bfloat16),
            pltpu.VMEM((count + 4, width, ch), jnp.bfloat16),
            pltpu.VMEM((count + 2, ch, width), jnp.bfloat16),
            pltpu.VMEM((count + 4, ch, width), jnp.bfloat16),
            pltpu.VMEM((big, big), jnp.float32),
            pltpu.VMEM((big, big), jnp.float32),
            pltpu.SemaphoreType.DMA((9,)),
            pltpu.VMEM((packed_rows, ch), jnp.float32),
        ],
        compiler_params=params,
        cost_estimate=pl.CostEstimate(
            flops=14 * unit, transcendentals=4 * width * ch, bytes_accessed=10 * count * width * ch
        ),
    )(level_index, level_table, inputs, cotangent, before, after, hid, bf, hidt, acc1, acc2, lv, k1f, k2b)
    step = count // 2 if count % 2 == 0 else count
    whole = jax.ShapeDtypeStruct((count, width, ch), jnp.bfloat16)
    chunks = []
    for first_row in range(0, count, step):
        aliased = first_row > 0
        chunks.append(functools.partial(
            pl.pallas_call(
                functools.partial(out_kernel, first_row, aliased),
                out_shape=(whole, whole),
                in_specs=[anywhere] * 4 + [spec] * 2 + [anywhere] * (2 if aliased else 0),
                out_specs=(anywhere, anywhere),
                scratch_shapes=[
                    pltpu.VMEM((step + 2, width, ch), jnp.bfloat16),
                    pltpu.VMEM((step + 2, width, ch), jnp.bfloat16),
                    pltpu.VMEM((step + 2, width, ch), jnp.bfloat16),
                    pltpu.VMEM((step + 2, width, ch), jnp.bfloat16),
                    pltpu.VMEM((step, width, ch), jnp.bfloat16),
                    pltpu.VMEM((step, width, ch), jnp.bfloat16),
                    pltpu.SemaphoreType.DMA((6,)),
                ],
                input_output_aliases={6: 0, 7: 1} if aliased else {},
                compiler_params=params,
                cost_estimate=pl.CostEstimate(
                    flops=2 * step * unit, transcendentals=0, bytes_accessed=8 * step * width * ch
                ),
            ),
            inputs, cotangent, hid, bf, k2f, k1b,
        ))
    return chunks, (keep, send)


def butterfly_sum(first_step, riders):
    n = lax.axis_size("rows")
    me = lax.axis_index("rows")
    bits = []
    k = 1
    while k < n:
        bits.append(k)
        k *= 2
    other = list(bits)
    if len(bits) > 2:
        other[1], other[2] = bits[2], bits[1]
    orders = list(zip(bits, other))
    even = me % 2 == 0

    def step_of(k0, k1):
        perm = [(i, i ^ (k0 if i % 2 == 0 else k1)) for i in range(n)]
        low = jnp.where(even, (me // k0) % 2, (me // k1) % 2) == 0
        return perm, low

    state = ()
    count = 0
    for k0, k1 in orders:
        perm, low = step_of(k0, k1)
        if count == 0:
            keep, send = first_step
        else:
            half = piece.shape[0] // 2
            lo, hi = piece[:half], piece[half:]
            keep = jnp.where(low, lo, hi)
            send = jnp.where(low, hi, lo)
        got = lax.ppermute(send, "rows", perm)
        if count in riders:
            got, state = lax.optimization_barrier((got, riders[count](*state)))
        count += 1
        piece = keep + got
    for k0, k1 in reversed(orders):
        perm, low = step_of(k0, k1)
        got = lax.ppermute(piece, "rows", perm)
        if count in riders:
            got, state = lax.optimization_barrier((got, riders[count](*state)))
        count += 1
        piece = jnp.where(low, jnp.concatenate([piece, got]), jnp.concatenate([got, piece]))
    return piece, state


def local(inputs, cotangent, first_kernel, second_kernel, level_table, level_index):
    count = inputs.shape[0]
    width = inputs.shape[1]
    ch = inputs.shape[2]
    size = lax.axis_size("rows")
    total_rows = count * size
    norm = 1.0 / math.sqrt(total_rows * width)

    up = [(i, i + 1) for i in range(size - 1)]
    down = [(i + 1, i) for i in range(size - 1)]
    before = lax.ppermute(jnp.concatenate([inputs[-2:], cotangent[-2:]]), "rows", up)
    after = lax.ppermute(jnp.concatenate([inputs[:2], cotangent[:2]]), "rows", down)
    halo = lambda: (before, after)

    used = 18 * ch + 2
    packed_rows = used + (-used % size)
    chunks, packed = section(
        norm, packed_rows, level_index, level_table, inputs, cotangent, halo,
        first_kernel, second_kernel,
    )
    steps = 2 * (size.bit_length() - 1)
    places = [1, steps - 2] if len(chunks) == 2 and steps >= 4 else list(range(len(chunks)))
    total, (outputs, input_grad) = butterfly_sum(packed, dict(zip(places, chunks)))
    first_sum = total[: 9 * ch].reshape(9, ch, ch)
    second_sum = total[9 * ch : 18 * ch].reshape(9, ch, ch)
    level_sum = total[18 * ch : 18 * ch + 2]
    return (outputs, input_grad, first_sum, second_sum, level_sum)


def solution(mesh):
    return jax.shard_map(
        local,
        mesh=mesh,
        in_specs=(
            P(("groups", "rows"), None, None),
            P(("groups", "rows"), None, None),
            P(),
            P(),
            P(),
            P("groups"),
        ),
        out_specs=(
            P(("groups", "rows"), None, None),
            P(("groups", "rows"), None, None),
            P("groups", None, None),
            P("groups", None, None),
            P("groups", None),
        ),
        check_vma=False,
    )
```

```python
import functools
import math

import jax
import jax.numpy as jnp
from jax import lax
from jax.experimental import pallas as pl
from jax.experimental.pallas import tpu as pltpu
from jax.sharding import PartitionSpec as P


def row_ops(width, ch, scale, shift, top, bottom, count):
    col = lax.broadcasted_iota(jnp.int32, (width, ch), 0)
    not_first = col > 0
    not_last = col < width - 1

    def combine(y):
        left = pltpu.roll(y[:, 0:ch], 1, 0)
        right = pltpu.roll(y[:, 2 * ch:3 * ch], width - 1, 0)
        return y[:, ch:2 * ch] + jnp.where(not_first, left, 0.0) + jnp.where(not_last, right, 0.0)

    def conv_row(ref, r, matrix_ref):
        rows = jnp.concatenate([ref[r], ref[r + 1], ref[r + 2]], axis=1)
        y = jnp.dot(rows, matrix_ref[...], preferred_element_type=jnp.float32)
        return combine(y)

    def shifted(g):
        g32 = g.astype(jnp.float32)
        g0 = jnp.where(not_last, pltpu.roll(g32, width - 1, 0), 0.0)
        g2 = jnp.where(not_first, pltpu.roll(g32, 1, 0), 0.0)
        return jnp.concatenate([g0.astype(g.dtype), g, g2.astype(g.dtype)], axis=1)

    def phase_one(r, x_ref, c_ref, hid_ref, hidt_ref, bf_ref, k1f_ref, k2b_ref, carry):
        lv0, lv1 = carry
        valid = jnp.logical_and(jnp.logical_or(r > 0, top), jnp.logical_or(r < count + 1, bottom))
        first = conv_row(x_ref, r, k1f_ref)
        mixed = first * scale + shift
        sig = 0.5 + 0.5 * jnp.tanh(0.5 * mixed)
        hidden = jnp.where(valid, mixed * sig, 0.0)
        hid_ref[r] = hidden.astype(hid_ref.dtype)
        hidt_ref[r] = hidden.T.astype(hidt_ref.dtype)
        back_hidden = conv_row(c_ref, r, k2b_ref)
        back_mixed = back_hidden * (sig * (1.0 + mixed * (1.0 - sig)))
        bf_ref[r] = jnp.where(valid, back_mixed * scale, 0.0).astype(bf_ref.dtype)
        own = jnp.logical_and(r >= 1, r <= count)
        lv0 = lv0 + jnp.where(own, jnp.sum(back_mixed * first, axis=0, keepdims=True), 0.0)
        lv1 = lv1 + jnp.where(own, jnp.sum(back_mixed, axis=0, keepdims=True), 0.0)
        return lv0, lv1

    def out_row(i, x_ref, c_ref, hid_ref, bf_ref, k2f_ref, k1b_ref, out_ref, ig_ref):
        out_ref[i] = (x_ref[i + 2].astype(jnp.float32) + conv_row(hid_ref, i, k2f_ref)).astype(out_ref.dtype)
        ig_ref[i] = (c_ref[i + 2].astype(jnp.float32) + conv_row(bf_ref, i, k1b_ref)).astype(ig_ref.dtype)

    def g1_row(i, xt_ref, bf_ref, acc1):
        xs = jnp.concatenate([xt_ref[i + 1], xt_ref[i + 2], xt_ref[i + 3]], axis=0)
        acc1[...] += jnp.dot(xs, shifted(bf_ref[i + 1]), preferred_element_type=jnp.float32)

    def g2_row(i, hidt_ref, c_ref, acc2):
        hs = jnp.concatenate([hidt_ref[i], hidt_ref[i + 1], hidt_ref[i + 2]], axis=0)
        acc2[...] += jnp.dot(hs, shifted(c_ref[i + 2]), preferred_element_type=jnp.float32)

    return phase_one, out_row, g1_row, g2_row, conv_row


def level_and_edges(idx_ref, lt_ref):
    me = lax.axis_index("rows")
    size = lax.axis_size("rows")
    level = lt_ref[idx_ref[0]]
    return level[0:1, :] + 1.0, level[1:2, :], me > 0, me < size - 1


def interior_kernel(idx_ref, lt_ref, x_hbm, c_hbm, k1_ref, k2_ref,
                    hid_ref, bf_ref, hidt_ref, acc1, acc2, lv_ref, k1f, k2f, k2b, k1b, xt_ref,
                    x_ref, c_ref, sems):
    count = hid_ref.shape[0] - 2
    width, ch = hid_ref.shape[1], hid_ref.shape[2]
    copies = [
        pltpu.make_async_copy(x_hbm, x_ref.at[2 : count + 2], sems.at[0]),
        pltpu.make_async_copy(c_hbm, c_ref.at[2 : count + 2], sems.at[1]),
    ]
    for cp in copies:
        cp.start()
    for a in range(3):
        for b in range(3):
            rows = slice(a * ch, (a + 1) * ch)
            cols = slice(b * ch, (b + 1) * ch)
            flip = 3 * (2 - a) + (2 - b)
            k1f[rows, cols] = k1_ref[3 * a + b]
            k2f[rows, cols] = k2_ref[3 * a + b]
            k2b[rows, cols] = k2_ref[flip].astype(jnp.float32).T.astype(k2b.dtype)
            k1b[rows, cols] = k1_ref[flip].astype(jnp.float32).T.astype(k1b.dtype)
    scale, shift, top, bottom = level_and_edges(idx_ref, lt_ref)
    phase_one, out_row, g1_row, g2_row, _ = row_ops(width, ch, scale, shift, top, bottom, count)
    for cp in copies:
        cp.wait()

    zero = jnp.zeros((1, ch), jnp.float32)
    lv0, lv1 = lax.fori_loop(
        2, count, lambda r, cr: phase_one(r, x_ref, c_ref, hid_ref, hidt_ref, bf_ref, k1f, k2b, cr), (zero, zero),
        unroll=True,
    )
    lv_ref[0:1, :] = lv0
    lv_ref[1:2, :] = lv1

    def transpose_rows(r, carry):
        xt_ref[r] = x_ref[r].astype(jnp.float32).T.astype(xt_ref.dtype)
        return carry

    lax.fori_loop(2, count + 2, transpose_rows, 0, unroll=True)
    acc1[...] = jnp.zeros_like(acc1)
    acc2[...] = jnp.zeros_like(acc2)

    def middle(i, carry):
        g2_row(i, hidt_ref, c_ref, acc2)
        return carry

    lax.fori_loop(2, count - 2, middle, 0, unroll=True)

    def g1_middle(i, carry):
        g1_row(i, xt_ref, bf_ref, acc1)
        return carry

    lax.fori_loop(1, count - 1, g1_middle, 0, unroll=True)


def edge_kernel(norm, idx_ref, lt_ref, x_hbm, c_hbm, before_hbm, after_hbm, hida_hbm, bfa_hbm, hidta_hbm,
                xta_hbm, acc1a_ref, acc2a_ref, lva_ref, k1f, k2b,
                grad_ref, hid_ref, bf_ref,
                x_ref, c_ref, hidt_ref, xt_ref, acc1, acc2, sems, xt_sem):
    count = hid_ref.shape[0] - 2
    width, ch = hid_ref.shape[1], hid_ref.shape[2]
    copies = [
        pltpu.make_async_copy(before_hbm.at[0:2], x_ref.at[0:2], sems.at[0]),
        pltpu.make_async_copy(x_hbm, x_ref.at[2 : count + 2], sems.at[1]),
        pltpu.make_async_copy(after_hbm.at[0:2], x_ref.at[count + 2 : count + 4], sems.at[2]),
        pltpu.make_async_copy(before_hbm.at[2:4], c_ref.at[0:2], sems.at[3]),
        pltpu.make_async_copy(c_hbm, c_ref.at[2 : count + 2], sems.at[4]),
        pltpu.make_async_copy(after_hbm.at[2:4], c_ref.at[count + 2 : count + 4], sems.at[5]),
    ]
    inner = [
        pltpu.make_async_copy(hida_hbm.at[2:count], hid_ref.at[2:count], sems.at[6]),
        pltpu.make_async_copy(bfa_hbm.at[2:count], bf_ref.at[2:count], sems.at[7]),
        pltpu.make_async_copy(hidta_hbm.at[2:count], hidt_ref.at[2:count], sems.at[8]),
    ]
    xt_copy = pltpu.make_async_copy(xta_hbm.at[2 : count + 2], xt_ref.at[2 : count + 2], xt_sem.at[0])
    for cp in copies + inner + [xt_copy]:
        cp.start()
    scale, shift, top, bottom = level_and_edges(idx_ref, lt_ref)
    phase_one, out_row, g1_row, g2_row, _ = row_ops(width, ch, scale, shift, top, bottom, count)
    acc1[...] = acc1a_ref[...]
    acc2[...] = acc2a_ref[...]
    for cp in copies:
        cp.wait()

    carry = (lva_ref[0:1, :], lva_ref[1:2, :])
    for r in (0, 1, count, count + 1):
        carry = phase_one(r, x_ref, c_ref, hid_ref, hidt_ref, bf_ref, k1f, k2b, carry)
    lv0, lv1 = carry
    for cp in inner:
        cp.wait()
    for r in (1, count + 2):
        xt_ref[r] = x_ref[r].astype(jnp.float32).T.astype(xt_ref.dtype)
    xt_copy.wait()
    for i in (0, 1, count - 2, count - 1):
        g2_row(i, hidt_ref, c_ref, acc2)
    for i in (0, count - 1):
        g1_row(i, xt_ref, bf_ref, acc1)

    for a in range(3):
        for b in range(3):
            t = 3 * a + b
            blk = (slice(a * ch, (a + 1) * ch), slice(b * ch, (b + 1) * ch))
            grad_ref[t * ch : (t + 1) * ch, :] = acc1[blk] * norm
            grad_ref[(9 + t) * ch : (10 + t) * ch, :] = acc2[blk] * norm
    base = 18 * ch
    tail = grad_ref.shape[0] - base
    grad_ref[base:, :] = jnp.zeros((tail, ch), jnp.float32)
    grad_ref[base : base + 1, :] = lv0 * norm
    grad_ref[base + 1 : base + 2, :] = lv1 * norm


def out_kernel(first_row, aliased, x_hbm, c_hbm, hid_hbm, bf_hbm, k2f, k1b, *refs):
    if aliased:
        refs = refs[2:]
    out_hbm, ig_hbm, x_ref, c_ref, hid_ref, bf_ref, o_ref, g_ref, sems = refs
    n, width, ch = o_ref.shape
    copies = [
        pltpu.make_async_copy(x_hbm.at[first_row : first_row + n], x_ref.at[2 : n + 2], sems.at[0]),
        pltpu.make_async_copy(c_hbm.at[first_row : first_row + n], c_ref.at[2 : n + 2], sems.at[1]),
        pltpu.make_async_copy(hid_hbm.at[first_row : first_row + n + 2], hid_ref, sems.at[2]),
        pltpu.make_async_copy(bf_hbm.at[first_row : first_row + n + 2], bf_ref, sems.at[3]),
    ]
    for cp in copies:
        cp.start()
    one = jnp.ones((1, ch), jnp.float32)
    conv_row = row_ops(width, ch, one, one, True, True, n)[4]
    copies[0].wait()
    copies[2].wait()
    for i in range(n):
        o_ref[i] = (x_ref[i + 2].astype(jnp.float32) + conv_row(hid_ref, i, k2f)).astype(o_ref.dtype)
    store_out = pltpu.make_async_copy(o_ref, out_hbm.at[first_row : first_row + n], sems.at[4])
    store_out.start()
    copies[1].wait()
    copies[3].wait()
    for i in range(n):
        g_ref[i] = (c_ref[i + 2].astype(jnp.float32) + conv_row(bf_ref, i, k1b)).astype(g_ref.dtype)
    store_ig = pltpu.make_async_copy(g_ref, ig_hbm.at[first_row : first_row + n], sems.at[5])
    store_ig.start()
    store_out.wait()
    store_ig.wait()


def section(norm, packed_rows, level_index, level_table, inputs, cotangent, before_fn, k1, k2):
    count, width, ch = inputs.shape
    vmem = pltpu.MemorySpace.VMEM if hasattr(pltpu, "MemorySpace") else pltpu.VMEM
    spec = pl.BlockSpec(memory_space=vmem)
    anywhere = pl.BlockSpec(memory_space=pl.ANY)
    smem = pl.BlockSpec(memory_space=pltpu.SMEM)
    big = 3 * ch
    unit = width * big * big * 2
    field = jax.ShapeDtypeStruct((count, width, ch), jnp.bfloat16)
    frame = jax.ShapeDtypeStruct((count + 2, width, ch), jnp.bfloat16)
    frame_t = jax.ShapeDtypeStruct((count + 2, ch, width), jnp.bfloat16)
    square = jax.ShapeDtypeStruct((big, big), jnp.float32)
    params = pltpu.CompilerParams(vmem_limit_bytes=60 * 1024 * 1024)
    matrix = jax.ShapeDtypeStruct((big, big), jnp.bfloat16)
    hid, bf, hidt, acc1, acc2, lv, k1f, k2f, k2b, k1b, xt = pl.pallas_call(
        interior_kernel,
        out_shape=(frame, frame, frame_t, square, square,
                   jax.ShapeDtypeStruct((2, ch), jnp.float32), matrix, matrix, matrix, matrix,
                   jax.ShapeDtypeStruct((count + 4, ch, width), jnp.bfloat16)),
        in_specs=[smem, spec, anywhere, anywhere, spec, spec],
        out_specs=(spec,) * 11,
        scratch_shapes=[
            pltpu.VMEM((count + 4, width, ch), jnp.bfloat16),
            pltpu.VMEM((count + 4, width, ch), jnp.bfloat16),
            pltpu.SemaphoreType.DMA((2,)),
        ],
        compiler_params=params,
        cost_estimate=pl.CostEstimate(
            flops=(4 * count - 6) * unit, transcendentals=count * width * ch, bytes_accessed=8 * count * width * ch
        ),
    )(level_index, level_table, inputs, cotangent, k1, k2)
    before, after = before_fn()
    packed, hid, bf = pl.pallas_call(
        functools.partial(edge_kernel, norm),
        out_shape=(jax.ShapeDtypeStruct((packed_rows, ch), jnp.float32), frame, frame),
        in_specs=[smem, spec] + [anywhere] * 8 + [spec] * 5,
        out_specs=(spec, spec, spec),
        scratch_shapes=[
            pltpu.VMEM((count + 4, width, ch), jnp.bfloat16),
            pltpu.VMEM((count + 4, width, ch), jnp.bfloat16),
            pltpu.VMEM((count + 2, ch, width), jnp.bfloat16),
            pltpu.VMEM((count + 4, ch, width), jnp.bfloat16),
            pltpu.VMEM((big, big), jnp.float32),
            pltpu.VMEM((big, big), jnp.float32),
            pltpu.SemaphoreType.DMA((9,)),
            pltpu.SemaphoreType.DMA((1,)),
        ],
        compiler_params=params,
        cost_estimate=pl.CostEstimate(
            flops=14 * unit, transcendentals=4 * width * ch, bytes_accessed=10 * count * width * ch
        ),
    )(level_index, level_table, inputs, cotangent, before, after, hid, bf, hidt, xt, acc1, acc2, lv, k1f, k2b)
    step = count // 2 if count % 2 == 0 else count
    whole = jax.ShapeDtypeStruct((count, width, ch), jnp.bfloat16)
    chunks = []
    for first_row in range(0, count, step):
        aliased = first_row > 0
        chunks.append(functools.partial(
            pl.pallas_call(
                functools.partial(out_kernel, first_row, aliased),
                out_shape=(whole, whole),
                in_specs=[anywhere] * 4 + [spec] * 2 + [anywhere] * (2 if aliased else 0),
                out_specs=(anywhere, anywhere),
                scratch_shapes=[
                    pltpu.VMEM((step + 2, width, ch), jnp.bfloat16),
                    pltpu.VMEM((step + 2, width, ch), jnp.bfloat16),
                    pltpu.VMEM((step + 2, width, ch), jnp.bfloat16),
                    pltpu.VMEM((step + 2, width, ch), jnp.bfloat16),
                    pltpu.VMEM((step, width, ch), jnp.bfloat16),
                    pltpu.VMEM((step, width, ch), jnp.bfloat16),
                    pltpu.SemaphoreType.DMA((6,)),
                ],
                input_output_aliases={6: 0, 7: 1} if aliased else {},
                compiler_params=params,
                cost_estimate=pl.CostEstimate(
                    flops=2 * step * unit, transcendentals=0, bytes_accessed=8 * step * width * ch
                ),
            ),
            inputs, cotangent, hid, bf, k2f, k1b,
        ))
    return chunks, packed


def butterfly_sum(block, riders):
    n = lax.axis_size("rows")
    me = lax.axis_index("rows")
    bits = []
    k = 1
    while k < n:
        bits.append(k)
        k *= 2
    other = list(bits)
    if len(bits) > 2:
        other[1], other[2] = bits[2], bits[1]
    orders = list(zip(bits, other))
    even = me % 2 == 0

    def step_of(k0, k1):
        perm = [(i, i ^ (k0 if i % 2 == 0 else k1)) for i in range(n)]
        low = jnp.where(even, (me // k0) % 2, (me // k1) % 2) == 0
        return perm, low

    state = ()
    count = 0
    piece = block
    for k0, k1 in orders:
        perm, low = step_of(k0, k1)
        half = piece.shape[0] // 2
        lo, hi = piece[:half], piece[half:]
        keep = jnp.where(low, lo, hi)
        send = jnp.where(low, hi, lo)
        got = lax.ppermute(send, "rows", perm)
        if count in riders:
            got, state = lax.optimization_barrier((got, riders[count](*state)))
        count += 1
        piece = keep + got
    for k0, k1 in reversed(orders):
        perm, low = step_of(k0, k1)
        got = lax.ppermute(piece, "rows", perm)
        if count in riders:
            got, state = lax.optimization_barrier((got, riders[count](*state)))
        count += 1
        piece = jnp.where(low, jnp.concatenate([piece, got]), jnp.concatenate([got, piece]))
    return piece, state


def local(inputs, cotangent, first_kernel, second_kernel, level_table, level_index):
    count = inputs.shape[0]
    width = inputs.shape[1]
    ch = inputs.shape[2]
    size = lax.axis_size("rows")
    total_rows = count * size
    norm = 1.0 / math.sqrt(total_rows * width)

    up = [(i, i + 1) for i in range(size - 1)]
    down = [(i + 1, i) for i in range(size - 1)]
    before = lax.ppermute(jnp.concatenate([inputs[-2:], cotangent[-2:]]), "rows", up)
    after = lax.ppermute(jnp.concatenate([inputs[:2], cotangent[:2]]), "rows", down)
    halo = lambda: (before, after)

    used = 18 * ch + 2
    packed_rows = used + (-used % size)
    chunks, packed = section(
        norm, packed_rows, level_index, level_table, inputs, cotangent, halo,
        first_kernel, second_kernel,
    )
    steps = 2 * (size.bit_length() - 1)
    places = [1, steps - 2] if len(chunks) == 2 and steps >= 4 else list(range(len(chunks)))
    total, (outputs, input_grad) = butterfly_sum(packed, dict(zip(places, chunks)))
    first_sum = total[: 9 * ch].reshape(9, ch, ch)
    second_sum = total[9 * ch : 18 * ch].reshape(9, ch, ch)
    level_sum = total[18 * ch : 18 * ch + 2]
    return (outputs, input_grad, first_sum, second_sum, level_sum)


def solution(mesh):
    return jax.shard_map(
        local,
        mesh=mesh,
        in_specs=(
            P(("groups", "rows"), None, None),
            P(("groups", "rows"), None, None),
            P(),
            P(),
            P(),
            P("groups"),
        ),
        out_specs=(
            P(("groups", "rows"), None, None),
            P(("groups", "rows"), None, None),
            P("groups", None, None),
            P("groups", None, None),
            P("groups", None),
        ),
        check_vma=False,
    )
```
